768 devices in a mesh: face: 12 (over z), row: 4 (over y_hi), col: 16 (over x, y_lo, core).
Axes of the slice: x: 4, y: 8 (y_hi: 4, y_lo: 2; y = y_hi * 2 + y_lo), z: 12, core: 2. Of those that a mesh axis runs over, the one named last changes fastest.
Arguments:
- state: bfloat16 [12, 128, 8192], P('face', 'row', 'col'), may hold values from -8 to 8
- kernel: bfloat16 [9, 64, 64], replicated, may hold values from -0.25 to 0.25
- gain: float32 [64], replicated, may hold values from 0.1 to 1.9
- shift: float32 [64], replicated, may hold values from -3 to 3
- upstream: bfloat16 [12, 128, 8192], P('face', 'row', 'col'), may hold values from -6 to 6
- face_links: int32 [12, 8, 4], replicated, may hold values from 0 to 11, as said below
Outputs:
- state_grad: bfloat16 [12, 128, 8192], P('face', 'row', 'col')
- kernel_grad: float32 [9, 64, 64], replicated
- gain_grad: float32 [64], replicated
- shift_grad: float32 [64], replicated
The draws below stay inside these ranges and needn't reach their ends.
Inputs may be any that keep to these rules, and one draw needn't show every extreme that they name: `face_links`: rows 0 to 3 of face f: the face across that side, the side of that face that touches it, the rotation code (that side + 2 - this side) mod 4, and 0. Rows 4 to 7: the face diagonally across that corner, its touching corner, the code (that corner + 2 - this corner) mod 4, and a flag 1 at the 24 face corners where only three faces meet (the face and corner then name the face itself). The links are those of the HEALPix base faces under some numbering of the faces and some quarter turn of each face, so that each link is the reverse of the link it names.
All inputs are finite; a program needn't handle non-finite values.
Results may differ from the reference program's by a relative error of at most 0.0049.
Values may be sent and summed in bfloat16 or wider, within the bound.
No kernel may reach another device: no remote copies, remote signals or barrier semaphores. Data moves between devices by JAX's collectives and lax.ppermute only.
A program may use at most 32 MiB of HBM per device.

```python
import jax
import jax.numpy as jnp
import numpy as np
from jax import lax

C = 64
SIDE = 128
FACES = 12


def base_links():
    side_face = np.zeros((12, 4), np.int32)
    side_side = np.zeros((12, 4), np.int32)
    corner_face = np.zeros((12, 4), np.int32)
    corner_corner = np.zeros((12, 4), np.int32)
    missing = np.zeros((12, 4), np.int32)
    for quarter in range(4):
        north = quarter
        middle = 4 + quarter
        south = 8 + quarter
        after = (quarter + 1) % 4
        before = (quarter + 3) % 4
        opposite = (quarter + 2) % 4
        side_face[north] = [before, 4 + quarter, 4 + after, after]
        side_side[north] = [3, 3, 0, 0]
        side_face[middle] = [before, 8 + before, 8 + quarter, quarter]
        side_side[middle] = [2, 3, 0, 1]
        side_face[south] = [4 + quarter, 8 + before, 8 + after, 4 + after]
        side_side[south] = [2, 2, 1, 1]
        corner_face[north] = [north, 8 + quarter, north, opposite]
        corner_corner[north] = [0, 3, 2, 3]
        missing[north] = [1, 0, 1, 0]
        corner_face[middle] = [4 + before, middle, 4 + after, middle]
        corner_corner[middle] = [2, 1, 0, 3]
        missing[middle] = [0, 1, 0, 1]
        corner_face[south] = [south, 8 + opposite, south, quarter]
        corner_corner[south] = [0, 1, 2, 1]
        missing[south] = [1, 0, 1, 0]
    return (side_face, side_side, corner_face, corner_corner, missing)


def draw_face_links(key, part):
    side_face, side_side, corner_face, corner_corner, missing = base_links()
    side_face = jnp.asarray(side_face)
    side_side = jnp.asarray(side_side)
    corner_face = jnp.asarray(corner_face)
    corner_corner = jnp.asarray(corner_corner)
    missing = jnp.asarray(missing)
    first, second = jax.random.split(jax.random.fold_in(key, 7))
    order = jax.random.permutation(first, FACES).astype(jnp.int32)
    turning = jax.random.randint(second, (FACES,), 0, 4).astype(jnp.int32)
    own_face = jnp.broadcast_to(jnp.arange(FACES, dtype=jnp.int32)[:, None], (FACES, 4))
    own_slot = (jnp.arange(4, dtype=jnp.int32)[None, :] + turning[:, None]) % 4
    new_owner = order[own_face]
    far_side = (side_side + turning[side_face]) % 4
    side_code = (far_side + 2 - own_slot) % 4
    side_rows = jnp.stack([order[side_face], far_side, side_code, jnp.zeros_like(side_code)], axis=-1)
    far_corner = (corner_corner + turning[corner_face]) % 4
    corner_code = (far_corner + 2 - own_slot) % 4
    corner_rows = jnp.stack([order[corner_face], far_corner, corner_code, missing], axis=-1)
    table = jnp.zeros((FACES, 8, 4), jnp.int32)
    table = table.at[new_owner, own_slot].set(side_rows)
    table = table.at[new_owner, own_slot + 4].set(corner_rows)
    return table


def draw_state(key, part):
    first = jax.random.fold_in(jax.random.fold_in(key, 11), 0)
    second = jax.random.fold_in(jax.random.fold_in(key, 11), 1)
    fourth = jax.random.fold_in(jax.random.fold_in(key, 11), 3)
    face_scale = 0.58 * jnp.exp(jnp.log(3.0) * jnp.arange(FACES, dtype=jnp.float32) / (FACES - 1))
    base = jax.random.normal(first, (FACES, SIDE, SIDE, C), jnp.float32)
    shared = 0.7 * jax.random.normal(fourth, (FACES, SIDE, SIDE, 1), jnp.float32)
    rough = jnp.exp(jax.random.uniform(second, (FACES, SIDE, 1), jnp.float32, -0.35, 0.35))
    mixed = (base + shared).reshape(FACES, SIDE, SIDE * C)
    values = mixed * rough * face_scale[:, None, None]
    return jnp.clip(values, -8.0, 8.0).astype(jnp.bfloat16)


def draw_upstream(key, part):
    first, second = jax.random.split(jax.random.fold_in(key, 13))
    base = jax.random.normal(first, (FACES, SIDE, SIDE * C), jnp.float32)
    offset = jnp.tile(jax.random.uniform(second, (C,), jnp.float32, -1.0, 1.0), SIDE)
    values = base + offset
    return jnp.clip(values, -6.0, 6.0).astype(jnp.bfloat16)


def scatter_about(key, dims, width, bound, held_as=jnp.bfloat16):
    return jnp.clip(width * jax.random.normal(key, dims, jnp.float32), -bound, bound).astype(held_as)


def setup_inputs(seed: int = 0) -> dict:
    arg_keys = jax.random.split(jax.random.key(seed), 7)
    state = draw_state(jax.random.fold_in(arg_keys[6], 71), 0)
    kernel = scatter_about(arg_keys[1], (9, C, C), (9 * C) ** -0.5, 0.25)
    gain = jnp.clip(1.0 + 0.18 * jax.random.normal(arg_keys[2], (C,), jnp.float32), 0.1, 1.9)
    shift = scatter_about(arg_keys[3], (C,), 0.5, 3.0, jnp.float32)
    upstream = draw_upstream(jax.random.fold_in(arg_keys[6], 71), 0)
    face_links = draw_face_links(jax.random.fold_in(arg_keys[6], 71), 0)
    return {"state": state, "kernel": kernel, "gain": gain, "shift": shift, "upstream": upstream, "face_links": face_links}


HALF_ROOT = 0.7071067811865476
GAUSS_NORM = 0.3989422804014327

def gelu_slope(values):
    return 0.5 * (1.0 + lax.erf(values * HALF_ROOT)) + values * jnp.exp(-0.5 * values * values) * GAUSS_NORM

def pad_faces(whole, face_links):
    edges = jnp.stack([whole[:, 0, ::-1], whole[:, :, 0], whole[:, SIDE - 1, :], whole[:, ::-1, SIDE - 1]], axis=1)
    corner_pix = jnp.stack([whole[:, 0, 0], whole[:, SIDE - 1, 0], whole[:, SIDE - 1, SIDE - 1], whole[:, 0, SIDE - 1]], axis=1)
    halos = edges[face_links[:, :4, 0], face_links[:, :4, 1]][:, :, ::-1]
    keeping = (1 - face_links[:, 4:, 3]).astype(whole.dtype)
    corners = corner_pix[face_links[:, 4:, 0], face_links[:, 4:, 1]] * keeping[:, :, None]
    top_line = jnp.concatenate([corners[:, 0:1], halos[:, 0, ::-1], corners[:, 3:4]], axis=1)
    bottom_line = jnp.concatenate([corners[:, 1:2], halos[:, 2], corners[:, 2:3]], axis=1)
    middle = jnp.concatenate([halos[:, 1][:, :, None], whole, halos[:, 3, ::-1][:, :, None]], axis=2)
    return jnp.concatenate([top_line[:, None], middle, bottom_line[:, None]], axis=1)

def convolve(padded, weights):
    return lax.conv_general_dilated(padded, weights.reshape(3, 3, C, C), (1, 1), 'VALID', dimension_numbers=('NHWC', 'HWIO', 'NHWC'), precision=lax.Precision.HIGHEST)

def reference(state, kernel, gain, shift, upstream, face_links):
    whole = state.astype(jnp.float32).reshape(FACES, SIDE, SIDE, C)
    weights = kernel.astype(jnp.float32)

    def forward(field, taps):
        return convolve(pad_faces(field, face_links), taps)
    response, pullback = jax.vjp(forward, whole, weights)
    count = float(FACES * SIDE * SIDE)
    centre = lax.optimization_barrier(jnp.sum(response, axis=(0, 1, 2))) / count
    square_mean = lax.optimization_barrier(jnp.sum(response * response, axis=(0, 1, 2))) / count
    inverse_spread = lax.rsqrt(square_mean - centre * centre + 1e-05)
    normed = (response - centre) * inverse_spread
    before = gain * normed + shift
    incoming = upstream.astype(jnp.float32).reshape(FACES, SIDE, SIDE, C)
    before_grad = incoming * gelu_slope(before)
    shift_grad = lax.optimization_barrier(jnp.sum(before_grad, axis=(0, 1, 2)))
    gain_grad = lax.optimization_barrier(jnp.sum(before_grad * normed, axis=(0, 1, 2)))
    response_grad = (gain * inverse_spread * (before_grad - shift_grad / count - normed * gain_grad / count)).astype(jnp.bfloat16)
    state_grad, kernel_grad = pullback(response_grad.astype(jnp.float32))
    state_grad = state_grad.astype(jnp.bfloat16).reshape(FACES, SIDE, SIDE * C)
    return (state_grad, kernel_grad, gain_grad, shift_grad)
```

```python
import jax
import jax.numpy as jnp
from jax import lax
from jax.sharding import PartitionSpec as P

FACES = 12


HALF_ROOT = 0.7071067811865476
GAUSS_NORM = 0.3989422804014327


def padded_2(cells, sides, width):
    for axis, dim in sides:
        count = lax.axis_size(axis)
        ends = count - 1
        head = lax.slice_in_dim(cells, 0, width, axis=dim)
        tail = lax.slice_in_dim(cells, cells.shape[dim] - width, cells.shape[dim], axis=dim)
        cells = jnp.concatenate(
            [
                lax.ppermute(tail, axis, [(i, (i + 1) % count) for i in range(ends)]),
                cells,
                lax.ppermute(head, axis, [((i + 1) % count, i) for i in range(ends)]),
            ],
            axis=dim,
        )
    return cells


def gelu_slope(values):
    return (
        0.5 * (1.0 + lax.erf(values * HALF_ROOT))
        + values * jnp.exp(-0.5 * values * values) * GAUSS_NORM
    )


def kernel_tap(row_step, col_step):
    return (row_step + 1) * 3 + (col_step + 1)


def turned_tap(turns, row_step, col_step):
    for repeat in range(turns):
        row_step, col_step = (-col_step, row_step)
    return kernel_tap(-row_step, -col_step)


def nested_sum(values):
    for axis in ("col", "row", "face"):
        values = lax.psum(values, axis)
    return values


def channel_pair(first_sum, second_sum):
    return nested_sum((first_sum, second_sum))


def butterfly(values, axis, count, span=None):
    span = count if span is None else span
    step = 1
    while step < span:
        values = values + lax.ppermute(values, axis, [(i, i ^ step) for i in range(count)])
        step *= 2
    return values


def mesh_sum(values):
    values = butterfly(butterfly(values, "col", lax.axis_size("col")), "row", lax.axis_size("row"))
    faces = lax.axis_size("face")
    values = butterfly(values, "face", faces, 4)
    from_before = lax.ppermute(values, "face", [(i, (i + 4) % faces) for i in range(faces)])
    from_after = lax.ppermute(values, "face", [(i, (i + 8) % faces) for i in range(faces)])
    group = lax.axis_index("face") // 4
    first = jnp.where(group == 0, values, jnp.where(group == 1, from_before, from_after))
    second = jnp.where(group == 0, from_after, jnp.where(group == 1, values, from_before))
    third = jnp.where(group == 0, from_before, jnp.where(group == 1, from_after, values))
    return (first + second) + third


def lined(first_val, middle_val, last_val, length):
    middle_part = jnp.broadcast_to(middle_val[:, None], (middle_val.shape[0], length))
    return jnp.concatenate([first_val[:, None], middle_part, last_val[:, None]], axis=1)


def on_device(state, kernel, gain, shift, upstream, face_links):
    local_faces = state.shape[0]
    tile_rows = state.shape[1]
    width = kernel.shape[1]
    tile_cols = state.shape[2] // width
    row_count = lax.axis_size("row")
    col_count = lax.axis_size("col")
    side = tile_rows * row_count
    row_index = lax.axis_index("row")
    col_index = lax.axis_index("col")
    face_ids = lax.axis_index("face") * local_faces + jnp.arange(local_faces, dtype=jnp.int32)
    links = face_links[face_ids]
    face_range = jnp.arange(FACES, dtype=jnp.int32)
    side_range = jnp.arange(4, dtype=jnp.int32)
    pixel_rows = local_faces * tile_rows * tile_cols

    def extend(values):
        padded = padded_2(values, (("row", 1), ("col", 2)), 1)
        row_strip = jnp.where(row_index == 0, values[:, 0], values[:, tile_rows - 1])
        col_strip = jnp.where(col_index == 0, values[:, :, 0], values[:, :, tile_cols - 1])
        by_row = lax.all_gather(
            jnp.concatenate([row_strip, col_strip], axis=1), "row", axis=0, tiled=False
        )
        top_seg = by_row[0, :, :tile_cols]
        bottom_seg = by_row[row_count - 1, :, :tile_cols]
        side_line = jnp.moveaxis(by_row[:, :, tile_cols:], 0, 1).reshape(local_faces, side, width)
        by_col = lax.all_gather(
            jnp.concatenate([top_seg, bottom_seg, side_line], axis=1), "col", axis=0, tiled=False
        )
        top_row = jnp.moveaxis(by_col[:, :, :tile_cols], 0, 1).reshape(local_faces, side, width)
        bottom_row = jnp.moveaxis(by_col[:, :, tile_cols : 2 * tile_cols], 0, 1).reshape(
            local_faces, side, width
        )
        left_col = by_col[0, :, 2 * tile_cols :]
        right_col = by_col[col_count - 1, :, 2 * tile_cols :]
        cycle = jnp.stack([top_row[:, ::-1], left_col, bottom_row, right_col[:, ::-1]], axis=1)
        all_cycle = lax.all_gather(cycle, "face", axis=0, tiled=True)
        all_corner = all_cycle[:, :, side - 1]
        side_pick = (
            (links[:, :4, 0][:, :, None, None] == face_range[:, None])
            & (links[:, :4, 1][:, :, None, None] == side_range)
        ).astype(jnp.bfloat16)
        halo_sides = jnp.einsum(
            "ksgt,gtpc->kspc", side_pick, all_cycle, preferred_element_type=jnp.float32
        ).astype(jnp.bfloat16)[:, :, ::-1]
        corner_pick = (
            (links[:, 4:, 0][:, :, None, None] == face_range[:, None])
            & (links[:, 4:, 1][:, :, None, None] == side_range)
            & (links[:, 4:, 3] == 0)[:, :, None, None]
        ).astype(jnp.bfloat16)
        corner_vals = jnp.einsum(
            "kqgt,gtc->kqc", corner_pick, all_corner, preferred_element_type=jnp.float32
        ).astype(jnp.bfloat16)
        full_top = jnp.concatenate(
            [corner_vals[:, 0:1], halo_sides[:, 0, ::-1], corner_vals[:, 3:4]], axis=1
        )
        full_bottom = jnp.concatenate(
            [corner_vals[:, 1:2], halo_sides[:, 2], corner_vals[:, 2:3]], axis=1
        )
        full_left = jnp.concatenate(
            [corner_vals[:, 0:1], halo_sides[:, 1], corner_vals[:, 1:2]], axis=1
        )
        full_right = jnp.concatenate(
            [corner_vals[:, 3:4], halo_sides[:, 3, ::-1], corner_vals[:, 2:3]], axis=1
        )
        top_piece = lax.dynamic_slice_in_dim(full_top, col_index * tile_cols, tile_cols + 2, 1)
        bottom_piece = lax.dynamic_slice_in_dim(
            full_bottom, col_index * tile_cols, tile_cols + 2, 1
        )
        left_piece = lax.dynamic_slice_in_dim(full_left, row_index * tile_rows, tile_rows + 2, 1)
        right_piece = lax.dynamic_slice_in_dim(full_right, row_index * tile_rows, tile_rows + 2, 1)
        padded = padded.at[:, 0].set(jnp.where(row_index == 0, top_piece, padded[:, 0]))
        padded = padded.at[:, tile_rows + 1].set(
            jnp.where(row_index == row_count - 1, bottom_piece, padded[:, tile_rows + 1])
        )
        padded = padded.at[:, :, 0].set(jnp.where(col_index == 0, left_piece, padded[:, :, 0]))
        padded = padded.at[:, :, tile_cols + 1].set(
            jnp.where(col_index == col_count - 1, right_piece, padded[:, :, tile_cols + 1])
        )
        return padded

    values = state.reshape(local_faces, tile_rows, tile_cols, width)
    padded_state = extend(values)

    def window(padded, row_step, col_step):
        return padded[
            :, 1 + row_step : 1 + row_step + tile_rows, 1 + col_step : 1 + col_step + tile_cols
        ].reshape(pixel_rows, width)

    def row_band(padded, row_step):
        return jnp.concatenate(
            [window(padded, row_step, col_step) for col_step in (-1, 0, 1)], axis=1
        )

    state_bands = [row_band(padded_state, row_step) for row_step in (-1, 0, 1)]
    response = jnp.zeros((pixel_rows, width), jnp.float32)
    for position, row_step in enumerate((-1, 0, 1)):
        band_weight = kernel[3 * position : 3 * position + 3].reshape(3 * width, width)
        response = response + jnp.dot(
            state_bands[position], band_weight, preferred_element_type=jnp.float32
        )
    total = float(FACES * side * side)
    sum_first, sum_square = channel_pair(
        jnp.sum(response, axis=0), jnp.sum(response * response, axis=0)
    )
    centre = sum_first / total
    inverse_spread = lax.rsqrt(sum_square / total - centre * centre + 1e-05)
    normed = (response - centre) * inverse_spread
    before = gain * normed + shift
    incoming = upstream.reshape(pixel_rows, width).astype(jnp.float32)
    before_grad = incoming * gelu_slope(before)
    shift_grad, gain_grad = channel_pair(
        jnp.sum(before_grad, axis=0), jnp.sum(before_grad * normed, axis=0)
    )
    response_grad = (
        gain * inverse_spread * (before_grad - shift_grad / total - normed * gain_grad / total)
    ).astype(jnp.bfloat16)
    kernel_terms = []
    for position in range(3):
        band_term = lax.dot_general(
            state_bands[position],
            response_grad,
            (((0,), (0,)), ((), ())),
            preferred_element_type=jnp.float32,
        )
        kernel_terms.append(band_term.reshape(3, width, width))
    kernel_grad = mesh_sum(jnp.concatenate(kernel_terms, axis=0))
    grad_tile = response_grad.reshape(local_faces, tile_rows, tile_cols, width)
    padded_grad = extend(grad_tile)
    zero_padded = jnp.pad(grad_tile, ((0, 0), (1, 1), (1, 1), (0, 0)))
    state_part = jnp.zeros((pixel_rows, width), jnp.float32)
    for row_step in (-1, 0, 1):
        flipped = jnp.concatenate(
            [kernel[kernel_tap(-row_step, -col_step)].T for col_step in (-1, 0, 1)], axis=0
        )
        state_part = state_part + jnp.dot(
            row_band(zero_padded, row_step), flipped, preferred_element_type=jnp.float32
        )
    state_part = state_part.reshape(local_faces, tile_rows, tile_cols, width)
    side_turns = links[:, :4, 2]
    corner_turns = links[:, 4:, 2]
    full_top_turn = lined(corner_turns[:, 0], side_turns[:, 0], corner_turns[:, 3], side)
    full_bottom_turn = lined(corner_turns[:, 1], side_turns[:, 2], corner_turns[:, 2], side)
    full_left_turn = lined(corner_turns[:, 0], side_turns[:, 1], corner_turns[:, 1], side)
    full_right_turn = lined(corner_turns[:, 3], side_turns[:, 3], corner_turns[:, 2], side)
    top_turn = jnp.where(
        row_index == 0,
        lax.dynamic_slice_in_dim(full_top_turn, col_index * tile_cols, tile_cols + 2, 1),
        0,
    )
    top_turn = top_turn.at[:, 0].set(
        jnp.where(col_index == 0, full_left_turn[:, row_index * tile_rows], top_turn[:, 0])
    )
    top_turn = top_turn.at[:, tile_cols + 1].set(
        jnp.where(
            col_index == col_count - 1,
            full_right_turn[:, row_index * tile_rows],
            top_turn[:, tile_cols + 1],
        )
    )
    bottom_turn = jnp.where(
        row_index == row_count - 1,
        lax.dynamic_slice_in_dim(full_bottom_turn, col_index * tile_cols, tile_cols + 2, 1),
        0,
    )
    bottom_turn = bottom_turn.at[:, 0].set(
        jnp.where(
            col_index == 0,
            full_left_turn[:, row_index * tile_rows + tile_rows + 1],
            bottom_turn[:, 0],
        )
    )
    bottom_turn = bottom_turn.at[:, tile_cols + 1].set(
        jnp.where(
            col_index == col_count - 1,
            full_right_turn[:, row_index * tile_rows + tile_rows + 1],
            bottom_turn[:, tile_cols + 1],
        )
    )
    left_turn = jnp.broadcast_to(
        jnp.where(col_index == 0, side_turns[:, 1], 0)[:, None], (local_faces, tile_rows + 2)
    )
    right_turn = jnp.broadcast_to(
        jnp.where(col_index == col_count - 1, side_turns[:, 3], 0)[:, None],
        (local_faces, tile_rows + 2),
    )

    def strip_terms(strip, turn_codes, steps, length):
        selector = (turn_codes[:, :, None] == side_range).astype(jnp.bfloat16)
        spread = strip[:, :, None, :] * selector[:, :, :, None]
        pieces = jnp.stack(
            [spread[:, 1 + offset : 1 + offset + length] for offset in (-1, 0, 1)], axis=2
        )
        pieces = pieces.reshape(local_faces * length, 12 * width)
        stacked = jnp.concatenate(
            [
                kernel[turned_tap(turn, step_pair[0], step_pair[1])].T
                for step_pair in steps
                for turn in range(4)
            ],
            axis=0,
        )
        summed = jnp.dot(pieces, stacked, preferred_element_type=jnp.float32)
        return summed.reshape(local_faces, length, width)

    left_strip = jnp.pad(padded_grad[:, 1 : tile_rows + 1, 0], ((0, 0), (1, 1), (0, 0)))
    right_strip = jnp.pad(
        padded_grad[:, 1 : tile_rows + 1, tile_cols + 1], ((0, 0), (1, 1), (0, 0))
    )
    top_terms = strip_terms(padded_grad[:, 0], top_turn, ((-1, -1), (-1, 0), (-1, 1)), tile_cols)
    bottom_terms = strip_terms(
        padded_grad[:, tile_rows + 1], bottom_turn, ((1, -1), (1, 0), (1, 1)), tile_cols
    )
    left_terms = strip_terms(left_strip, left_turn, ((-1, -1), (0, -1), (1, -1)), tile_rows)
    right_terms = strip_terms(right_strip, right_turn, ((-1, 1), (0, 1), (1, 1)), tile_rows)
    state_part = state_part.at[:, 0].add(top_terms)
    state_part = state_part.at[:, tile_rows - 1].add(bottom_terms)
    state_part = state_part.at[:, :, 0].add(left_terms)
    state_part = state_part.at[:, :, tile_cols - 1].add(right_terms)
    state_grad = state_part.astype(jnp.bfloat16).reshape(local_faces, tile_rows, tile_cols * width)
    return (state_grad, kernel_grad, gain_grad, shift_grad)


def solution(mesh):
    return jax.shard_map(
        on_device,
        mesh=mesh,
        in_specs=(P("face", "row", "col"), P(), P(), P(), P("face", "row", "col"), P()),
        out_specs=(P("face", "row", "col"), P(), P(), P()),
        check_vma=False,
    )
```

```python
import jax
import jax.numpy as jnp
from jax import lax
from jax.sharding import PartitionSpec as P

FACES = 12


HALF_ROOT = 0.7071067811865476
GAUSS_NORM = 0.3989422804014327


def padded_2(cells, sides, width):
    for axis, dim in sides:
        count = lax.axis_size(axis)
        ends = count - 1
        head = lax.slice_in_dim(cells, 0, width, axis=dim)
        tail = lax.slice_in_dim(cells, cells.shape[dim] - width, cells.shape[dim], axis=dim)
        cells = jnp.concatenate(
            [
                lax.ppermute(tail, axis, [(i, (i + 1) % count) for i in range(ends)]),
                cells,
                lax.ppermute(head, axis, [((i + 1) % count, i) for i in range(ends)]),
            ],
            axis=dim,
        )
    return cells


def gelu_slope(values):
    return (
        0.5 * (1.0 + lax.erf(values * HALF_ROOT))
        + values * jnp.exp(-0.5 * values * values) * GAUSS_NORM
    )


def kernel_tap(row_step, col_step):
    return (row_step + 1) * 3 + (col_step + 1)


def turned_tap(turns, row_step, col_step):
    for repeat in range(turns):
        row_step, col_step = (-col_step, row_step)
    return kernel_tap(-row_step, -col_step)


def nested_sum(values, carried=None):
    for axis in ("col", "row", "face"):
        if carried is None:
            values = lax.psum(values, axis)
        else:
            values = carried.beside(lambda part, axis=axis: lax.psum(part, axis), values)
    return values


def channel_pair(first_sum, second_sum, carried=None):
    return nested_sum((first_sum, second_sum), carried)


def sum_steps():
    steps = []
    for axis in ("col", "row"):
        count = lax.axis_size(axis)
        step = 1
        while step < count:
            steps.append((axis, [[(i, i ^ step) for i in range(count)]]))
            step *= 2
    faces = lax.axis_size("face")
    steps.append(("face", [[(i, i ^ 1) for i in range(faces)]]))
    steps.append(("face", [[(i, i ^ 2) for i in range(faces)]]))
    steps.append(
        (
            "face",
            [
                [(i, (i + 4) % faces) for i in range(faces)],
                [(i, (i + 8) % faces) for i in range(faces)],
            ],
        )
    )
    return steps


def step_send(step, values):
    axis, pair_sets = step
    return [lax.ppermute(values, axis, pairs) for pairs in pair_sets]


def step_land(step, values, moved):
    if len(moved) == 1:
        return values + moved[0]
    from_before, from_after = moved
    group = lax.axis_index("face") // 4
    first = jnp.where(group == 0, values, jnp.where(group == 1, from_before, from_after))
    second = jnp.where(group == 0, from_after, jnp.where(group == 1, values, from_before))
    third = jnp.where(group == 0, from_before, jnp.where(group == 1, from_after, values))
    return (first + second) + third


class Carried:
    def __init__(self, values):
        self.values = values
        self.steps = sum_steps()

    def beside(self, collective, operand):
        if not self.steps:
            return collective(operand)
        step = self.steps.pop(0)
        values, operand = lax.optimization_barrier((self.values, operand))
        moved = step_send(step, values)
        result = collective(operand)
        self.values = step_land(step, values, moved)
        return result

    def finish(self):
        while self.steps:
            step = self.steps.pop(0)
            self.values = step_land(step, self.values, step_send(step, self.values))
        return self.values


def lined(first_val, middle_val, last_val, length):
    middle_part = jnp.broadcast_to(middle_val[:, None], (middle_val.shape[0], length))
    return jnp.concatenate([first_val[:, None], middle_part, last_val[:, None]], axis=1)


def on_device(state, kernel, gain, shift, upstream, face_links):
    local_faces = state.shape[0]
    tile_rows = state.shape[1]
    width = kernel.shape[1]
    tile_cols = state.shape[2] // width
    row_count = lax.axis_size("row")
    col_count = lax.axis_size("col")
    side = tile_rows * row_count
    row_index = lax.axis_index("row")
    col_index = lax.axis_index("col")
    face_ids = lax.axis_index("face") * local_faces + jnp.arange(local_faces, dtype=jnp.int32)
    links = face_links[face_ids]
    face_range = jnp.arange(FACES, dtype=jnp.int32)
    side_range = jnp.arange(4, dtype=jnp.int32)
    pixel_rows = local_faces * tile_rows * tile_cols

    def extend(values, carried=None):
        def gather(part, axis, tiled):
            def run(operand):
                return lax.all_gather(operand, axis, axis=0, tiled=tiled)

            return run(part) if carried is None else carried.beside(run, part)

        padded = padded_2(values, (("row", 1), ("col", 2)), 1)
        row_strip = jnp.where(row_index == 0, values[:, 0], values[:, tile_rows - 1])
        col_strip = jnp.where(col_index == 0, values[:, :, 0], values[:, :, tile_cols - 1])
        by_row = gather(jnp.concatenate([row_strip, col_strip], axis=1), "row", False)
        top_seg = by_row[0, :, :tile_cols]
        bottom_seg = by_row[row_count - 1, :, :tile_cols]
        side_line = jnp.moveaxis(by_row[:, :, tile_cols:], 0, 1).reshape(local_faces, side, width)
        by_col = gather(jnp.concatenate([top_seg, bottom_seg, side_line], axis=1), "col", False)
        top_row = jnp.moveaxis(by_col[:, :, :tile_cols], 0, 1).reshape(local_faces, side, width)
        bottom_row = jnp.moveaxis(by_col[:, :, tile_cols : 2 * tile_cols], 0, 1).reshape(
            local_faces, side, width
        )
        left_col = by_col[0, :, 2 * tile_cols :]
        right_col = by_col[col_count - 1, :, 2 * tile_cols :]
        cycle = jnp.stack([top_row[:, ::-1], left_col, bottom_row, right_col[:, ::-1]], axis=1)
        all_cycle = gather(cycle, "face", True)
        all_corner = all_cycle[:, :, side - 1]
        side_pick = (
            (links[:, :4, 0][:, :, None, None] == face_range[:, None])
            & (links[:, :4, 1][:, :, None, None] == side_range)
        ).astype(jnp.bfloat16)
        halo_sides = jnp.einsum(
            "ksgt,gtpc->kspc", side_pick, all_cycle, preferred_element_type=jnp.float32
        ).astype(jnp.bfloat16)[:, :, ::-1]
        corner_pick = (
            (links[:, 4:, 0][:, :, None, None] == face_range[:, None])
            & (links[:, 4:, 1][:, :, None, None] == side_range)
            & (links[:, 4:, 3] == 0)[:, :, None, None]
        ).astype(jnp.bfloat16)
        corner_vals = jnp.einsum(
            "kqgt,gtc->kqc", corner_pick, all_corner, preferred_element_type=jnp.float32
        ).astype(jnp.bfloat16)
        full_top = jnp.concatenate(
            [corner_vals[:, 0:1], halo_sides[:, 0, ::-1], corner_vals[:, 3:4]], axis=1
        )
        full_bottom = jnp.concatenate(
            [corner_vals[:, 1:2], halo_sides[:, 2], corner_vals[:, 2:3]], axis=1
        )
        full_left = jnp.concatenate(
            [corner_vals[:, 0:1], halo_sides[:, 1], corner_vals[:, 1:2]], axis=1
        )
        full_right = jnp.concatenate(
            [corner_vals[:, 3:4], halo_sides[:, 3, ::-1], corner_vals[:, 2:3]], axis=1
        )
        top_piece = lax.dynamic_slice_in_dim(full_top, col_index * tile_cols, tile_cols + 2, 1)
        bottom_piece = lax.dynamic_slice_in_dim(
            full_bottom, col_index * tile_cols, tile_cols + 2, 1
        )
        left_piece = lax.dynamic_slice_in_dim(full_left, row_index * tile_rows, tile_rows + 2, 1)
        right_piece = lax.dynamic_slice_in_dim(full_right, row_index * tile_rows, tile_rows + 2, 1)
        padded = padded.at[:, 0].set(jnp.where(row_index == 0, top_piece, padded[:, 0]))
        padded = padded.at[:, tile_rows + 1].set(
            jnp.where(row_index == row_count - 1, bottom_piece, padded[:, tile_rows + 1])
        )
        padded = padded.at[:, :, 0].set(jnp.where(col_index == 0, left_piece, padded[:, :, 0]))
        padded = padded.at[:, :, tile_cols + 1].set(
            jnp.where(col_index == col_count - 1, right_piece, padded[:, :, tile_cols + 1])
        )
        return padded

    values = state.reshape(local_faces, tile_rows, tile_cols, width)
    padded_state = extend(values)

    def window(padded, row_step, col_step):
        return padded[
            :, 1 + row_step : 1 + row_step + tile_rows, 1 + col_step : 1 + col_step + tile_cols
        ].reshape(pixel_rows, width)

    def row_band(padded, row_step):
        return jnp.concatenate(
            [window(padded, row_step, col_step) for col_step in (-1, 0, 1)], axis=1
        )

    state_bands = [row_band(padded_state, row_step) for row_step in (-1, 0, 1)]
    response = jnp.zeros((pixel_rows, width), jnp.float32)
    for position, row_step in enumerate((-1, 0, 1)):
        band_weight = kernel[3 * position : 3 * position + 3].reshape(3 * width, width)
        response = response + jnp.dot(
            state_bands[position], band_weight, preferred_element_type=jnp.float32
        )
    total = float(FACES * side * side)
    sum_first, sum_square = channel_pair(
        jnp.sum(response, axis=0), jnp.sum(response * response, axis=0)
    )
    centre = sum_first / total
    inverse_spread = lax.rsqrt(sum_square / total - centre * centre + 1e-05)
    normed = (response - centre) * inverse_spread
    before = gain * normed + shift
    incoming = upstream.reshape(pixel_rows, width).astype(jnp.float32)
    before_grad = incoming * gelu_slope(before)
    centred = response - centre
    state_sums = []
    centred_sums = []
    slope_sums = []
    for position in range(3):
        state_sums.append(jnp.sum(state_bands[position].astype(jnp.float32), axis=0))
        centred_sums.append(
            lax.dot_general(
                state_bands[position],
                centred,
                (((0,), (0,)), ((), ())),
                precision=lax.Precision.HIGHEST,
                preferred_element_type=jnp.float32,
            )
        )
        slope_sums.append(
            lax.dot_general(
                state_bands[position],
                before_grad,
                (((0,), (0,)), ((), ())),
                precision=lax.Precision.HIGHEST,
                preferred_element_type=jnp.float32,
            )
        )
    taps = 9
    carried = Carried(
        jnp.concatenate(
            [
                jnp.stack(slope_sums).reshape(-1),
                jnp.stack(centred_sums).reshape(-1),
                jnp.stack(state_sums).reshape(-1),
            ]
        )
    )
    shift_grad, gain_grad = channel_pair(
        jnp.sum(before_grad, axis=0), jnp.sum(before_grad * normed, axis=0), carried
    )
    response_grad = (
        gain * inverse_spread * (before_grad - shift_grad / total - normed * gain_grad / total)
    ).astype(jnp.bfloat16)
    grad_tile = response_grad.reshape(local_faces, tile_rows, tile_cols, width)
    padded_grad = extend(grad_tile, carried)
    kernel_sums = carried.finish()
    block = taps * width * width
    slope_total = kernel_sums[:block].reshape(taps, width, width)
    centred_total = kernel_sums[block : 2 * block].reshape(taps, width, width)
    state_total = kernel_sums[2 * block :].reshape(taps, width, 1)
    kernel_grad = (gain * inverse_spread) * (
        slope_total
        - state_total * (shift_grad / total)
        - centred_total * (gain_grad * inverse_spread / total)
    )
    zero_padded = jnp.pad(grad_tile, ((0, 0), (1, 1), (1, 1), (0, 0)))
    state_part = jnp.zeros((pixel_rows, width), jnp.float32)
    for row_step in (-1, 0, 1):
        flipped = jnp.concatenate(
            [kernel[kernel_tap(-row_step, -col_step)].T for col_step in (-1, 0, 1)], axis=0
        )
        state_part = state_part + jnp.dot(
            row_band(zero_padded, row_step), flipped, preferred_element_type=jnp.float32
        )
    state_part = state_part.reshape(local_faces, tile_rows, tile_cols, width)
    side_turns = links[:, :4, 2]
    corner_turns = links[:, 4:, 2]
    full_top_turn = lined(corner_turns[:, 0], side_turns[:, 0], corner_turns[:, 3], side)
    full_bottom_turn = lined(corner_turns[:, 1], side_turns[:, 2], corner_turns[:, 2], side)
    full_left_turn = lined(corner_turns[:, 0], side_turns[:, 1], corner_turns[:, 1], side)
    full_right_turn = lined(corner_turns[:, 3], side_turns[:, 3], corner_turns[:, 2], side)
    top_turn = jnp.where(
        row_index == 0,
        lax.dynamic_slice_in_dim(full_top_turn, col_index * tile_cols, tile_cols + 2, 1),
        0,
    )
    top_turn = top_turn.at[:, 0].set(
        jnp.where(col_index == 0, full_left_turn[:, row_index * tile_rows], top_turn[:, 0])
    )
    top_turn = top_turn.at[:, tile_cols + 1].set(
        jnp.where(
            col_index == col_count - 1,
            full_right_turn[:, row_index * tile_rows],
            top_turn[:, tile_cols + 1],
        )
    )
    bottom_turn = jnp.where(
        row_index == row_count - 1,
        lax.dynamic_slice_in_dim(full_bottom_turn, col_index * tile_cols, tile_cols + 2, 1),
        0,
    )
    bottom_turn = bottom_turn.at[:, 0].set(
        jnp.where(
            col_index == 0,
            full_left_turn[:, row_index * tile_rows + tile_rows + 1],
            bottom_turn[:, 0],
        )
    )
    bottom_turn = bottom_turn.at[:, tile_cols + 1].set(
        jnp.where(
            col_index == col_count - 1,
            full_right_turn[:, row_index * tile_rows + tile_rows + 1],
            bottom_turn[:, tile_cols + 1],
        )
    )
    left_turn = jnp.broadcast_to(
        jnp.where(col_index == 0, side_turns[:, 1], 0)[:, None], (local_faces, tile_rows + 2)
    )
    right_turn = jnp.broadcast_to(
        jnp.where(col_index == col_count - 1, side_turns[:, 3], 0)[:, None],
        (local_faces, tile_rows + 2),
    )

    def strip_terms(strip, turn_codes, steps, length):
        selector = (turn_codes[:, :, None] == side_range).astype(jnp.bfloat16)
        spread = strip[:, :, None, :] * selector[:, :, :, None]
        pieces = jnp.stack(
            [spread[:, 1 + offset : 1 + offset + length] for offset in (-1, 0, 1)], axis=2
        )
        pieces = pieces.reshape(local_faces * length, 12 * width)
        stacked = jnp.concatenate(
            [
                kernel[turned_tap(turn, step_pair[0], step_pair[1])].T
                for step_pair in steps
                for turn in range(4)
            ],
            axis=0,
        )
        summed = jnp.dot(pieces, stacked, preferred_element_type=jnp.float32)
        return summed.reshape(local_faces, length, width)

    left_strip = jnp.pad(padded_grad[:, 1 : tile_rows + 1, 0], ((0, 0), (1, 1), (0, 0)))
    right_strip = jnp.pad(
        padded_grad[:, 1 : tile_rows + 1, tile_cols + 1], ((0, 0), (1, 1), (0, 0))
    )
    top_terms = strip_terms(padded_grad[:, 0], top_turn, ((-1, -1), (-1, 0), (-1, 1)), tile_cols)
    bottom_terms = strip_terms(
        padded_grad[:, tile_rows + 1], bottom_turn, ((1, -1), (1, 0), (1, 1)), tile_cols
    )
    left_terms = strip_terms(left_strip, left_turn, ((-1, -1), (0, -1), (1, -1)), tile_rows)
    right_terms = strip_terms(right_strip, right_turn, ((-1, 1), (0, 1), (1, 1)), tile_rows)
    state_part = state_part.at[:, 0].add(top_terms)
    state_part = state_part.at[:, tile_rows - 1].add(bottom_terms)
    state_part = state_part.at[:, :, 0].add(left_terms)
    state_part = state_part.at[:, :, tile_cols - 1].add(right_terms)
    state_grad = state_part.astype(jnp.bfloat16).reshape(local_faces, tile_rows, tile_cols * width)
    return (state_grad, kernel_grad, gain_grad, shift_grad)


def solution(mesh):
    return jax.shard_map(
        on_device,
        mesh=mesh,
        in_specs=(P("face", "row", "col"), P(), P(), P(), P("face", "row", "col"), P()),
        out_specs=(P("face", "row", "col"), P(), P(), P()),
        check_vma=False,
    )
```

```python
import jax
import jax.numpy as jnp
from jax import lax
from jax.sharding import PartitionSpec as P

FACES = 12


HALF_ROOT = 0.7071067811865476
GAUSS_NORM = 0.3989422804014327


def padded_2(cells, sides, width):
    for axis, dim in sides:
        count = lax.axis_size(axis)
        ends = count - 1
        head = lax.slice_in_dim(cells, 0, width, axis=dim)
        tail = lax.slice_in_dim(cells, cells.shape[dim] - width, cells.shape[dim], axis=dim)
        cells = jnp.concatenate(
            [
                lax.ppermute(tail, axis, [(i, (i + 1) % count) for i in range(ends)]),
                cells,
                lax.ppermute(head, axis, [((i + 1) % count, i) for i in range(ends)]),
            ],
            axis=dim,
        )
    return cells


def gelu_slope(values):
    return (
        0.5 * (1.0 + lax.erf(values * HALF_ROOT))
        + values * jnp.exp(-0.5 * values * values) * GAUSS_NORM
    )


def kernel_tap(row_step, col_step):
    return (row_step + 1) * 3 + (col_step + 1)


def turned_tap(turns, row_step, col_step):
    for repeat in range(turns):
        row_step, col_step = (-col_step, row_step)
    return kernel_tap(-row_step, -col_step)


def nested_sum(values, carried=None):
    for axis in ("col", "row", "face"):
        if carried is None:
            values = lax.psum(values, axis)
        else:
            values = carried.beside(lambda part, axis=axis: lax.psum(part, axis), values)
    return values


def channel_pair(first_sum, second_sum, carried=None):
    return nested_sum((first_sum, second_sum), carried)


def gathered_sum(values):
    for axis in ("col", "row", "face"):
        values = jnp.sum(lax.all_gather(values, axis, axis=0, tiled=False), axis=0)
    return values


def sum_steps():
    faces = lax.axis_size("face")
    steps = [
        ("face", [[(i, i ^ 1) for i in range(faces)]]),
        ("face", [[(i, i ^ 2) for i in range(faces)]]),
        (
            "face",
            [
                [(i, (i + 4) % faces) for i in range(faces)],
                [(i, (i + 8) % faces) for i in range(faces)],
            ],
        ),
    ]
    for axis in ("row", "col"):
        count = lax.axis_size(axis)
        step = count // 2
        while step >= 1:
            steps.append((axis, [[(i, i ^ step) for i in range(count)]]))
            step //= 2
    return steps


def step_send(step, values):
    axis, pair_sets = step
    return [lax.ppermute(values, axis, pairs) for pairs in pair_sets]


def step_land(step, values, moved):
    if len(moved) == 1:
        return values + moved[0]
    from_before, from_after = moved
    group = lax.axis_index("face") // 4
    first = jnp.where(group == 0, values, jnp.where(group == 1, from_before, from_after))
    second = jnp.where(group == 0, from_after, jnp.where(group == 1, values, from_before))
    third = jnp.where(group == 0, from_before, jnp.where(group == 1, from_after, values))
    return (first + second) + third


class Carried:
    def __init__(self, values):
        self.values = values
        self.steps = sum_steps()

    def beside(self, collective, operand):
        if not self.steps:
            return collective(operand)
        step = self.steps.pop(0)
        values, operand = lax.optimization_barrier((self.values, operand))
        moved = step_send(step, values)
        result = collective(operand)
        self.values = step_land(step, values, moved)
        return result

    def finish(self):
        while self.steps:
            step = self.steps.pop(0)
            self.values = step_land(step, self.values, step_send(step, self.values))
        return self.values


def lined(first_val, middle_val, last_val, length):
    middle_part = jnp.broadcast_to(middle_val[:, None], (middle_val.shape[0], length))
    return jnp.concatenate([first_val[:, None], middle_part, last_val[:, None]], axis=1)


def on_device(state, kernel, gain, shift, upstream, face_links):
    local_faces = state.shape[0]
    tile_rows = state.shape[1]
    width = kernel.shape[1]
    tile_cols = state.shape[2] // width
    row_count = lax.axis_size("row")
    col_count = lax.axis_size("col")
    side = tile_rows * row_count
    row_index = lax.axis_index("row")
    col_index = lax.axis_index("col")
    face_ids = lax.axis_index("face") * local_faces + jnp.arange(local_faces, dtype=jnp.int32)
    links = face_links[face_ids]
    face_range = jnp.arange(FACES, dtype=jnp.int32)
    side_range = jnp.arange(4, dtype=jnp.int32)
    pixel_rows = local_faces * tile_rows * tile_cols

    def extend(values, carried=None):
        def gather(part, axis, tiled):
            def run(operand):
                return lax.all_gather(operand, axis, axis=0, tiled=tiled)

            return run(part) if carried is None else carried.beside(run, part)

        padded = padded_2(values, (("row", 1), ("col", 2)), 1)
        row_strip = jnp.where(row_index == 0, values[:, 0], values[:, tile_rows - 1])
        col_strip = jnp.where(col_index == 0, values[:, :, 0], values[:, :, tile_cols - 1])
        by_row = gather(jnp.concatenate([row_strip, col_strip], axis=1), "row", False)
        top_seg = by_row[0, :, :tile_cols]
        bottom_seg = by_row[row_count - 1, :, :tile_cols]
        side_line = jnp.moveaxis(by_row[:, :, tile_cols:], 0, 1).reshape(local_faces, side, width)
        by_col = gather(jnp.concatenate([top_seg, bottom_seg, side_line], axis=1), "col", False)
        top_row = jnp.moveaxis(by_col[:, :, :tile_cols], 0, 1).reshape(local_faces, side, width)
        bottom_row = jnp.moveaxis(by_col[:, :, tile_cols : 2 * tile_cols], 0, 1).reshape(
            local_faces, side, width
        )
        left_col = by_col[0, :, 2 * tile_cols :]
        right_col = by_col[col_count - 1, :, 2 * tile_cols :]
        cycle = jnp.stack([top_row[:, ::-1], left_col, bottom_row, right_col[:, ::-1]], axis=1)
        all_cycle = gather(cycle, "face", True)
        all_corner = all_cycle[:, :, side - 1]
        side_pick = (
            (links[:, :4, 0][:, :, None, None] == face_range[:, None])
            & (links[:, :4, 1][:, :, None, None] == side_range)
        ).astype(jnp.bfloat16)
        halo_sides = jnp.einsum(
            "ksgt,gtpc->kspc", side_pick, all_cycle, preferred_element_type=jnp.float32
        ).astype(jnp.bfloat16)[:, :, ::-1]
        corner_pick = (
            (links[:, 4:, 0][:, :, None, None] == face_range[:, None])
            & (links[:, 4:, 1][:, :, None, None] == side_range)
            & (links[:, 4:, 3] == 0)[:, :, None, None]
        ).astype(jnp.bfloat16)
        corner_vals = jnp.einsum(
            "kqgt,gtc->kqc", corner_pick, all_corner, preferred_element_type=jnp.float32
        ).astype(jnp.bfloat16)
        full_top = jnp.concatenate(
            [corner_vals[:, 0:1], halo_sides[:, 0, ::-1], corner_vals[:, 3:4]], axis=1
        )
        full_bottom = jnp.concatenate(
            [corner_vals[:, 1:2], halo_sides[:, 2], corner_vals[:, 2:3]], axis=1
        )
        full_left = jnp.concatenate(
            [corner_vals[:, 0:1], halo_sides[:, 1], corner_vals[:, 1:2]], axis=1
        )
        full_right = jnp.concatenate(
            [corner_vals[:, 3:4], halo_sides[:, 3, ::-1], corner_vals[:, 2:3]], axis=1
        )
        top_piece = lax.dynamic_slice_in_dim(full_top, col_index * tile_cols, tile_cols + 2, 1)
        bottom_piece = lax.dynamic_slice_in_dim(
            full_bottom, col_index * tile_cols, tile_cols + 2, 1
        )
        left_piece = lax.dynamic_slice_in_dim(full_left, row_index * tile_rows, tile_rows + 2, 1)
        right_piece = lax.dynamic_slice_in_dim(full_right, row_index * tile_rows, tile_rows + 2, 1)
        padded = padded.at[:, 0].set(jnp.where(row_index == 0, top_piece, padded[:, 0]))
        padded = padded.at[:, tile_rows + 1].set(
            jnp.where(row_index == row_count - 1, bottom_piece, padded[:, tile_rows + 1])
        )
        padded = padded.at[:, :, 0].set(jnp.where(col_index == 0, left_piece, padded[:, :, 0]))
        padded = padded.at[:, :, tile_cols + 1].set(
            jnp.where(col_index == col_count - 1, right_piece, padded[:, :, tile_cols + 1])
        )
        return padded

    values = state.reshape(local_faces, tile_rows, tile_cols, width)
    padded_state = extend(values)

    def window(padded, row_step, col_step):
        return padded[
            :, 1 + row_step : 1 + row_step + tile_rows, 1 + col_step : 1 + col_step + tile_cols
        ].reshape(pixel_rows, width)

    def row_band(padded, row_step):
        return jnp.concatenate(
            [window(padded, row_step, col_step) for col_step in (-1, 0, 1)], axis=1
        )

    state_bands = [row_band(padded_state, row_step) for row_step in (-1, 0, 1)]
    response = jnp.zeros((pixel_rows, width), jnp.float32)
    for position, row_step in enumerate((-1, 0, 1)):
        band_weight = kernel[3 * position : 3 * position + 3].reshape(3 * width, width)
        response = response + jnp.dot(
            state_bands[position], band_weight, preferred_element_type=jnp.float32
        )
    total = float(FACES * side * side)
    sum_first, sum_square = gathered_sum(
        jnp.stack([jnp.sum(response, axis=0), jnp.sum(response * response, axis=0)])
    )
    centre = sum_first / total
    inverse_spread = lax.rsqrt(sum_square / total - centre * centre + 1e-05)
    normed = (response - centre) * inverse_spread
    before = gain * normed + shift
    incoming = upstream.reshape(pixel_rows, width).astype(jnp.float32)
    before_grad = incoming * gelu_slope(before)
    centred = response - centre
    state_sums = []
    centred_sums = []
    slope_sums = []
    for position in range(3):
        state_sums.append(jnp.sum(state_bands[position].astype(jnp.float32), axis=0))
        centred_sums.append(
            lax.dot_general(
                state_bands[position],
                centred,
                (((0,), (0,)), ((), ())),
                precision=lax.Precision.HIGHEST,
                preferred_element_type=jnp.float32,
            )
        )
        slope_sums.append(
            lax.dot_general(
                state_bands[position],
                before_grad,
                (((0,), (0,)), ((), ())),
                precision=lax.Precision.HIGHEST,
                preferred_element_type=jnp.float32,
            )
        )
    taps = 9
    carried = Carried(
        jnp.concatenate(
            [
                jnp.stack(slope_sums).reshape(-1),
                jnp.stack(centred_sums).reshape(-1),
                jnp.stack(state_sums).reshape(-1),
            ]
        )
    )
    shift_grad, gain_grad = channel_pair(
        jnp.sum(before_grad, axis=0), jnp.sum(before_grad * normed, axis=0), carried
    )
    response_grad = (
        gain * inverse_spread * (before_grad - shift_grad / total - normed * gain_grad / total)
    ).astype(jnp.bfloat16)
    grad_tile = response_grad.reshape(local_faces, tile_rows, tile_cols, width)
    padded_grad = extend(grad_tile, carried)
    kernel_sums = carried.finish()
    block = taps * width * width
    slope_total = kernel_sums[:block].reshape(taps, width, width)
    centred_total = kernel_sums[block : 2 * block].reshape(taps, width, width)
    state_total = kernel_sums[2 * block :].reshape(taps, width, 1)
    kernel_grad = (gain * inverse_spread) * (
        slope_total
        - state_total * (shift_grad / total)
        - centred_total * (gain_grad * inverse_spread / total)
    )
    zero_padded = jnp.pad(grad_tile, ((0, 0), (1, 1), (1, 1), (0, 0)))
    state_part = jnp.zeros((pixel_rows, width), jnp.float32)
    for row_step in (-1, 0, 1):
        flipped = jnp.concatenate(
            [kernel[kernel_tap(-row_step, -col_step)].T for col_step in (-1, 0, 1)], axis=0
        )
        state_part = state_part + jnp.dot(
            row_band(zero_padded, row_step), flipped, preferred_element_type=jnp.float32
        )
    state_part = state_part.reshape(local_faces, tile_rows, tile_cols, width)
    side_turns = links[:, :4, 2]
    corner_turns = links[:, 4:, 2]
    full_top_turn = lined(corner_turns[:, 0], side_turns[:, 0], corner_turns[:, 3], side)
    full_bottom_turn = lined(corner_turns[:, 1], side_turns[:, 2], corner_turns[:, 2], side)
    full_left_turn = lined(corner_turns[:, 0], side_turns[:, 1], corner_turns[:, 1], side)
    full_right_turn = lined(corner_turns[:, 3], side_turns[:, 3], corner_turns[:, 2], side)
    top_turn = jnp.where(
        row_index == 0,
        lax.dynamic_slice_in_dim(full_top_turn, col_index * tile_cols, tile_cols + 2, 1),
        0,
    )
    top_turn = top_turn.at[:, 0].set(
        jnp.where(col_index == 0, full_left_turn[:, row_index * tile_rows], top_turn[:, 0])
    )
    top_turn = top_turn.at[:, tile_cols + 1].set(
        jnp.where(
            col_index == col_count - 1,
            full_right_turn[:, row_index * tile_rows],
            top_turn[:, tile_cols + 1],
        )
    )
    bottom_turn = jnp.where(
        row_index == row_count - 1,
        lax.dynamic_slice_in_dim(full_bottom_turn, col_index * tile_cols, tile_cols + 2, 1),
        0,
    )
    bottom_turn = bottom_turn.at[:, 0].set(
        jnp.where(
            col_index == 0,
            full_left_turn[:, row_index * tile_rows + tile_rows + 1],
            bottom_turn[:, 0],
        )
    )
    bottom_turn = bottom_turn.at[:, tile_cols + 1].set(
        jnp.where(
            col_index == col_count - 1,
            full_right_turn[:, row_index * tile_rows + tile_rows + 1],
            bottom_turn[:, tile_cols + 1],
        )
    )
    left_turn = jnp.broadcast_to(
        jnp.where(col_index == 0, side_turns[:, 1], 0)[:, None], (local_faces, tile_rows + 2)
    )
    right_turn = jnp.broadcast_to(
        jnp.where(col_index == col_count - 1, side_turns[:, 3], 0)[:, None],
        (local_faces, tile_rows + 2),
    )

    def strip_terms(strip, turn_codes, steps, length):
        selector = (turn_codes[:, :, None] == side_range).astype(jnp.bfloat16)
        spread = strip[:, :, None, :] * selector[:, :, :, None]
        pieces = jnp.stack(
            [spread[:, 1 + offset : 1 + offset + length] for offset in (-1, 0, 1)], axis=2
        )
        pieces = pieces.reshape(local_faces * length, 12 * width)
        stacked = jnp.concatenate(
            [
                kernel[turned_tap(turn, step_pair[0], step_pair[1])].T
                for step_pair in steps
                for turn in range(4)
            ],
            axis=0,
        )
        summed = jnp.dot(pieces, stacked, preferred_element_type=jnp.float32)
        return summed.reshape(local_faces, length, width)

    left_strip = jnp.pad(padded_grad[:, 1 : tile_rows + 1, 0], ((0, 0), (1, 1), (0, 0)))
    right_strip = jnp.pad(
        padded_grad[:, 1 : tile_rows + 1, tile_cols + 1], ((0, 0), (1, 1), (0, 0))
    )
    top_terms = strip_terms(padded_grad[:, 0], top_turn, ((-1, -1), (-1, 0), (-1, 1)), tile_cols)
    bottom_terms = strip_terms(
        padded_grad[:, tile_rows + 1], bottom_turn, ((1, -1), (1, 0), (1, 1)), tile_cols
    )
    left_terms = strip_terms(left_strip, left_turn, ((-1, -1), (0, -1), (1, -1)), tile_rows)
    right_terms = strip_terms(right_strip, right_turn, ((-1, 1), (0, 1), (1, 1)), tile_rows)
    state_part = state_part.at[:, 0].add(top_terms)
    state_part = state_part.at[:, tile_rows - 1].add(bottom_terms)
    state_part = state_part.at[:, :, 0].add(left_terms)
    state_part = state_part.at[:, :, tile_cols - 1].add(right_terms)
    state_grad = state_part.astype(jnp.bfloat16).reshape(local_faces, tile_rows, tile_cols * width)
    return (state_grad, kernel_grad, gain_grad, shift_grad)


def solution(mesh):
    return jax.shard_map(
        on_device,
        mesh=mesh,
        in_specs=(P("face", "row", "col"), P(), P(), P(), P("face", "row", "col"), P()),
        out_specs=(P("face", "row", "col"), P(), P(), P()),
        check_vma=False,
    )
```

```python
import jax
import jax.numpy as jnp
from jax import lax
from jax.sharding import PartitionSpec as P

FACES = 12


HALF_ROOT = 0.7071067811865476
GAUSS_NORM = 0.3989422804014327


def padded_2(cells, sides, width):
    for axis, dim in sides:
        count = lax.axis_size(axis)
        ends = count - 1
        head = lax.slice_in_dim(cells, 0, width, axis=dim)
        tail = lax.slice_in_dim(cells, cells.shape[dim] - width, cells.shape[dim], axis=dim)
        cells = jnp.concatenate(
            [
                lax.ppermute(tail, axis, [(i, (i + 1) % count) for i in range(ends)]),
                cells,
                lax.ppermute(head, axis, [((i + 1) % count, i) for i in range(ends)]),
            ],
            axis=dim,
        )
    return cells


def gelu_slope(values):
    return (
        0.5 * (1.0 + lax.erf(values * HALF_ROOT))
        + values * jnp.exp(-0.5 * values * values) * GAUSS_NORM
    )


def kernel_tap(row_step, col_step):
    return (row_step + 1) * 3 + (col_step + 1)


def turned_tap(turns, row_step, col_step):
    for repeat in range(turns):
        row_step, col_step = (-col_step, row_step)
    return kernel_tap(-row_step, -col_step)


def nested_sum(values, carried=None):
    for axis in ("col", "row", "face"):
        if carried is None:
            values = lax.psum(values, axis)
        else:
            values = carried.beside(lambda part, axis=axis: lax.psum(part, axis), values)
    return values


def channel_pair(first_sum, second_sum, carried=None):
    return nested_sum((first_sum, second_sum), carried)


def gathered_sum(values):
    for axis in ("col", "row", "face"):
        values = jnp.sum(lax.all_gather(values, axis, axis=0, tiled=False), axis=0)
    return values


def sum_steps():
    faces = lax.axis_size("face")
    steps = [
        (
            "face",
            [
                [(i, (i + 4) % faces) for i in range(faces)],
                [(i, (i + 8) % faces) for i in range(faces)],
            ],
        ),
        ("face", [[(i, i ^ 1) for i in range(faces)]]),
        ("face", [[(i, i ^ 2) for i in range(faces)]]),
    ]
    for axis in ("row", "col"):
        count = lax.axis_size(axis)
        step = count // 2
        while step >= 1:
            steps.append((axis, [[(i, i ^ step) for i in range(count)]]))
            step //= 2
    return steps


def step_send(step, values):
    axis, pair_sets = step
    return [lax.ppermute(values, axis, pairs) for pairs in pair_sets]


def step_land(step, values, moved):
    if len(moved) == 1:
        return values + moved[0]
    from_before, from_after = moved
    group = lax.axis_index("face") // 4
    first = jnp.where(group == 0, values, jnp.where(group == 1, from_before, from_after))
    second = jnp.where(group == 0, from_after, jnp.where(group == 1, values, from_before))
    third = jnp.where(group == 0, from_before, jnp.where(group == 1, from_after, values))
    return (first + second) + third


class Carried:
    def __init__(self, values):
        self.values = values
        self.steps = sum_steps()

    def beside(self, collective, operand):
        if not self.steps:
            return collective(operand)
        step = self.steps.pop(0)
        values, operand = lax.optimization_barrier((self.values, operand))
        moved = step_send(step, values)
        result = collective(operand)
        self.values = step_land(step, values, moved)
        return result

    def finish(self):
        while self.steps:
            step = self.steps.pop(0)
            self.values = step_land(step, self.values, step_send(step, self.values))
        return self.values


def lined(first_val, middle_val, last_val, length):
    middle_part = jnp.broadcast_to(middle_val[:, None], (middle_val.shape[0], length))
    return jnp.concatenate([first_val[:, None], middle_part, last_val[:, None]], axis=1)


def on_device(state, kernel, gain, shift, upstream, face_links):
    local_faces = state.shape[0]
    tile_rows = state.shape[1]
    width = kernel.shape[1]
    tile_cols = state.shape[2] // width
    row_count = lax.axis_size("row")
    col_count = lax.axis_size("col")
    side = tile_rows * row_count
    row_index = lax.axis_index("row")
    col_index = lax.axis_index("col")
    face_ids = lax.axis_index("face") * local_faces + jnp.arange(local_faces, dtype=jnp.int32)
    links = face_links[face_ids]
    face_range = jnp.arange(FACES, dtype=jnp.int32)
    side_range = jnp.arange(4, dtype=jnp.int32)
    pixel_rows = local_faces * tile_rows * tile_cols

    def extend(values, carried=None):
        def gather(part, axis, tiled):
            def run(operand):
                return lax.all_gather(operand, axis, axis=0, tiled=tiled)

            return run(part) if carried is None else carried.beside(run, part)

        padded = padded_2(values, (("row", 1), ("col", 2)), 1)
        row_strip = jnp.where(row_index == 0, values[:, 0], values[:, tile_rows - 1])
        col_strip = jnp.where(col_index == 0, values[:, :, 0], values[:, :, tile_cols - 1])
        by_row = gather(jnp.concatenate([row_strip, col_strip], axis=1), "row", False)
        top_seg = by_row[0, :, :tile_cols]
        bottom_seg = by_row[row_count - 1, :, :tile_cols]
        side_line = jnp.moveaxis(by_row[:, :, tile_cols:], 0, 1).reshape(local_faces, side, width)
        by_col = gather(jnp.concatenate([top_seg, bottom_seg, side_line], axis=1), "col", False)
        top_row = jnp.moveaxis(by_col[:, :, :tile_cols], 0, 1).reshape(local_faces, side, width)
        bottom_row = jnp.moveaxis(by_col[:, :, tile_cols : 2 * tile_cols], 0, 1).reshape(
            local_faces, side, width
        )
        left_col = by_col[0, :, 2 * tile_cols :]
        right_col = by_col[col_count - 1, :, 2 * tile_cols :]
        cycle = jnp.stack([top_row[:, ::-1], left_col, bottom_row, right_col[:, ::-1]], axis=1)
        all_cycle = gather(cycle, "face", True)
        all_corner = all_cycle[:, :, side - 1]
        side_pick = (
            (links[:, :4, 0][:, :, None, None] == face_range[:, None])
            & (links[:, :4, 1][:, :, None, None] == side_range)
        ).astype(jnp.bfloat16)
        halo_sides = jnp.einsum(
            "ksgt,gtpc->kspc", side_pick, all_cycle, preferred_element_type=jnp.float32
        ).astype(jnp.bfloat16)[:, :, ::-1]
        corner_pick = (
            (links[:, 4:, 0][:, :, None, None] == face_range[:, None])
            & (links[:, 4:, 1][:, :, None, None] == side_range)
            & (links[:, 4:, 3] == 0)[:, :, None, None]
        ).astype(jnp.bfloat16)
        corner_vals = jnp.einsum(
            "kqgt,gtc->kqc", corner_pick, all_corner, preferred_element_type=jnp.float32
        ).astype(jnp.bfloat16)
        full_top = jnp.concatenate(
            [corner_vals[:, 0:1], halo_sides[:, 0, ::-1], corner_vals[:, 3:4]], axis=1
        )
        full_bottom = jnp.concatenate(
            [corner_vals[:, 1:2], halo_sides[:, 2], corner_vals[:, 2:3]], axis=1
        )
        full_left = jnp.concatenate(
            [corner_vals[:, 0:1], halo_sides[:, 1], corner_vals[:, 1:2]], axis=1
        )
        full_right = jnp.concatenate(
            [corner_vals[:, 3:4], halo_sides[:, 3, ::-1], corner_vals[:, 2:3]], axis=1
        )
        top_piece = lax.dynamic_slice_in_dim(full_top, col_index * tile_cols, tile_cols + 2, 1)
        bottom_piece = lax.dynamic_slice_in_dim(
            full_bottom, col_index * tile_cols, tile_cols + 2, 1
        )
        left_piece = lax.dynamic_slice_in_dim(full_left, row_index * tile_rows, tile_rows + 2, 1)
        right_piece = lax.dynamic_slice_in_dim(full_right, row_index * tile_rows, tile_rows + 2, 1)
        padded = padded.at[:, 0].set(jnp.where(row_index == 0, top_piece, padded[:, 0]))
        padded = padded.at[:, tile_rows + 1].set(
            jnp.where(row_index == row_count - 1, bottom_piece, padded[:, tile_rows + 1])
        )
        padded = padded.at[:, :, 0].set(jnp.where(col_index == 0, left_piece, padded[:, :, 0]))
        padded = padded.at[:, :, tile_cols + 1].set(
            jnp.where(col_index == col_count - 1, right_piece, padded[:, :, tile_cols + 1])
        )
        return padded

    values = state.reshape(local_faces, tile_rows, tile_cols, width)
    padded_state = extend(values)

    def window(padded, row_step, col_step):
        return padded[
            :, 1 + row_step : 1 + row_step + tile_rows, 1 + col_step : 1 + col_step + tile_cols
        ].reshape(pixel_rows, width)

    def row_band(padded, row_step):
        return jnp.concatenate(
            [window(padded, row_step, col_step) for col_step in (-1, 0, 1)], axis=1
        )

    state_bands = [row_band(padded_state, row_step) for row_step in (-1, 0, 1)]
    response = jnp.zeros((pixel_rows, width), jnp.float32)
    for position, row_step in enumerate((-1, 0, 1)):
        band_weight = kernel[3 * position : 3 * position + 3].reshape(3 * width, width)
        response = response + jnp.dot(
            state_bands[position], band_weight, preferred_element_type=jnp.float32
        )
    total = float(FACES * side * side)
    sum_first, sum_square = gathered_sum(
        jnp.stack([jnp.sum(response, axis=0), jnp.sum(response * response, axis=0)])
    )
    centre = sum_first / total
    inverse_spread = lax.rsqrt(sum_square / total - centre * centre + 1e-05)
    normed = (response - centre) * inverse_spread
    before = gain * normed + shift
    incoming = upstream.reshape(pixel_rows, width).astype(jnp.float32)
    before_grad = incoming * gelu_slope(before)
    centred = response - centre
    state_sums = []
    centred_sums = []
    slope_sums = []
    for position in range(3):
        state_sums.append(jnp.sum(state_bands[position].astype(jnp.float32), axis=0))
        centred_sums.append(
            lax.dot_general(
                state_bands[position],
                centred,
                (((0,), (0,)), ((), ())),
                precision=lax.Precision.HIGHEST,
                preferred_element_type=jnp.float32,
            )
        )
        slope_sums.append(
            lax.dot_general(
                state_bands[position],
                before_grad,
                (((0,), (0,)), ((), ())),
                precision=lax.Precision.HIGHEST,
                preferred_element_type=jnp.float32,
            )
        )
    taps = 9
    carried = Carried(
        jnp.concatenate(
            [
                jnp.stack(slope_sums).reshape(-1),
                jnp.stack(centred_sums).reshape(-1),
                jnp.stack(state_sums).reshape(-1),
            ]
        )
    )
    shift_grad, gain_grad = channel_pair(
        jnp.sum(before_grad, axis=0), jnp.sum(before_grad * normed, axis=0), carried
    )
    response_grad = (
        gain * inverse_spread * (before_grad - shift_grad / total - normed * gain_grad / total)
    ).astype(jnp.bfloat16)
    grad_tile = response_grad.reshape(local_faces, tile_rows, tile_cols, width)
    padded_grad = extend(grad_tile, carried)
    kernel_sums = carried.finish()
    block = taps * width * width
    slope_total = kernel_sums[:block].reshape(taps, width, width)
    centred_total = kernel_sums[block : 2 * block].reshape(taps, width, width)
    state_total = kernel_sums[2 * block :].reshape(taps, width, 1)
    kernel_grad = (gain * inverse_spread) * (
        slope_total
        - state_total * (shift_grad / total)
        - centred_total * (gain_grad * inverse_spread / total)
    )
    zero_padded = jnp.pad(grad_tile, ((0, 0), (1, 1), (1, 1), (0, 0)))
    state_part = jnp.zeros((pixel_rows, width), jnp.float32)
    for row_step in (-1, 0, 1):
        flipped = jnp.concatenate(
            [kernel[kernel_tap(-row_step, -col_step)].T for col_step in (-1, 0, 1)], axis=0
        )
        state_part = state_part + jnp.dot(
            row_band(zero_padded, row_step), flipped, preferred_element_type=jnp.float32
        )
    state_part = state_part.reshape(local_faces, tile_rows, tile_cols, width)
    side_turns = links[:, :4, 2]
    corner_turns = links[:, 4:, 2]
    full_top_turn = lined(corner_turns[:, 0], side_turns[:, 0], corner_turns[:, 3], side)
    full_bottom_turn = lined(corner_turns[:, 1], side_turns[:, 2], corner_turns[:, 2], side)
    full_left_turn = lined(corner_turns[:, 0], side_turns[:, 1], corner_turns[:, 1], side)
    full_right_turn = lined(corner_turns[:, 3], side_turns[:, 3], corner_turns[:, 2], side)
    top_turn = jnp.where(
        row_index == 0,
        lax.dynamic_slice_in_dim(full_top_turn, col_index * tile_cols, tile_cols + 2, 1),
        0,
    )
    top_turn = top_turn.at[:, 0].set(
        jnp.where(col_index == 0, full_left_turn[:, row_index * tile_rows], top_turn[:, 0])
    )
    top_turn = top_turn.at[:, tile_cols + 1].set(
        jnp.where(
            col_index == col_count - 1,
            full_right_turn[:, row_index * tile_rows],
            top_turn[:, tile_cols + 1],
        )
    )
    bottom_turn = jnp.where(
        row_index == row_count - 1,
        lax.dynamic_slice_in_dim(full_bottom_turn, col_index * tile_cols, tile_cols + 2, 1),
        0,
    )
    bottom_turn = bottom_turn.at[:, 0].set(
        jnp.where(
            col_index == 0,
            full_left_turn[:, row_index * tile_rows + tile_rows + 1],
            bottom_turn[:, 0],
        )
    )
    bottom_turn = bottom_turn.at[:, tile_cols + 1].set(
        jnp.where(
            col_index == col_count - 1,
            full_right_turn[:, row_index * tile_rows + tile_rows + 1],
            bottom_turn[:, tile_cols + 1],
        )
    )
    left_turn = jnp.broadcast_to(
        jnp.where(col_index == 0, side_turns[:, 1], 0)[:, None], (local_faces, tile_rows + 2)
    )
    right_turn = jnp.broadcast_to(
        jnp.where(col_index == col_count - 1, side_turns[:, 3], 0)[:, None],
        (local_faces, tile_rows + 2),
    )

    def strip_terms(strip, turn_codes, steps, length):
        selector = (turn_codes[:, :, None] == side_range).astype(jnp.bfloat16)
        spread = strip[:, :, None, :] * selector[:, :, :, None]
        pieces = jnp.stack(
            [spread[:, 1 + offset : 1 + offset + length] for offset in (-1, 0, 1)], axis=2
        )
        pieces = pieces.reshape(local_faces * length, 12 * width)
        stacked = jnp.concatenate(
            [
                kernel[turned_tap(turn, step_pair[0], step_pair[1])].T
                for step_pair in steps
                for turn in range(4)
            ],
            axis=0,
        )
        summed = jnp.dot(pieces, stacked, preferred_element_type=jnp.float32)
        return summed.reshape(local_faces, length, width)

    left_strip = jnp.pad(padded_grad[:, 1 : tile_rows + 1, 0], ((0, 0), (1, 1), (0, 0)))
    right_strip = jnp.pad(
        padded_grad[:, 1 : tile_rows + 1, tile_cols + 1], ((0, 0), (1, 1), (0, 0))
    )
    top_terms = strip_terms(padded_grad[:, 0], top_turn, ((-1, -1), (-1, 0), (-1, 1)), tile_cols)
    bottom_terms = strip_terms(
        padded_grad[:, tile_rows + 1], bottom_turn, ((1, -1), (1, 0), (1, 1)), tile_cols
    )
    left_terms = strip_terms(left_strip, left_turn, ((-1, -1), (0, -1), (1, -1)), tile_rows)
    right_terms = strip_terms(right_strip, right_turn, ((-1, 1), (0, 1), (1, 1)), tile_rows)
    state_part = state_part.at[:, 0].add(top_terms)
    state_part = state_part.at[:, tile_rows - 1].add(bottom_terms)
    state_part = state_part.at[:, :, 0].add(left_terms)
    state_part = state_part.at[:, :, tile_cols - 1].add(right_terms)
    state_grad = state_part.astype(jnp.bfloat16).reshape(local_faces, tile_rows, tile_cols * width)
    return (state_grad, kernel_grad, gain_grad, shift_grad)


def solution(mesh):
    return jax.shard_map(
        on_device,
        mesh=mesh,
        in_specs=(P("face", "row", "col"), P(), P(), P(), P("face", "row", "col"), P()),
        out_specs=(P("face", "row", "col"), P(), P(), P()),
        check_vma=False,
    )
```

```python
import jax
import jax.numpy as jnp
from jax import lax
from jax.sharding import PartitionSpec as P

FACES = 12


HALF_ROOT = 0.7071067811865476
GAUSS_NORM = 0.3989422804014327


def padded_2(cells, sides, width):
    for axis, dim in sides:
        count = lax.axis_size(axis)
        ends = count - 1
        head = lax.slice_in_dim(cells, 0, width, axis=dim)
        tail = lax.slice_in_dim(cells, cells.shape[dim] - width, cells.shape[dim], axis=dim)
        cells = jnp.concatenate(
            [
                lax.ppermute(tail, axis, [(i, (i + 1) % count) for i in range(ends)]),
                cells,
                lax.ppermute(head, axis, [((i + 1) % count, i) for i in range(ends)]),
            ],
            axis=dim,
        )
    return cells


def gelu_slope(values):
    return (
        0.5 * (1.0 + lax.erf(values * HALF_ROOT))
        + values * jnp.exp(-0.5 * values * values) * GAUSS_NORM
    )


def kernel_tap(row_step, col_step):
    return (row_step + 1) * 3 + (col_step + 1)


def turned_tap(turns, row_step, col_step):
    for repeat in range(turns):
        row_step, col_step = (-col_step, row_step)
    return kernel_tap(-row_step, -col_step)


def nested_sum(values, carried=None):
    for axis in ("col", "row", "face"):
        if carried is None:
            values = lax.psum(values, axis)
        else:
            values = carried.beside(lambda part, axis=axis: lax.psum(part, axis), values)
    return values


def channel_pair(first_sum, second_sum, carried=None):
    return nested_sum((first_sum, second_sum), carried)


def gathered_sum(values):
    for axis in ("col", "row", "face"):
        values = jnp.sum(lax.all_gather(values, axis, axis=0, tiled=False), axis=0)
    return values


def sum_steps():
    faces = lax.axis_size("face")
    steps = [
        (
            "face",
            [
                [(i, (i + 4) % faces) for i in range(faces)],
                [(i, (i + 8) % faces) for i in range(faces)],
            ],
        ),
        ("face", [[(i, i ^ 1) for i in range(faces)]]),
        ("face", [[(i, i ^ 2) for i in range(faces)]]),
    ]
    for axis in ("row", "col"):
        count = lax.axis_size(axis)
        step = count // 2
        while step >= 1:
            steps.append((axis, [[(i, i ^ step) for i in range(count)]]))
            step //= 2
    return steps


def step_send(step, values):
    axis, pair_sets = step
    return [lax.ppermute(values, axis, pairs) for pairs in pair_sets]


def step_land(step, values, moved):
    if len(moved) == 1:
        return values + moved[0]
    from_before, from_after = moved
    group = lax.axis_index("face") // 4
    first = jnp.where(group == 0, values, jnp.where(group == 1, from_before, from_after))
    second = jnp.where(group == 0, from_after, jnp.where(group == 1, values, from_before))
    third = jnp.where(group == 0, from_before, jnp.where(group == 1, from_after, values))
    return (first + second) + third


class Carried:
    def __init__(self, values):
        self.values = values
        self.steps = sum_steps()

    def beside(self, collective, operand):
        if not self.steps:
            return collective(operand)
        step = self.steps.pop(0)
        values, operand = lax.optimization_barrier((self.values, operand))
        moved = step_send(step, values)
        result = collective(operand)
        self.values = step_land(step, values, moved)
        return result

    def doubling(self, part, axis):
        count = lax.axis_size(axis)
        index = lax.axis_index(axis)
        gathered = part[None]
        step_size = 1
        while step_size < count:
            step = self.steps.pop(0) if self.steps else None
            values, gathered = lax.optimization_barrier((self.values, gathered))
            moved = step_send(step, values) if step else None
            arrived = lax.ppermute(
                gathered, axis, [(i, i ^ step_size) for i in range(count)]
            )
            gathered = jnp.where(
                (index // step_size) % 2 == 1,
                jnp.concatenate([arrived, gathered], axis=0),
                jnp.concatenate([gathered, arrived], axis=0),
            )
            self.values = step_land(step, values, moved) if step else values
            step_size *= 2
        return gathered

    def finish(self):
        while self.steps:
            step = self.steps.pop(0)
            self.values = step_land(step, self.values, step_send(step, self.values))
        return self.values


def lined(first_val, middle_val, last_val, length):
    middle_part = jnp.broadcast_to(middle_val[:, None], (middle_val.shape[0], length))
    return jnp.concatenate([first_val[:, None], middle_part, last_val[:, None]], axis=1)


def on_device(state, kernel, gain, shift, upstream, face_links):
    local_faces = state.shape[0]
    tile_rows = state.shape[1]
    width = kernel.shape[1]
    tile_cols = state.shape[2] // width
    row_count = lax.axis_size("row")
    col_count = lax.axis_size("col")
    side = tile_rows * row_count
    row_index = lax.axis_index("row")
    col_index = lax.axis_index("col")
    face_ids = lax.axis_index("face") * local_faces + jnp.arange(local_faces, dtype=jnp.int32)
    links = face_links[face_ids]
    face_range = jnp.arange(FACES, dtype=jnp.int32)
    side_range = jnp.arange(4, dtype=jnp.int32)
    pixel_rows = local_faces * tile_rows * tile_cols

    def extend(values, carried=None):
        def gather(part, axis, tiled):
            if carried is None or axis == "face":
                return lax.all_gather(part, axis, axis=0, tiled=tiled)
            return carried.doubling(part, axis)

        padded = padded_2(values, (("row", 1), ("col", 2)), 1)
        row_strip = jnp.where(row_index == 0, values[:, 0], values[:, tile_rows - 1])
        col_strip = jnp.where(col_index == 0, values[:, :, 0], values[:, :, tile_cols - 1])
        by_row = gather(jnp.concatenate([row_strip, col_strip], axis=1), "row", False)
        top_seg = by_row[0, :, :tile_cols]
        bottom_seg = by_row[row_count - 1, :, :tile_cols]
        side_line = jnp.moveaxis(by_row[:, :, tile_cols:], 0, 1).reshape(local_faces, side, width)
        by_col = gather(jnp.concatenate([top_seg, bottom_seg, side_line], axis=1), "col", False)
        top_row = jnp.moveaxis(by_col[:, :, :tile_cols], 0, 1).reshape(local_faces, side, width)
        bottom_row = jnp.moveaxis(by_col[:, :, tile_cols : 2 * tile_cols], 0, 1).reshape(
            local_faces, side, width
        )
        left_col = by_col[0, :, 2 * tile_cols :]
        right_col = by_col[col_count - 1, :, 2 * tile_cols :]
        cycle = jnp.stack([top_row[:, ::-1], left_col, bottom_row, right_col[:, ::-1]], axis=1)
        all_cycle = gather(cycle, "face", True)
        all_corner = all_cycle[:, :, side - 1]
        side_pick = (
            (links[:, :4, 0][:, :, None, None] == face_range[:, None])
            & (links[:, :4, 1][:, :, None, None] == side_range)
        ).astype(jnp.bfloat16)
        halo_sides = jnp.einsum(
            "ksgt,gtpc->kspc", side_pick, all_cycle, preferred_element_type=jnp.float32
        ).astype(jnp.bfloat16)[:, :, ::-1]
        corner_pick = (
            (links[:, 4:, 0][:, :, None, None] == face_range[:, None])
            & (links[:, 4:, 1][:, :, None, None] == side_range)
            & (links[:, 4:, 3] == 0)[:, :, None, None]
        ).astype(jnp.bfloat16)
        corner_vals = jnp.einsum(
            "kqgt,gtc->kqc", corner_pick, all_corner, preferred_element_type=jnp.float32
        ).astype(jnp.bfloat16)
        full_top = jnp.concatenate(
            [corner_vals[:, 0:1], halo_sides[:, 0, ::-1], corner_vals[:, 3:4]], axis=1
        )
        full_bottom = jnp.concatenate(
            [corner_vals[:, 1:2], halo_sides[:, 2], corner_vals[:, 2:3]], axis=1
        )
        full_left = jnp.concatenate(
            [corner_vals[:, 0:1], halo_sides[:, 1], corner_vals[:, 1:2]], axis=1
        )
        full_right = jnp.concatenate(
            [corner_vals[:, 3:4], halo_sides[:, 3, ::-1], corner_vals[:, 2:3]], axis=1
        )
        top_piece = lax.dynamic_slice_in_dim(full_top, col_index * tile_cols, tile_cols + 2, 1)
        bottom_piece = lax.dynamic_slice_in_dim(
            full_bottom, col_index * tile_cols, tile_cols + 2, 1
        )
        left_piece = lax.dynamic_slice_in_dim(full_left, row_index * tile_rows, tile_rows + 2, 1)
        right_piece = lax.dynamic_slice_in_dim(full_right, row_index * tile_rows, tile_rows + 2, 1)
        padded = padded.at[:, 0].set(jnp.where(row_index == 0, top_piece, padded[:, 0]))
        padded = padded.at[:, tile_rows + 1].set(
            jnp.where(row_index == row_count - 1, bottom_piece, padded[:, tile_rows + 1])
        )
        padded = padded.at[:, :, 0].set(jnp.where(col_index == 0, left_piece, padded[:, :, 0]))
        padded = padded.at[:, :, tile_cols + 1].set(
            jnp.where(col_index == col_count - 1, right_piece, padded[:, :, tile_cols + 1])
        )
        return padded

    values = state.reshape(local_faces, tile_rows, tile_cols, width)
    padded_state = extend(values)

    def window(padded, row_step, col_step):
        return padded[
            :, 1 + row_step : 1 + row_step + tile_rows, 1 + col_step : 1 + col_step + tile_cols
        ].reshape(pixel_rows, width)

    def row_band(padded, row_step):
        return jnp.concatenate(
            [window(padded, row_step, col_step) for col_step in (-1, 0, 1)], axis=1
        )

    state_bands = [row_band(padded_state, row_step) for row_step in (-1, 0, 1)]
    response = jnp.zeros((pixel_rows, width), jnp.float32)
    for position, row_step in enumerate((-1, 0, 1)):
        band_weight = kernel[3 * position : 3 * position + 3].reshape(3 * width, width)
        response = response + jnp.dot(
            state_bands[position], band_weight, preferred_element_type=jnp.float32
        )
    total = float(FACES * side * side)
    sum_first, sum_square = gathered_sum(
        jnp.stack([jnp.sum(response, axis=0), jnp.sum(response * response, axis=0)])
    )
    centre = sum_first / total
    inverse_spread = lax.rsqrt(sum_square / total - centre * centre + 1e-05)
    normed = (response - centre) * inverse_spread
    before = gain * normed + shift
    incoming = upstream.reshape(pixel_rows, width).astype(jnp.float32)
    before_grad = incoming * gelu_slope(before)
    centred = response - centre
    state_sums = []
    centred_sums = []
    slope_sums = []
    for position in range(3):
        state_sums.append(jnp.sum(state_bands[position].astype(jnp.float32), axis=0))
        centred_sums.append(
            lax.dot_general(
                state_bands[position],
                centred,
                (((0,), (0,)), ((), ())),
                precision=lax.Precision.HIGHEST,
                preferred_element_type=jnp.float32,
            )
        )
        slope_sums.append(
            lax.dot_general(
                state_bands[position],
                before_grad,
                (((0,), (0,)), ((), ())),
                precision=lax.Precision.HIGHEST,
                preferred_element_type=jnp.float32,
            )
        )
    taps = 9
    carried = Carried(
        jnp.concatenate(
            [
                jnp.stack(slope_sums).reshape(-1),
                jnp.stack(centred_sums).reshape(-1),
                jnp.stack(state_sums).reshape(-1),
            ]
        )
    )
    shift_grad, gain_grad = channel_pair(
        jnp.sum(before_grad, axis=0), jnp.sum(before_grad * normed, axis=0), carried
    )
    response_grad = (
        gain * inverse_spread * (before_grad - shift_grad / total - normed * gain_grad / total)
    ).astype(jnp.bfloat16)
    grad_tile = response_grad.reshape(local_faces, tile_rows, tile_cols, width)
    padded_grad = extend(grad_tile, carried)
    kernel_sums = carried.finish()
    block = taps * width * width
    slope_total = kernel_sums[:block].reshape(taps, width, width)
    centred_total = kernel_sums[block : 2 * block].reshape(taps, width, width)
    state_total = kernel_sums[2 * block :].reshape(taps, width, 1)
    kernel_grad = (gain * inverse_spread) * (
        slope_total
        - state_total * (shift_grad / total)
        - centred_total * (gain_grad * inverse_spread / total)
    )
    zero_padded = jnp.pad(grad_tile, ((0, 0), (1, 1), (1, 1), (0, 0)))
    state_part = jnp.zeros((pixel_rows, width), jnp.float32)
    for row_step in (-1, 0, 1):
        flipped = jnp.concatenate(
            [kernel[kernel_tap(-row_step, -col_step)].T for col_step in (-1, 0, 1)], axis=0
        )
        state_part = state_part + jnp.dot(
            row_band(zero_padded, row_step), flipped, preferred_element_type=jnp.float32
        )
    state_part = state_part.reshape(local_faces, tile_rows, tile_cols, width)
    side_turns = links[:, :4, 2]
    corner_turns = links[:, 4:, 2]
    full_top_turn = lined(corner_turns[:, 0], side_turns[:, 0], corner_turns[:, 3], side)
    full_bottom_turn = lined(corner_turns[:, 1], side_turns[:, 2], corner_turns[:, 2], side)
    full_left_turn = lined(corner_turns[:, 0], side_turns[:, 1], corner_turns[:, 1], side)
    full_right_turn = lined(corner_turns[:, 3], side_turns[:, 3], corner_turns[:, 2], side)
    top_turn = jnp.where(
        row_index == 0,
        lax.dynamic_slice_in_dim(full_top_turn, col_index * tile_cols, tile_cols + 2, 1),
        0,
    )
    top_turn = top_turn.at[:, 0].set(
        jnp.where(col_index == 0, full_left_turn[:, row_index * tile_rows], top_turn[:, 0])
    )
    top_turn = top_turn.at[:, tile_cols + 1].set(
        jnp.where(
            col_index == col_count - 1,
            full_right_turn[:, row_index * tile_rows],
            top_turn[:, tile_cols + 1],
        )
    )
    bottom_turn = jnp.where(
        row_index == row_count - 1,
        lax.dynamic_slice_in_dim(full_bottom_turn, col_index * tile_cols, tile_cols + 2, 1),
        0,
    )
    bottom_turn = bottom_turn.at[:, 0].set(
        jnp.where(
            col_index == 0,
            full_left_turn[:, row_index * tile_rows + tile_rows + 1],
            bottom_turn[:, 0],
        )
    )
    bottom_turn = bottom_turn.at[:, tile_cols + 1].set(
        jnp.where(
            col_index == col_count - 1,
            full_right_turn[:, row_index * tile_rows + tile_rows + 1],
            bottom_turn[:, tile_cols + 1],
        )
    )
    left_turn = jnp.broadcast_to(
        jnp.where(col_index == 0, side_turns[:, 1], 0)[:, None], (local_faces, tile_rows + 2)
    )
    right_turn = jnp.broadcast_to(
        jnp.where(col_index == col_count - 1, side_turns[:, 3], 0)[:, None],
        (local_faces, tile_rows + 2),
    )

    def strip_terms(strip, turn_codes, steps, length):
        selector = (turn_codes[:, :, None] == side_range).astype(jnp.bfloat16)
        spread = strip[:, :, None, :] * selector[:, :, :, None]
        pieces = jnp.stack(
            [spread[:, 1 + offset : 1 + offset + length] for offset in (-1, 0, 1)], axis=2
        )
        pieces = pieces.reshape(local_faces * length, 12 * width)
        stacked = jnp.concatenate(
            [
                kernel[turned_tap(turn, step_pair[0], step_pair[1])].T
                for step_pair in steps
                for turn in range(4)
            ],
            axis=0,
        )
        summed = jnp.dot(pieces, stacked, preferred_element_type=jnp.float32)
        return summed.reshape(local_faces, length, width)

    left_strip = jnp.pad(padded_grad[:, 1 : tile_rows + 1, 0], ((0, 0), (1, 1), (0, 0)))
    right_strip = jnp.pad(
        padded_grad[:, 1 : tile_rows + 1, tile_cols + 1], ((0, 0), (1, 1), (0, 0))
    )
    top_terms = strip_terms(padded_grad[:, 0], top_turn, ((-1, -1), (-1, 0), (-1, 1)), tile_cols)
    bottom_terms = strip_terms(
        padded_grad[:, tile_rows + 1], bottom_turn, ((1, -1), (1, 0), (1, 1)), tile_cols
    )
    left_terms = strip_terms(left_strip, left_turn, ((-1, -1), (0, -1), (1, -1)), tile_rows)
    right_terms = strip_terms(right_strip, right_turn, ((-1, 1), (0, 1), (1, 1)), tile_rows)
    state_part = state_part.at[:, 0].add(top_terms)
    state_part = state_part.at[:, tile_rows - 1].add(bottom_terms)
    state_part = state_part.at[:, :, 0].add(left_terms)
    state_part = state_part.at[:, :, tile_cols - 1].add(right_terms)
    state_grad = state_part.astype(jnp.bfloat16).reshape(local_faces, tile_rows, tile_cols * width)
    return (state_grad, kernel_grad, gain_grad, shift_grad)


def solution(mesh):
    return jax.shard_map(
        on_device,
        mesh=mesh,
        in_specs=(P("face", "row", "col"), P(), P(), P(), P("face", "row", "col"), P()),
        out_specs=(P("face", "row", "col"), P(), P(), P()),
        check_vma=False,
    )
```

```python
import jax
import jax.numpy as jnp
from jax import lax
from jax.sharding import PartitionSpec as P

FACES = 12


HALF_ROOT = 0.7071067811865476
GAUSS_NORM = 0.3989422804014327


def padded_2(cells, sides, width):
    for axis, dim in sides:
        count = lax.axis_size(axis)
        ends = count - 1
        head = lax.slice_in_dim(cells, 0, width, axis=dim)
        tail = lax.slice_in_dim(cells, cells.shape[dim] - width, cells.shape[dim], axis=dim)
        cells = jnp.concatenate(
            [
                lax.ppermute(tail, axis, [(i, (i + 1) % count) for i in range(ends)]),
                cells,
                lax.ppermute(head, axis, [((i + 1) % count, i) for i in range(ends)]),
            ],
            axis=dim,
        )
    return cells


def gelu_slope(values):
    return (
        0.5 * (1.0 + lax.erf(values * HALF_ROOT))
        + values * jnp.exp(-0.5 * values * values) * GAUSS_NORM
    )


def kernel_tap(row_step, col_step):
    return (row_step + 1) * 3 + (col_step + 1)


def turned_tap(turns, row_step, col_step):
    for repeat in range(turns):
        row_step, col_step = (-col_step, row_step)
    return kernel_tap(-row_step, -col_step)


def gathered_sum(values):
    for axis in ("col", "row", "face"):
        values = jnp.sum(lax.all_gather(values, axis, axis=0, tiled=False), axis=0)
    return values


def axis_pairs(axis, step_size):
    return [(i, i ^ step_size) for i in range(lax.axis_size(axis))]


def upper(axis, step_size):
    return (lax.axis_index(axis) // step_size) % 2 == 1


def adding_step(axis, step_size):
    def send(values):
        return [lax.ppermute(values, axis, axis_pairs(axis, step_size))]

    def land(values, moved):
        return values + moved[0]

    return send, land


def grouping_step():
    def send(values):
        faces = lax.axis_size("face")
        return [
            lax.ppermute(values, "face", [(i, (i + 4) % faces) for i in range(faces)]),
            lax.ppermute(values, "face", [(i, (i + 8) % faces) for i in range(faces)]),
        ]

    def land(values, moved):
        from_before, from_after = moved
        group = lax.axis_index("face") // 4
        first = jnp.where(group == 0, values, jnp.where(group == 1, from_before, from_after))
        second = jnp.where(group == 0, from_after, jnp.where(group == 1, values, from_before))
        third = jnp.where(group == 0, from_before, jnp.where(group == 1, from_after, values))
        return (first + second) + third

    return send, land


def halving_step(axis, step_size):
    def send(values):
        half = values.shape[0] // 2
        given = jnp.where(upper(axis, step_size), values[:half], values[half:])
        return [lax.ppermute(given, axis, axis_pairs(axis, step_size))]

    def land(values, moved):
        half = values.shape[0] // 2
        return jnp.where(upper(axis, step_size), values[half:], values[:half]) + moved[0]

    return send, land


def doubling_step(axis, step_size):
    def send(values):
        return [lax.ppermute(values, axis, axis_pairs(axis, step_size))]

    def land(values, moved):
        return jnp.where(
            upper(axis, step_size),
            jnp.concatenate([moved[0], values], axis=0),
            jnp.concatenate([values, moved[0]], axis=0),
        )

    return send, land


def bits(axis):
    count = lax.axis_size(axis)
    sizes = []
    step_size = 1
    while step_size < count:
        sizes.append(step_size)
        step_size *= 2
    return sizes


def face_steps():
    return [grouping_step(), adding_step("face", 1), adding_step("face", 2)]


def butterfly_steps():
    steps = [adding_step("col", b) for b in bits("col")]
    steps += [adding_step("row", b) for b in bits("row")]
    return steps + face_steps()


def scatter_gather_steps():
    steps = [halving_step("col", b) for b in bits("col")]
    steps += [halving_step("row", b) for b in bits("row")]
    steps += face_steps()
    steps += [doubling_step("row", b) for b in reversed(bits("row"))]
    return steps + [doubling_step("col", b) for b in reversed(bits("col"))]


class Chain:
    def __init__(self, values, steps):
        self.values = values
        self.steps = steps


def lockstep(chains):
    active = [chain for chain in chains if chain.steps]
    steps = [chain.steps.pop(0) for chain in active]
    values = lax.optimization_barrier(tuple(chain.values for chain in active))
    moved = [step[0](value) for step, value in zip(steps, values)]
    for chain, step, value, arrived in zip(active, steps, values, moved):
        chain.values = step[1](value, arrived)


def run_chains(chains):
    while any(chain.steps for chain in chains):
        lockstep(chains)
    return [chain.values for chain in chains]


def lined(first_val, middle_val, last_val, length):
    middle_part = jnp.broadcast_to(middle_val[:, None], (middle_val.shape[0], length))
    return jnp.concatenate([first_val[:, None], middle_part, last_val[:, None]], axis=1)


def on_device(state, kernel, gain, shift, upstream, face_links):
    local_faces = state.shape[0]
    tile_rows = state.shape[1]
    width = kernel.shape[1]
    tile_cols = state.shape[2] // width
    row_count = lax.axis_size("row")
    col_count = lax.axis_size("col")
    side = tile_rows * row_count
    row_index = lax.axis_index("row")
    col_index = lax.axis_index("col")
    face_ids = lax.axis_index("face") * local_faces + jnp.arange(local_faces, dtype=jnp.int32)
    links = face_links[face_ids]
    face_range = jnp.arange(FACES, dtype=jnp.int32)
    side_range = jnp.arange(4, dtype=jnp.int32)
    pixel_rows = local_faces * tile_rows * tile_cols

    def extend(values, carried=None):
        def gather(part, axis, tiled):
            if carried is None or axis == "face":
                return lax.all_gather(part, axis, axis=0, tiled=tiled)
            own = Chain(part[None], [doubling_step(axis, b) for b in bits(axis)])
            while own.steps:
                lockstep([own, carried])
            return own.values

        padded = padded_2(values, (("row", 1), ("col", 2)), 1)
        row_strip = jnp.where(row_index == 0, values[:, 0], values[:, tile_rows - 1])
        col_strip = jnp.where(col_index == 0, values[:, :, 0], values[:, :, tile_cols - 1])
        by_row = gather(jnp.concatenate([row_strip, col_strip], axis=1), "row", False)
        top_seg = by_row[0, :, :tile_cols]
        bottom_seg = by_row[row_count - 1, :, :tile_cols]
        side_line = jnp.moveaxis(by_row[:, :, tile_cols:], 0, 1).reshape(local_faces, side, width)
        by_col = gather(jnp.concatenate([top_seg, bottom_seg, side_line], axis=1), "col", False)
        top_row = jnp.moveaxis(by_col[:, :, :tile_cols], 0, 1).reshape(local_faces, side, width)
        bottom_row = jnp.moveaxis(by_col[:, :, tile_cols : 2 * tile_cols], 0, 1).reshape(
            local_faces, side, width
        )
        left_col = by_col[0, :, 2 * tile_cols :]
        right_col = by_col[col_count - 1, :, 2 * tile_cols :]
        cycle = jnp.stack([top_row[:, ::-1], left_col, bottom_row, right_col[:, ::-1]], axis=1)
        all_cycle = gather(cycle, "face", True)
        all_corner = all_cycle[:, :, side - 1]
        side_pick = (
            (links[:, :4, 0][:, :, None, None] == face_range[:, None])
            & (links[:, :4, 1][:, :, None, None] == side_range)
        ).astype(jnp.bfloat16)
        halo_sides = jnp.einsum(
            "ksgt,gtpc->kspc", side_pick, all_cycle, preferred_element_type=jnp.float32
        ).astype(jnp.bfloat16)[:, :, ::-1]
        corner_pick = (
            (links[:, 4:, 0][:, :, None, None] == face_range[:, None])
            & (links[:, 4:, 1][:, :, None, None] == side_range)
            & (links[:, 4:, 3] == 0)[:, :, None, None]
        ).astype(jnp.bfloat16)
        corner_vals = jnp.einsum(
            "kqgt,gtc->kqc", corner_pick, all_corner, preferred_element_type=jnp.float32
        ).astype(jnp.bfloat16)
        full_top = jnp.concatenate(
            [corner_vals[:, 0:1], halo_sides[:, 0, ::-1], corner_vals[:, 3:4]], axis=1
        )
        full_bottom = jnp.concatenate(
            [corner_vals[:, 1:2], halo_sides[:, 2], corner_vals[:, 2:3]], axis=1
        )
        full_left = jnp.concatenate(
            [corner_vals[:, 0:1], halo_sides[:, 1], corner_vals[:, 1:2]], axis=1
        )
        full_right = jnp.concatenate(
            [corner_vals[:, 3:4], halo_sides[:, 3, ::-1], corner_vals[:, 2:3]], axis=1
        )
        top_piece = lax.dynamic_slice_in_dim(full_top, col_index * tile_cols, tile_cols + 2, 1)
        bottom_piece = lax.dynamic_slice_in_dim(
            full_bottom, col_index * tile_cols, tile_cols + 2, 1
        )
        left_piece = lax.dynamic_slice_in_dim(full_left, row_index * tile_rows, tile_rows + 2, 1)
        right_piece = lax.dynamic_slice_in_dim(full_right, row_index * tile_rows, tile_rows + 2, 1)
        padded = padded.at[:, 0].set(jnp.where(row_index == 0, top_piece, padded[:, 0]))
        padded = padded.at[:, tile_rows + 1].set(
            jnp.where(row_index == row_count - 1, bottom_piece, padded[:, tile_rows + 1])
        )
        padded = padded.at[:, :, 0].set(jnp.where(col_index == 0, left_piece, padded[:, :, 0]))
        padded = padded.at[:, :, tile_cols + 1].set(
            jnp.where(col_index == col_count - 1, right_piece, padded[:, :, tile_cols + 1])
        )
        return padded

    values = state.reshape(local_faces, tile_rows, tile_cols, width)
    padded_state = extend(values)

    def window(padded, row_step, col_step):
        return padded[
            :, 1 + row_step : 1 + row_step + tile_rows, 1 + col_step : 1 + col_step + tile_cols
        ].reshape(pixel_rows, width)

    def row_band(padded, row_step):
        return jnp.concatenate(
            [window(padded, row_step, col_step) for col_step in (-1, 0, 1)], axis=1
        )

    state_bands = [row_band(padded_state, row_step) for row_step in (-1, 0, 1)]
    response = jnp.zeros((pixel_rows, width), jnp.float32)
    for position, row_step in enumerate((-1, 0, 1)):
        band_weight = kernel[3 * position : 3 * position + 3].reshape(3 * width, width)
        response = response + jnp.dot(
            state_bands[position], band_weight, preferred_element_type=jnp.float32
        )
    total = float(FACES * side * side)
    sum_first, sum_square = gathered_sum(
        jnp.stack([jnp.sum(response, axis=0), jnp.sum(response * response, axis=0)])
    )
    centre = sum_first / total
    inverse_spread = lax.rsqrt(sum_square / total - centre * centre + 1e-05)
    normed = (response - centre) * inverse_spread
    before = gain * normed + shift
    incoming = upstream.reshape(pixel_rows, width).astype(jnp.float32)
    before_grad = incoming * gelu_slope(before)
    centred = response - centre
    state_sums = []
    centred_sums = []
    slope_sums = []
    for position in range(3):
        state_sums.append(jnp.sum(state_bands[position].astype(jnp.float32), axis=0))
        centred_sums.append(
            lax.dot_general(
                state_bands[position],
                centred,
                (((0,), (0,)), ((), ())),
                precision=lax.Precision.HIGHEST,
                preferred_element_type=jnp.float32,
            )
        )
        slope_sums.append(
            lax.dot_general(
                state_bands[position],
                before_grad,
                (((0,), (0,)), ((), ())),
                precision=lax.Precision.HIGHEST,
                preferred_element_type=jnp.float32,
            )
        )
    taps = 9
    payload = jnp.concatenate(
        [
            jnp.stack(slope_sums).reshape(-1),
            jnp.stack(centred_sums).reshape(-1),
            jnp.stack(state_sums).reshape(-1),
        ]
    )
    pieces = row_count * col_count
    padding = (-payload.shape[0]) % pieces
    carried = Chain(jnp.pad(payload, (0, padding)), scatter_gather_steps())
    stats = Chain(
        jnp.stack([jnp.sum(before_grad, axis=0), jnp.sum(before_grad * normed, axis=0)]),
        butterfly_steps(),
    )
    while stats.steps:
        lockstep([stats, carried])
    shift_grad, gain_grad = stats.values[0], stats.values[1]
    response_grad = (
        gain * inverse_spread * (before_grad - shift_grad / total - normed * gain_grad / total)
    ).astype(jnp.bfloat16)
    grad_tile = response_grad.reshape(local_faces, tile_rows, tile_cols, width)
    padded_grad = extend(grad_tile, carried)
    kernel_sums = run_chains([carried])[0]
    block = taps * width * width
    slope_total = kernel_sums[:block].reshape(taps, width, width)
    centred_total = kernel_sums[block : 2 * block].reshape(taps, width, width)
    state_total = kernel_sums[2 * block :].reshape(taps, width, 1)
    kernel_grad = (gain * inverse_spread) * (
        slope_total
        - state_total * (shift_grad / total)
        - centred_total * (gain_grad * inverse_spread / total)
    )
    zero_padded = jnp.pad(grad_tile, ((0, 0), (1, 1), (1, 1), (0, 0)))
    state_part = jnp.zeros((pixel_rows, width), jnp.float32)
    for row_step in (-1, 0, 1):
        flipped = jnp.concatenate(
            [kernel[kernel_tap(-row_step, -col_step)].T for col_step in (-1, 0, 1)], axis=0
        )
        state_part = state_part + jnp.dot(
            row_band(zero_padded, row_step), flipped, preferred_element_type=jnp.float32
        )
    state_part = state_part.reshape(local_faces, tile_rows, tile_cols, width)
    side_turns = links[:, :4, 2]
    corner_turns = links[:, 4:, 2]
    full_top_turn = lined(corner_turns[:, 0], side_turns[:, 0], corner_turns[:, 3], side)
    full_bottom_turn = lined(corner_turns[:, 1], side_turns[:, 2], corner_turns[:, 2], side)
    full_left_turn = lined(corner_turns[:, 0], side_turns[:, 1], corner_turns[:, 1], side)
    full_right_turn = lined(corner_turns[:, 3], side_turns[:, 3], corner_turns[:, 2], side)
    top_turn = jnp.where(
        row_index == 0,
        lax.dynamic_slice_in_dim(full_top_turn, col_index * tile_cols, tile_cols + 2, 1),
        0,
    )
    top_turn = top_turn.at[:, 0].set(
        jnp.where(col_index == 0, full_left_turn[:, row_index * tile_rows], top_turn[:, 0])
    )
    top_turn = top_turn.at[:, tile_cols + 1].set(
        jnp.where(
            col_index == col_count - 1,
            full_right_turn[:, row_index * tile_rows],
            top_turn[:, tile_cols + 1],
        )
    )
    bottom_turn = jnp.where(
        row_index == row_count - 1,
        lax.dynamic_slice_in_dim(full_bottom_turn, col_index * tile_cols, tile_cols + 2, 1),
        0,
    )
    bottom_turn = bottom_turn.at[:, 0].set(
        jnp.where(
            col_index == 0,
            full_left_turn[:, row_index * tile_rows + tile_rows + 1],
            bottom_turn[:, 0],
        )
    )
    bottom_turn = bottom_turn.at[:, tile_cols + 1].set(
        jnp.where(
            col_index == col_count - 1,
            full_right_turn[:, row_index * tile_rows + tile_rows + 1],
            bottom_turn[:, tile_cols + 1],
        )
    )
    left_turn = jnp.broadcast_to(
        jnp.where(col_index == 0, side_turns[:, 1], 0)[:, None], (local_faces, tile_rows + 2)
    )
    right_turn = jnp.broadcast_to(
        jnp.where(col_index == col_count - 1, side_turns[:, 3], 0)[:, None],
        (local_faces, tile_rows + 2),
    )

    def strip_terms(strip, turn_codes, steps, length):
        selector = (turn_codes[:, :, None] == side_range).astype(jnp.bfloat16)
        spread = strip[:, :, None, :] * selector[:, :, :, None]
        pieces = jnp.stack(
            [spread[:, 1 + offset : 1 + offset + length] for offset in (-1, 0, 1)], axis=2
        )
        pieces = pieces.reshape(local_faces * length, 12 * width)
        stacked = jnp.concatenate(
            [
                kernel[turned_tap(turn, step_pair[0], step_pair[1])].T
                for step_pair in steps
                for turn in range(4)
            ],
            axis=0,
        )
        summed = jnp.dot(pieces, stacked, preferred_element_type=jnp.float32)
        return summed.reshape(local_faces, length, width)

    left_strip = jnp.pad(padded_grad[:, 1 : tile_rows + 1, 0], ((0, 0), (1, 1), (0, 0)))
    right_strip = jnp.pad(
        padded_grad[:, 1 : tile_rows + 1, tile_cols + 1], ((0, 0), (1, 1), (0, 0))
    )
    top_terms = strip_terms(padded_grad[:, 0], top_turn, ((-1, -1), (-1, 0), (-1, 1)), tile_cols)
    bottom_terms = strip_terms(
        padded_grad[:, tile_rows + 1], bottom_turn, ((1, -1), (1, 0), (1, 1)), tile_cols
    )
    left_terms = strip_terms(left_strip, left_turn, ((-1, -1), (0, -1), (1, -1)), tile_rows)
    right_terms = strip_terms(right_strip, right_turn, ((-1, 1), (0, 1), (1, 1)), tile_rows)
    state_part = state_part.at[:, 0].add(top_terms)
    state_part = state_part.at[:, tile_rows - 1].add(bottom_terms)
    state_part = state_part.at[:, :, 0].add(left_terms)
    state_part = state_part.at[:, :, tile_cols - 1].add(right_terms)
    state_grad = state_part.astype(jnp.bfloat16).reshape(local_faces, tile_rows, tile_cols * width)
    return (state_grad, kernel_grad, gain_grad, shift_grad)


def solution(mesh):
    return jax.shard_map(
        on_device,
        mesh=mesh,
        in_specs=(P("face", "row", "col"), P(), P(), P(), P("face", "row", "col"), P()),
        out_specs=(P("face", "row", "col"), P(), P(), P()),
        check_vma=False,
    )
```

```python
import jax
import jax.numpy as jnp
from jax import lax
from jax.sharding import PartitionSpec as P

FACES = 12


HALF_ROOT = 0.7071067811865476
GAUSS_NORM = 0.3989422804014327


def halo_strips(cells, axis, dim):
    count = lax.axis_size(axis)
    ends = count - 1
    head = lax.slice_in_dim(cells, 0, 1, axis=dim)
    tail = lax.slice_in_dim(cells, cells.shape[dim] - 1, cells.shape[dim], axis=dim)
    from_before = lax.ppermute(tail, axis, [(i, (i + 1) % count) for i in range(ends)])
    from_after = lax.ppermute(head, axis, [((i + 1) % count, i) for i in range(ends)])
    return from_before, from_after


def gelu_slope(values):
    return (
        0.5 * (1.0 + lax.erf(values * HALF_ROOT))
        + values * jnp.exp(-0.5 * values * values) * GAUSS_NORM
    )


def kernel_tap(row_step, col_step):
    return (row_step + 1) * 3 + (col_step + 1)


def turned_tap(turns, row_step, col_step):
    for repeat in range(turns):
        row_step, col_step = (-col_step, row_step)
    return kernel_tap(-row_step, -col_step)


def nested_sum(values, carried=None):
    for axis in ("col", "row", "face"):
        if carried is None:
            values = lax.psum(values, axis)
        else:
            values = carried.beside(lambda part, axis=axis: lax.psum(part, axis), values)
    return values


def channel_pair(first_sum, second_sum, carried=None):
    return nested_sum((first_sum, second_sum), carried)


def gathered_sum(values):
    for axis in ("col", "row", "face"):
        values = jnp.sum(lax.all_gather(values, axis, axis=0, tiled=False), axis=0)
    return values


def sum_steps():
    faces = lax.axis_size("face")
    steps = [
        (
            "face",
            [
                [(i, (i + 4) % faces) for i in range(faces)],
                [(i, (i + 8) % faces) for i in range(faces)],
            ],
        ),
        ("face", [[(i, i ^ 1) for i in range(faces)]]),
        ("face", [[(i, i ^ 2) for i in range(faces)]]),
    ]
    for axis in ("row", "col"):
        count = lax.axis_size(axis)
        step = count // 2
        while step >= 1:
            steps.append((axis, [[(i, i ^ step) for i in range(count)]]))
            step //= 2
    return steps


def step_send(step, values):
    axis, pair_sets = step
    return [lax.ppermute(values, axis, pairs) for pairs in pair_sets]


def step_land(step, values, moved):
    if len(moved) == 1:
        return values + moved[0]
    from_before, from_after = moved
    group = lax.axis_index("face") // 4
    first = jnp.where(group == 0, values, jnp.where(group == 1, from_before, from_after))
    second = jnp.where(group == 0, from_after, jnp.where(group == 1, values, from_before))
    third = jnp.where(group == 0, from_before, jnp.where(group == 1, from_after, values))
    return (first + second) + third


class Carried:
    def __init__(self, values):
        self.values = values
        self.steps = sum_steps()

    def beside(self, collective, operand):
        if not self.steps:
            return collective(operand)
        step = self.steps.pop(0)
        values, operand = lax.optimization_barrier((self.values, operand))
        moved = step_send(step, values)
        result = collective(operand)
        self.values = step_land(step, values, moved)
        return result

    def doubling(self, part, axis):
        count = lax.axis_size(axis)
        index = lax.axis_index(axis)
        gathered = part[None]
        step_size = 1
        while step_size < count:
            step = self.steps.pop(0) if self.steps else None
            values, gathered = lax.optimization_barrier((self.values, gathered))
            moved = step_send(step, values) if step else None
            arrived = lax.ppermute(
                gathered, axis, [(i, i ^ step_size) for i in range(count)]
            )
            gathered = jnp.where(
                (index // step_size) % 2 == 1,
                jnp.concatenate([arrived, gathered], axis=0),
                jnp.concatenate([gathered, arrived], axis=0),
            )
            self.values = step_land(step, values, moved) if step else values
            step_size *= 2
        return gathered

    def finish(self):
        while self.steps:
            step = self.steps.pop(0)
            self.values = step_land(step, self.values, step_send(step, self.values))
        return self.values


def lined(first_val, middle_val, last_val, length):
    middle_part = jnp.broadcast_to(middle_val[:, None], (middle_val.shape[0], length))
    return jnp.concatenate([first_val[:, None], middle_part, last_val[:, None]], axis=1)


def on_device(state, kernel, gain, shift, upstream, face_links):
    local_faces = state.shape[0]
    tile_rows = state.shape[1]
    width = kernel.shape[1]
    tile_cols = state.shape[2] // width
    row_count = lax.axis_size("row")
    col_count = lax.axis_size("col")
    side = tile_rows * row_count
    row_index = lax.axis_index("row")
    col_index = lax.axis_index("col")
    face_ids = lax.axis_index("face") * local_faces + jnp.arange(local_faces, dtype=jnp.int32)
    links = face_links[face_ids]
    face_range = jnp.arange(FACES, dtype=jnp.int32)
    side_range = jnp.arange(4, dtype=jnp.int32)
    pixel_rows = local_faces * tile_rows * tile_cols

    def extend(values, carried=None):
        def gather(part, axis, tiled):
            if carried is None or axis == "face":
                return lax.all_gather(part, axis, axis=0, tiled=tiled)
            return carried.doubling(part, axis)

        row_strip = jnp.where(row_index == 0, values[:, 0], values[:, tile_rows - 1])
        col_strip = jnp.where(col_index == 0, values[:, :, 0], values[:, :, tile_cols - 1])
        above, below = halo_strips(values, "row", 1)
        by_row = gather(jnp.concatenate([row_strip, col_strip], axis=1), "row", False)
        above, below, by_row = lax.optimization_barrier((above, below, by_row))
        padded = jnp.concatenate([above, values, below], axis=1)
        before_col, after_col = halo_strips(padded, "col", 2)
        top_seg = by_row[0, :, :tile_cols]
        bottom_seg = by_row[row_count - 1, :, :tile_cols]
        side_line = jnp.moveaxis(by_row[:, :, tile_cols:], 0, 1).reshape(local_faces, side, width)
        by_col = gather(jnp.concatenate([top_seg, bottom_seg, side_line], axis=1), "col", False)
        before_col, after_col, by_col = lax.optimization_barrier((before_col, after_col, by_col))
        padded = jnp.concatenate([before_col, padded, after_col], axis=2)
        top_row = jnp.moveaxis(by_col[:, :, :tile_cols], 0, 1).reshape(local_faces, side, width)
        bottom_row = jnp.moveaxis(by_col[:, :, tile_cols : 2 * tile_cols], 0, 1).reshape(
            local_faces, side, width
        )
        left_col = by_col[0, :, 2 * tile_cols :]
        right_col = by_col[col_count - 1, :, 2 * tile_cols :]
        cycle = jnp.stack([top_row[:, ::-1], left_col, bottom_row, right_col[:, ::-1]], axis=1)
        all_cycle = gather(cycle, "face", True)
        all_corner = all_cycle[:, :, side - 1]
        side_pick = (
            (links[:, :4, 0][:, :, None, None] == face_range[:, None])
            & (links[:, :4, 1][:, :, None, None] == side_range)
        ).astype(jnp.bfloat16)
        halo_sides = jnp.einsum(
            "ksgt,gtpc->kspc", side_pick, all_cycle, preferred_element_type=jnp.float32
        ).astype(jnp.bfloat16)[:, :, ::-1]
        corner_pick = (
            (links[:, 4:, 0][:, :, None, None] == face_range[:, None])
            & (links[:, 4:, 1][:, :, None, None] == side_range)
            & (links[:, 4:, 3] == 0)[:, :, None, None]
        ).astype(jnp.bfloat16)
        corner_vals = jnp.einsum(
            "kqgt,gtc->kqc", corner_pick, all_corner, preferred_element_type=jnp.float32
        ).astype(jnp.bfloat16)
        full_top = jnp.concatenate(
            [corner_vals[:, 0:1], halo_sides[:, 0, ::-1], corner_vals[:, 3:4]], axis=1
        )
        full_bottom = jnp.concatenate(
            [corner_vals[:, 1:2], halo_sides[:, 2], corner_vals[:, 2:3]], axis=1
        )
        full_left = jnp.concatenate(
            [corner_vals[:, 0:1], halo_sides[:, 1], corner_vals[:, 1:2]], axis=1
        )
        full_right = jnp.concatenate(
            [corner_vals[:, 3:4], halo_sides[:, 3, ::-1], corner_vals[:, 2:3]], axis=1
        )
        top_piece = lax.dynamic_slice_in_dim(full_top, col_index * tile_cols, tile_cols + 2, 1)
        bottom_piece = lax.dynamic_slice_in_dim(
            full_bottom, col_index * tile_cols, tile_cols + 2, 1
        )
        left_piece = lax.dynamic_slice_in_dim(full_left, row_index * tile_rows, tile_rows + 2, 1)
        right_piece = lax.dynamic_slice_in_dim(full_right, row_index * tile_rows, tile_rows + 2, 1)
        padded = padded.at[:, 0].set(jnp.where(row_index == 0, top_piece, padded[:, 0]))
        padded = padded.at[:, tile_rows + 1].set(
            jnp.where(row_index == row_count - 1, bottom_piece, padded[:, tile_rows + 1])
        )
        padded = padded.at[:, :, 0].set(jnp.where(col_index == 0, left_piece, padded[:, :, 0]))
        padded = padded.at[:, :, tile_cols + 1].set(
            jnp.where(col_index == col_count - 1, right_piece, padded[:, :, tile_cols + 1])
        )
        return padded

    values = state.reshape(local_faces, tile_rows, tile_cols, width)
    padded_state = extend(values)

    def window(padded, row_step, col_step):
        return padded[
            :, 1 + row_step : 1 + row_step + tile_rows, 1 + col_step : 1 + col_step + tile_cols
        ].reshape(pixel_rows, width)

    def row_band(padded, row_step):
        return jnp.concatenate(
            [window(padded, row_step, col_step) for col_step in (-1, 0, 1)], axis=1
        )

    state_bands = [row_band(padded_state, row_step) for row_step in (-1, 0, 1)]
    response = jnp.zeros((pixel_rows, width), jnp.float32)
    for position, row_step in enumerate((-1, 0, 1)):
        band_weight = kernel[3 * position : 3 * position + 3].reshape(3 * width, width)
        response = response + jnp.dot(
            state_bands[position], band_weight, preferred_element_type=jnp.float32
        )
    total = float(FACES * side * side)
    sum_first, sum_square = gathered_sum(
        jnp.stack([jnp.sum(response, axis=0), jnp.sum(response * response, axis=0)])
    )
    centre = sum_first / total
    inverse_spread = lax.rsqrt(sum_square / total - centre * centre + 1e-05)
    normed = (response - centre) * inverse_spread
    before = gain * normed + shift
    incoming = upstream.reshape(pixel_rows, width).astype(jnp.float32)
    before_grad = incoming * gelu_slope(before)
    centred = response - centre
    state_sums = []
    centred_sums = []
    slope_sums = []
    for position in range(3):
        state_sums.append(jnp.sum(state_bands[position].astype(jnp.float32), axis=0))
        centred_sums.append(
            lax.dot_general(
                state_bands[position],
                centred,
                (((0,), (0,)), ((), ())),
                precision=lax.Precision.HIGHEST,
                preferred_element_type=jnp.float32,
            )
        )
        slope_sums.append(
            lax.dot_general(
                state_bands[position],
                before_grad,
                (((0,), (0,)), ((), ())),
                precision=lax.Precision.HIGHEST,
                preferred_element_type=jnp.float32,
            )
        )
    taps = 9
    carried = Carried(
        jnp.concatenate(
            [
                jnp.stack(slope_sums).reshape(-1),
                jnp.stack(centred_sums).reshape(-1),
                jnp.stack(state_sums).reshape(-1),
            ]
        )
    )
    shift_grad, gain_grad = channel_pair(
        jnp.sum(before_grad, axis=0), jnp.sum(before_grad * normed, axis=0), carried
    )
    response_grad = (
        gain * inverse_spread * (before_grad - shift_grad / total - normed * gain_grad / total)
    ).astype(jnp.bfloat16)
    grad_tile = response_grad.reshape(local_faces, tile_rows, tile_cols, width)
    padded_grad = extend(grad_tile, carried)
    kernel_sums = carried.finish()
    block = taps * width * width
    slope_total = kernel_sums[:block].reshape(taps, width, width)
    centred_total = kernel_sums[block : 2 * block].reshape(taps, width, width)
    state_total = kernel_sums[2 * block :].reshape(taps, width, 1)
    kernel_grad = (gain * inverse_spread) * (
        slope_total
        - state_total * (shift_grad / total)
        - centred_total * (gain_grad * inverse_spread / total)
    )
    zero_padded = jnp.pad(grad_tile, ((0, 0), (1, 1), (1, 1), (0, 0)))
    state_part = jnp.zeros((pixel_rows, width), jnp.float32)
    for row_step in (-1, 0, 1):
        flipped = jnp.concatenate(
            [kernel[kernel_tap(-row_step, -col_step)].T for col_step in (-1, 0, 1)], axis=0
        )
        state_part = state_part + jnp.dot(
            row_band(zero_padded, row_step), flipped, preferred_element_type=jnp.float32
        )
    state_part = state_part.reshape(local_faces, tile_rows, tile_cols, width)
    side_turns = links[:, :4, 2]
    corner_turns = links[:, 4:, 2]
    full_top_turn = lined(corner_turns[:, 0], side_turns[:, 0], corner_turns[:, 3], side)
    full_bottom_turn = lined(corner_turns[:, 1], side_turns[:, 2], corner_turns[:, 2], side)
    full_left_turn = lined(corner_turns[:, 0], side_turns[:, 1], corner_turns[:, 1], side)
    full_right_turn = lined(corner_turns[:, 3], side_turns[:, 3], corner_turns[:, 2], side)
    top_turn = jnp.where(
        row_index == 0,
        lax.dynamic_slice_in_dim(full_top_turn, col_index * tile_cols, tile_cols + 2, 1),
        0,
    )
    top_turn = top_turn.at[:, 0].set(
        jnp.where(col_index == 0, full_left_turn[:, row_index * tile_rows], top_turn[:, 0])
    )
    top_turn = top_turn.at[:, tile_cols + 1].set(
        jnp.where(
            col_index == col_count - 1,
            full_right_turn[:, row_index * tile_rows],
            top_turn[:, tile_cols + 1],
        )
    )
    bottom_turn = jnp.where(
        row_index == row_count - 1,
        lax.dynamic_slice_in_dim(full_bottom_turn, col_index * tile_cols, tile_cols + 2, 1),
        0,
    )
    bottom_turn = bottom_turn.at[:, 0].set(
        jnp.where(
            col_index == 0,
            full_left_turn[:, row_index * tile_rows + tile_rows + 1],
            bottom_turn[:, 0],
        )
    )
    bottom_turn = bottom_turn.at[:, tile_cols + 1].set(
        jnp.where(
            col_index == col_count - 1,
            full_right_turn[:, row_index * tile_rows + tile_rows + 1],
            bottom_turn[:, tile_cols + 1],
        )
    )
    left_turn = jnp.broadcast_to(
        jnp.where(col_index == 0, side_turns[:, 1], 0)[:, None], (local_faces, tile_rows + 2)
    )
    right_turn = jnp.broadcast_to(
        jnp.where(col_index == col_count - 1, side_turns[:, 3], 0)[:, None],
        (local_faces, tile_rows + 2),
    )

    def strip_terms(strip, turn_codes, steps, length):
        selector = (turn_codes[:, :, None] == side_range).astype(jnp.bfloat16)
        spread = strip[:, :, None, :] * selector[:, :, :, None]
        pieces = jnp.stack(
            [spread[:, 1 + offset : 1 + offset + length] for offset in (-1, 0, 1)], axis=2
        )
        pieces = pieces.reshape(local_faces * length, 12 * width)
        stacked = jnp.concatenate(
            [
                kernel[turned_tap(turn, step_pair[0], step_pair[1])].T
                for step_pair in steps
                for turn in range(4)
            ],
            axis=0,
        )
        summed = jnp.dot(pieces, stacked, preferred_element_type=jnp.float32)
        return summed.reshape(local_faces, length, width)

    left_strip = jnp.pad(padded_grad[:, 1 : tile_rows + 1, 0], ((0, 0), (1, 1), (0, 0)))
    right_strip = jnp.pad(
        padded_grad[:, 1 : tile_rows + 1, tile_cols + 1], ((0, 0), (1, 1), (0, 0))
    )
    top_terms = strip_terms(padded_grad[:, 0], top_turn, ((-1, -1), (-1, 0), (-1, 1)), tile_cols)
    bottom_terms = strip_terms(
        padded_grad[:, tile_rows + 1], bottom_turn, ((1, -1), (1, 0), (1, 1)), tile_cols
    )
    left_terms = strip_terms(left_strip, left_turn, ((-1, -1), (0, -1), (1, -1)), tile_rows)
    right_terms = strip_terms(right_strip, right_turn, ((-1, 1), (0, 1), (1, 1)), tile_rows)
    state_part = state_part.at[:, 0].add(top_terms)
    state_part = state_part.at[:, tile_rows - 1].add(bottom_terms)
    state_part = state_part.at[:, :, 0].add(left_terms)
    state_part = state_part.at[:, :, tile_cols - 1].add(right_terms)
    state_grad = state_part.astype(jnp.bfloat16).reshape(local_faces, tile_rows, tile_cols * width)
    return (state_grad, kernel_grad, gain_grad, shift_grad)


def solution(mesh):
    return jax.shard_map(
        on_device,
        mesh=mesh,
        in_specs=(P("face", "row", "col"), P(), P(), P(), P("face", "row", "col"), P()),
        out_specs=(P("face", "row", "col"), P(), P(), P()),
        check_vma=False,
    )
```

```python
import jax
import jax.numpy as jnp
from jax import lax
from jax.sharding import PartitionSpec as P

FACES = 12


HALF_ROOT = 0.7071067811865476
GAUSS_NORM = 0.3989422804014327


def halo_strips(cells, axis, dim):
    count = lax.axis_size(axis)
    ends = count - 1
    head = lax.slice_in_dim(cells, 0, 1, axis=dim)
    tail = lax.slice_in_dim(cells, cells.shape[dim] - 1, cells.shape[dim], axis=dim)
    from_before = lax.ppermute(tail, axis, [(i, (i + 1) % count) for i in range(ends)])
    from_after = lax.ppermute(head, axis, [((i + 1) % count, i) for i in range(ends)])
    return from_before, from_after


def gelu_slope(values):
    return (
        0.5 * (1.0 + lax.erf(values * HALF_ROOT))
        + values * jnp.exp(-0.5 * values * values) * GAUSS_NORM
    )


def kernel_tap(row_step, col_step):
    return (row_step + 1) * 3 + (col_step + 1)


def turned_tap(turns, row_step, col_step):
    for repeat in range(turns):
        row_step, col_step = (-col_step, row_step)
    return kernel_tap(-row_step, -col_step)


def nested_sum(values, carried=None):
    for axis in ("col", "row", "face"):
        if carried is None:
            values = lax.psum(values, axis)
        else:
            values = carried.beside(
                lambda part, axis=axis: jnp.sum(
                    lax.all_gather(part, axis, axis=0, tiled=False), axis=0
                ),
                values,
            )
    return values


def channel_pair(first_sum, second_sum, carried=None):
    both = nested_sum(jnp.stack([first_sum, second_sum]), carried)
    return both[0], both[1]


def gathered_sum(values):
    for axis in ("col", "row", "face"):
        values = jnp.sum(lax.all_gather(values, axis, axis=0, tiled=False), axis=0)
    return values


def sum_steps():
    faces = lax.axis_size("face")
    steps = [
        (
            "face",
            [
                [(i, (i + 4) % faces) for i in range(faces)],
                [(i, (i + 8) % faces) for i in range(faces)],
            ],
        ),
        ("face", [[(i, i ^ 1) for i in range(faces)]]),
        ("face", [[(i, i ^ 2) for i in range(faces)]]),
    ]
    for axis in ("row", "col"):
        count = lax.axis_size(axis)
        step = count // 2
        while step >= 1:
            steps.append((axis, [[(i, i ^ step) for i in range(count)]]))
            step //= 2
    return steps


def step_send(step, values):
    axis, pair_sets = step
    return [lax.ppermute(values, axis, pairs) for pairs in pair_sets]


def step_land(step, values, moved):
    if len(moved) == 1:
        return values + moved[0]
    from_before, from_after = moved
    group = lax.axis_index("face") // 4
    first = jnp.where(group == 0, values, jnp.where(group == 1, from_before, from_after))
    second = jnp.where(group == 0, from_after, jnp.where(group == 1, values, from_before))
    third = jnp.where(group == 0, from_before, jnp.where(group == 1, from_after, values))
    return (first + second) + third


class Carried:
    def __init__(self, values):
        self.values = values
        self.steps = sum_steps()

    def beside(self, collective, operand):
        if not self.steps:
            return collective(operand)
        step = self.steps.pop(0)
        values, operand = lax.optimization_barrier((self.values, operand))
        moved = step_send(step, values)
        result = collective(operand)
        self.values = step_land(step, values, moved)
        return result

    def doubling(self, part, axis):
        count = lax.axis_size(axis)
        index = lax.axis_index(axis)
        gathered = part[None]
        step_size = 1
        while step_size < count:
            step = self.steps.pop(0) if self.steps else None
            values, gathered = lax.optimization_barrier((self.values, gathered))
            moved = step_send(step, values) if step else None
            arrived = lax.ppermute(
                gathered, axis, [(i, i ^ step_size) for i in range(count)]
            )
            gathered = jnp.where(
                (index // step_size) % 2 == 1,
                jnp.concatenate([arrived, gathered], axis=0),
                jnp.concatenate([gathered, arrived], axis=0),
            )
            self.values = step_land(step, values, moved) if step else values
            step_size *= 2
        return gathered

    def finish(self):
        while self.steps:
            step = self.steps.pop(0)
            self.values = step_land(step, self.values, step_send(step, self.values))
        return self.values


def lined(first_val, middle_val, last_val, length):
    middle_part = jnp.broadcast_to(middle_val[:, None], (middle_val.shape[0], length))
    return jnp.concatenate([first_val[:, None], middle_part, last_val[:, None]], axis=1)


def on_device(state, kernel, gain, shift, upstream, face_links):
    local_faces = state.shape[0]
    tile_rows = state.shape[1]
    width = kernel.shape[1]
    tile_cols = state.shape[2] // width
    row_count = lax.axis_size("row")
    col_count = lax.axis_size("col")
    side = tile_rows * row_count
    row_index = lax.axis_index("row")
    col_index = lax.axis_index("col")
    face_ids = lax.axis_index("face") * local_faces + jnp.arange(local_faces, dtype=jnp.int32)
    links = face_links[face_ids]
    face_range = jnp.arange(FACES, dtype=jnp.int32)
    side_range = jnp.arange(4, dtype=jnp.int32)
    pixel_rows = local_faces * tile_rows * tile_cols

    def extend(values, carried=None):
        def gather(part, axis, tiled):
            if carried is None or axis == "face":
                return lax.all_gather(part, axis, axis=0, tiled=tiled)
            return carried.doubling(part, axis)

        row_strip = jnp.where(row_index == 0, values[:, 0], values[:, tile_rows - 1])
        col_strip = jnp.where(col_index == 0, values[:, :, 0], values[:, :, tile_cols - 1])
        above, below = halo_strips(values, "row", 1)
        by_row = gather(jnp.concatenate([row_strip, col_strip], axis=1), "row", False)
        above, below, by_row = lax.optimization_barrier((above, below, by_row))
        padded = jnp.concatenate([above, values, below], axis=1)
        before_col, after_col = halo_strips(padded, "col", 2)
        top_seg = by_row[0, :, :tile_cols]
        bottom_seg = by_row[row_count - 1, :, :tile_cols]
        side_line = jnp.moveaxis(by_row[:, :, tile_cols:], 0, 1).reshape(local_faces, side, width)
        by_col = gather(jnp.concatenate([top_seg, bottom_seg, side_line], axis=1), "col", False)
        before_col, after_col, by_col = lax.optimization_barrier((before_col, after_col, by_col))
        padded = jnp.concatenate([before_col, padded, after_col], axis=2)
        top_row = jnp.moveaxis(by_col[:, :, :tile_cols], 0, 1).reshape(local_faces, side, width)
        bottom_row = jnp.moveaxis(by_col[:, :, tile_cols : 2 * tile_cols], 0, 1).reshape(
            local_faces, side, width
        )
        left_col = by_col[0, :, 2 * tile_cols :]
        right_col = by_col[col_count - 1, :, 2 * tile_cols :]
        cycle = jnp.stack([top_row[:, ::-1], left_col, bottom_row, right_col[:, ::-1]], axis=1)
        all_cycle = gather(cycle, "face", True)
        all_corner = all_cycle[:, :, side - 1]
        side_pick = (
            (links[:, :4, 0][:, :, None, None] == face_range[:, None])
            & (links[:, :4, 1][:, :, None, None] == side_range)
        ).astype(jnp.bfloat16)
        halo_sides = jnp.einsum(
            "ksgt,gtpc->kspc", side_pick, all_cycle, preferred_element_type=jnp.float32
        ).astype(jnp.bfloat16)[:, :, ::-1]
        corner_pick = (
            (links[:, 4:, 0][:, :, None, None] == face_range[:, None])
            & (links[:, 4:, 1][:, :, None, None] == side_range)
            & (links[:, 4:, 3] == 0)[:, :, None, None]
        ).astype(jnp.bfloat16)
        corner_vals = jnp.einsum(
            "kqgt,gtc->kqc", corner_pick, all_corner, preferred_element_type=jnp.float32
        ).astype(jnp.bfloat16)
        full_top = jnp.concatenate(
            [corner_vals[:, 0:1], halo_sides[:, 0, ::-1], corner_vals[:, 3:4]], axis=1
        )
        full_bottom = jnp.concatenate(
            [corner_vals[:, 1:2], halo_sides[:, 2], corner_vals[:, 2:3]], axis=1
        )
        full_left = jnp.concatenate(
            [corner_vals[:, 0:1], halo_sides[:, 1], corner_vals[:, 1:2]], axis=1
        )
        full_right = jnp.concatenate(
            [corner_vals[:, 3:4], halo_sides[:, 3, ::-1], corner_vals[:, 2:3]], axis=1
        )
        top_piece = lax.dynamic_slice_in_dim(full_top, col_index * tile_cols, tile_cols + 2, 1)
        bottom_piece = lax.dynamic_slice_in_dim(
            full_bottom, col_index * tile_cols, tile_cols + 2, 1
        )
        left_piece = lax.dynamic_slice_in_dim(full_left, row_index * tile_rows, tile_rows + 2, 1)
        right_piece = lax.dynamic_slice_in_dim(full_right, row_index * tile_rows, tile_rows + 2, 1)
        padded = padded.at[:, 0].set(jnp.where(row_index == 0, top_piece, padded[:, 0]))
        padded = padded.at[:, tile_rows + 1].set(
            jnp.where(row_index == row_count - 1, bottom_piece, padded[:, tile_rows + 1])
        )
        padded = padded.at[:, :, 0].set(jnp.where(col_index == 0, left_piece, padded[:, :, 0]))
        padded = padded.at[:, :, tile_cols + 1].set(
            jnp.where(col_index == col_count - 1, right_piece, padded[:, :, tile_cols + 1])
        )
        return padded

    values = state.reshape(local_faces, tile_rows, tile_cols, width)
    padded_state = extend(values)

    def window(padded, row_step, col_step):
        return padded[
            :, 1 + row_step : 1 + row_step + tile_rows, 1 + col_step : 1 + col_step + tile_cols
        ].reshape(pixel_rows, width)

    def row_band(padded, row_step):
        return jnp.concatenate(
            [window(padded, row_step, col_step) for col_step in (-1, 0, 1)], axis=1
        )

    state_bands = [row_band(padded_state, row_step) for row_step in (-1, 0, 1)]
    response = jnp.zeros((pixel_rows, width), jnp.float32)
    for position, row_step in enumerate((-1, 0, 1)):
        band_weight = kernel[3 * position : 3 * position + 3].reshape(3 * width, width)
        response = response + jnp.dot(
            state_bands[position], band_weight, preferred_element_type=jnp.float32
        )
    total = float(FACES * side * side)
    sum_first, sum_square = gathered_sum(
        jnp.stack([jnp.sum(response, axis=0), jnp.sum(response * response, axis=0)])
    )
    centre = sum_first / total
    inverse_spread = lax.rsqrt(sum_square / total - centre * centre + 1e-05)
    normed = (response - centre) * inverse_spread
    before = gain * normed + shift
    incoming = upstream.reshape(pixel_rows, width).astype(jnp.float32)
    before_grad = incoming * gelu_slope(before)
    centred = response - centre
    state_sums = []
    centred_sums = []
    slope_sums = []
    for position in range(3):
        state_sums.append(jnp.sum(state_bands[position].astype(jnp.float32), axis=0))
        centred_sums.append(
            lax.dot_general(
                state_bands[position],
                centred,
                (((0,), (0,)), ((), ())),
                precision=lax.Precision.HIGHEST,
                preferred_element_type=jnp.float32,
            )
        )
        slope_sums.append(
            lax.dot_general(
                state_bands[position],
                before_grad,
                (((0,), (0,)), ((), ())),
                precision=lax.Precision.HIGHEST,
                preferred_element_type=jnp.float32,
            )
        )
    taps = 9
    carried = Carried(
        jnp.concatenate(
            [
                jnp.stack(slope_sums).reshape(-1),
                jnp.stack(centred_sums).reshape(-1),
                jnp.stack(state_sums).reshape(-1),
            ]
        )
    )
    shift_grad, gain_grad = channel_pair(
        jnp.sum(before_grad, axis=0), jnp.sum(before_grad * normed, axis=0), carried
    )
    response_grad = (
        gain * inverse_spread * (before_grad - shift_grad / total - normed * gain_grad / total)
    ).astype(jnp.bfloat16)
    grad_tile = response_grad.reshape(local_faces, tile_rows, tile_cols, width)
    padded_grad = extend(grad_tile, carried)
    kernel_sums = carried.finish()
    block = taps * width * width
    slope_total = kernel_sums[:block].reshape(taps, width, width)
    centred_total = kernel_sums[block : 2 * block].reshape(taps, width, width)
    state_total = kernel_sums[2 * block :].reshape(taps, width, 1)
    kernel_grad = (gain * inverse_spread) * (
        slope_total
        - state_total * (shift_grad / total)
        - centred_total * (gain_grad * inverse_spread / total)
    )
    zero_padded = jnp.pad(grad_tile, ((0, 0), (1, 1), (1, 1), (0, 0)))
    state_part = jnp.zeros((pixel_rows, width), jnp.float32)
    for row_step in (-1, 0, 1):
        flipped = jnp.concatenate(
            [kernel[kernel_tap(-row_step, -col_step)].T for col_step in (-1, 0, 1)], axis=0
        )
        state_part = state_part + jnp.dot(
            row_band(zero_padded, row_step), flipped, preferred_element_type=jnp.float32
        )
    state_part = state_part.reshape(local_faces, tile_rows, tile_cols, width)
    side_turns = links[:, :4, 2]
    corner_turns = links[:, 4:, 2]
    full_top_turn = lined(corner_turns[:, 0], side_turns[:, 0], corner_turns[:, 3], side)
    full_bottom_turn = lined(corner_turns[:, 1], side_turns[:, 2], corner_turns[:, 2], side)
    full_left_turn = lined(corner_turns[:, 0], side_turns[:, 1], corner_turns[:, 1], side)
    full_right_turn = lined(corner_turns[:, 3], side_turns[:, 3], corner_turns[:, 2], side)
    top_turn = jnp.where(
        row_index == 0,
        lax.dynamic_slice_in_dim(full_top_turn, col_index * tile_cols, tile_cols + 2, 1),
        0,
    )
    top_turn = top_turn.at[:, 0].set(
        jnp.where(col_index == 0, full_left_turn[:, row_index * tile_rows], top_turn[:, 0])
    )
    top_turn = top_turn.at[:, tile_cols + 1].set(
        jnp.where(
            col_index == col_count - 1,
            full_right_turn[:, row_index * tile_rows],
            top_turn[:, tile_cols + 1],
        )
    )
    bottom_turn = jnp.where(
        row_index == row_count - 1,
        lax.dynamic_slice_in_dim(full_bottom_turn, col_index * tile_cols, tile_cols + 2, 1),
        0,
    )
    bottom_turn = bottom_turn.at[:, 0].set(
        jnp.where(
            col_index == 0,
            full_left_turn[:, row_index * tile_rows + tile_rows + 1],
            bottom_turn[:, 0],
        )
    )
    bottom_turn = bottom_turn.at[:, tile_cols + 1].set(
        jnp.where(
            col_index == col_count - 1,
            full_right_turn[:, row_index * tile_rows + tile_rows + 1],
            bottom_turn[:, tile_cols + 1],
        )
    )
    left_turn = jnp.broadcast_to(
        jnp.where(col_index == 0, side_turns[:, 1], 0)[:, None], (local_faces, tile_rows + 2)
    )
    right_turn = jnp.broadcast_to(
        jnp.where(col_index == col_count - 1, side_turns[:, 3], 0)[:, None],
        (local_faces, tile_rows + 2),
    )

    def strip_terms(strip, turn_codes, steps, length):
        selector = (turn_codes[:, :, None] == side_range).astype(jnp.bfloat16)
        spread = strip[:, :, None, :] * selector[:, :, :, None]
        pieces = jnp.stack(
            [spread[:, 1 + offset : 1 + offset + length] for offset in (-1, 0, 1)], axis=2
        )
        pieces = pieces.reshape(local_faces * length, 12 * width)
        stacked = jnp.concatenate(
            [
                kernel[turned_tap(turn, step_pair[0], step_pair[1])].T
                for step_pair in steps
                for turn in range(4)
            ],
            axis=0,
        )
        summed = jnp.dot(pieces, stacked, preferred_element_type=jnp.float32)
        return summed.reshape(local_faces, length, width)

    left_strip = jnp.pad(padded_grad[:, 1 : tile_rows + 1, 0], ((0, 0), (1, 1), (0, 0)))
    right_strip = jnp.pad(
        padded_grad[:, 1 : tile_rows + 1, tile_cols + 1], ((0, 0), (1, 1), (0, 0))
    )
    top_terms = strip_terms(padded_grad[:, 0], top_turn, ((-1, -1), (-1, 0), (-1, 1)), tile_cols)
    bottom_terms = strip_terms(
        padded_grad[:, tile_rows + 1], bottom_turn, ((1, -1), (1, 0), (1, 1)), tile_cols
    )
    left_terms = strip_terms(left_strip, left_turn, ((-1, -1), (0, -1), (1, -1)), tile_rows)
    right_terms = strip_terms(right_strip, right_turn, ((-1, 1), (0, 1), (1, 1)), tile_rows)
    state_part = state_part.at[:, 0].add(top_terms)
    state_part = state_part.at[:, tile_rows - 1].add(bottom_terms)
    state_part = state_part.at[:, :, 0].add(left_terms)
    state_part = state_part.at[:, :, tile_cols - 1].add(right_terms)
    state_grad = state_part.astype(jnp.bfloat16).reshape(local_faces, tile_rows, tile_cols * width)
    return (state_grad, kernel_grad, gain_grad, shift_grad)


def solution(mesh):
    return jax.shard_map(
        on_device,
        mesh=mesh,
        in_specs=(P("face", "row", "col"), P(), P(), P(), P("face", "row", "col"), P()),
        out_specs=(P("face", "row", "col"), P(), P(), P()),
        check_vma=False,
    )
```

```python
import jax
import jax.numpy as jnp
from jax import lax
from jax.sharding import PartitionSpec as P

FACES = 12


HALF_ROOT = 0.7071067811865476
GAUSS_NORM = 0.3989422804014327


def halo_strips(cells, axis, dim):
    count = lax.axis_size(axis)
    ends = count - 1
    head = lax.slice_in_dim(cells, 0, 1, axis=dim)
    tail = lax.slice_in_dim(cells, cells.shape[dim] - 1, cells.shape[dim], axis=dim)
    from_before = lax.ppermute(tail, axis, [(i, (i + 1) % count) for i in range(ends)])
    from_after = lax.ppermute(head, axis, [((i + 1) % count, i) for i in range(ends)])
    return from_before, from_after


def gelu_slope(values):
    return (
        0.5 * (1.0 + lax.erf(values * HALF_ROOT))
        + values * jnp.exp(-0.5 * values * values) * GAUSS_NORM
    )


def kernel_tap(row_step, col_step):
    return (row_step + 1) * 3 + (col_step + 1)


def turned_tap(turns, row_step, col_step):
    for repeat in range(turns):
        row_step, col_step = (-col_step, row_step)
    return kernel_tap(-row_step, -col_step)


def nested_sum(values, carried=None):
    for axis in ("col", "row", "face"):
        if carried is None:
            values = lax.psum(values, axis)
        else:
            values = carried.beside(
                lambda part, axis=axis: jnp.sum(
                    lax.all_gather(part, axis, axis=0, tiled=False), axis=0
                ),
                values,
            )
    return values


def channel_pair(first_sum, second_sum, carried=None):
    both = nested_sum(jnp.stack([first_sum, second_sum]), carried)
    return both[0], both[1]


def gathered_sum(values):
    for axis in ("col", "row", "face"):
        values = jnp.sum(lax.all_gather(values, axis, axis=0, tiled=False), axis=0)
    return values


def sum_steps():
    faces = lax.axis_size("face")
    steps = [
        (
            "face",
            [
                [(i, (i + 4) % faces) for i in range(faces)],
                [(i, (i + 8) % faces) for i in range(faces)],
            ],
        ),
        ("face", [[(i, i ^ 1) for i in range(faces)]]),
        ("face", [[(i, i ^ 2) for i in range(faces)]]),
    ]
    for axis in ("row", "col"):
        count = lax.axis_size(axis)
        step = count // 2
        while step >= 1:
            steps.append((axis, [[(i, i ^ step) for i in range(count)]]))
            step //= 2
    return steps


def step_send(step, values):
    axis, pair_sets = step
    return [lax.ppermute(values, axis, pairs) for pairs in pair_sets]


def step_land(step, values, moved):
    if len(moved) == 1:
        return values + moved[0]
    from_before, from_after = moved
    group = lax.axis_index("face") // 4
    first = jnp.where(group == 0, values, jnp.where(group == 1, from_before, from_after))
    second = jnp.where(group == 0, from_after, jnp.where(group == 1, values, from_before))
    third = jnp.where(group == 0, from_before, jnp.where(group == 1, from_after, values))
    return (first + second) + third


class Carried:
    def __init__(self, values):
        self.values = values
        self.steps = sum_steps()

    def beside(self, collective, operand):
        if not self.steps:
            return collective(operand)
        step = self.steps.pop(0)
        values, operand = lax.optimization_barrier((self.values, operand))
        moved = step_send(step, values)
        result = collective(operand)
        self.values = step_land(step, values, moved)
        return result

    def doubling(self, part, axis):
        count = lax.axis_size(axis)
        index = lax.axis_index(axis)
        gathered = part[None]
        step_size = 1
        while step_size < count:
            step = self.steps.pop(0) if self.steps else None
            values, gathered = lax.optimization_barrier((self.values, gathered))
            moved = step_send(step, values) if step else None
            arrived = lax.ppermute(
                gathered, axis, [(i, i ^ step_size) for i in range(count)]
            )
            gathered = jnp.where(
                (index // step_size) % 2 == 1,
                jnp.concatenate([arrived, gathered], axis=0),
                jnp.concatenate([gathered, arrived], axis=0),
            )
            self.values = step_land(step, values, moved) if step else values
            step_size *= 2
        return gathered

    def finish(self):
        while self.steps:
            step = self.steps.pop(0)
            self.values = step_land(step, self.values, step_send(step, self.values))
        return self.values


def lined(first_val, middle_val, last_val, length):
    middle_part = jnp.broadcast_to(middle_val[:, None], (middle_val.shape[0], length))
    return jnp.concatenate([first_val[:, None], middle_part, last_val[:, None]], axis=1)


def on_device(state, kernel, gain, shift, upstream, face_links):
    local_faces = state.shape[0]
    tile_rows = state.shape[1]
    width = kernel.shape[1]
    tile_cols = state.shape[2] // width
    row_count = lax.axis_size("row")
    col_count = lax.axis_size("col")
    side = tile_rows * row_count
    row_index = lax.axis_index("row")
    col_index = lax.axis_index("col")
    face_ids = lax.axis_index("face") * local_faces + jnp.arange(local_faces, dtype=jnp.int32)
    links = face_links[face_ids]
    face_range = jnp.arange(FACES, dtype=jnp.int32)
    side_range = jnp.arange(4, dtype=jnp.int32)
    pixel_rows = local_faces * tile_rows * tile_cols

    def extend(values, carried=None):
        def gather(part, axis, tiled):
            if carried is None or axis == "face":
                return lax.all_gather(part, axis, axis=0, tiled=tiled)
            return carried.doubling(part, axis)

        col_strip = jnp.where(col_index == 0, values[:, :, 0], values[:, :, tile_cols - 1])
        by_row = gather(
            jnp.concatenate([values[:, 0], values[:, tile_rows - 1], col_strip], axis=1), "row", False
        )
        above = lax.dynamic_index_in_dim(by_row, (row_index + row_count - 1) % row_count, 0, False)
        below = lax.dynamic_index_in_dim(by_row, (row_index + 1) % row_count, 0, False)
        padded = jnp.concatenate(
            [above[:, None, tile_cols : 2 * tile_cols], values, below[:, None, :tile_cols]], axis=1
        )
        top_seg = by_row[0, :, :tile_cols]
        bottom_seg = by_row[row_count - 1, :, tile_cols : 2 * tile_cols]
        side_line = jnp.moveaxis(by_row[:, :, 2 * tile_cols :], 0, 1).reshape(
            local_faces, side, width
        )
        by_col = gather(
            jnp.concatenate(
                [top_seg, bottom_seg, side_line, padded[:, :, 0], padded[:, :, tile_cols - 1]],
                axis=1,
            ),
            "col",
            False,
        )
        lined_up = 2 * tile_cols + side
        before_col = lax.dynamic_index_in_dim(by_col, (col_index + col_count - 1) % col_count, 0, False)
        after_col = lax.dynamic_index_in_dim(by_col, (col_index + 1) % col_count, 0, False)
        padded = jnp.concatenate(
            [
                before_col[:, lined_up + tile_rows + 2 :, None],
                padded,
                after_col[:, lined_up : lined_up + tile_rows + 2, None],
            ],
            axis=2,
        )
        top_row = jnp.moveaxis(by_col[:, :, :tile_cols], 0, 1).reshape(local_faces, side, width)
        bottom_row = jnp.moveaxis(by_col[:, :, tile_cols : 2 * tile_cols], 0, 1).reshape(
            local_faces, side, width
        )
        left_col = by_col[0, :, 2 * tile_cols : lined_up]
        right_col = by_col[col_count - 1, :, 2 * tile_cols : lined_up]
        cycle = jnp.stack([top_row[:, ::-1], left_col, bottom_row, right_col[:, ::-1]], axis=1)
        all_cycle = gather(cycle, "face", True)
        all_corner = all_cycle[:, :, side - 1]
        side_pick = (
            (links[:, :4, 0][:, :, None, None] == face_range[:, None])
            & (links[:, :4, 1][:, :, None, None] == side_range)
        ).astype(jnp.bfloat16)
        halo_sides = jnp.einsum(
            "ksgt,gtpc->kspc", side_pick, all_cycle, preferred_element_type=jnp.float32
        ).astype(jnp.bfloat16)[:, :, ::-1]
        corner_pick = (
            (links[:, 4:, 0][:, :, None, None] == face_range[:, None])
            & (links[:, 4:, 1][:, :, None, None] == side_range)
            & (links[:, 4:, 3] == 0)[:, :, None, None]
        ).astype(jnp.bfloat16)
        corner_vals = jnp.einsum(
            "kqgt,gtc->kqc", corner_pick, all_corner, preferred_element_type=jnp.float32
        ).astype(jnp.bfloat16)
        full_top = jnp.concatenate(
            [corner_vals[:, 0:1], halo_sides[:, 0, ::-1], corner_vals[:, 3:4]], axis=1
        )
        full_bottom = jnp.concatenate(
            [corner_vals[:, 1:2], halo_sides[:, 2], corner_vals[:, 2:3]], axis=1
        )
        full_left = jnp.concatenate(
            [corner_vals[:, 0:1], halo_sides[:, 1], corner_vals[:, 1:2]], axis=1
        )
        full_right = jnp.concatenate(
            [corner_vals[:, 3:4], halo_sides[:, 3, ::-1], corner_vals[:, 2:3]], axis=1
        )
        top_piece = lax.dynamic_slice_in_dim(full_top, col_index * tile_cols, tile_cols + 2, 1)
        bottom_piece = lax.dynamic_slice_in_dim(
            full_bottom, col_index * tile_cols, tile_cols + 2, 1
        )
        left_piece = lax.dynamic_slice_in_dim(full_left, row_index * tile_rows, tile_rows + 2, 1)
        right_piece = lax.dynamic_slice_in_dim(full_right, row_index * tile_rows, tile_rows + 2, 1)
        padded = padded.at[:, 0].set(jnp.where(row_index == 0, top_piece, padded[:, 0]))
        padded = padded.at[:, tile_rows + 1].set(
            jnp.where(row_index == row_count - 1, bottom_piece, padded[:, tile_rows + 1])
        )
        padded = padded.at[:, :, 0].set(jnp.where(col_index == 0, left_piece, padded[:, :, 0]))
        padded = padded.at[:, :, tile_cols + 1].set(
            jnp.where(col_index == col_count - 1, right_piece, padded[:, :, tile_cols + 1])
        )
        return padded

    values = state.reshape(local_faces, tile_rows, tile_cols, width)
    padded_state = extend(values)

    def window(padded, row_step, col_step):
        return padded[
            :, 1 + row_step : 1 + row_step + tile_rows, 1 + col_step : 1 + col_step + tile_cols
        ].reshape(pixel_rows, width)

    def row_band(padded, row_step):
        return jnp.concatenate(
            [window(padded, row_step, col_step) for col_step in (-1, 0, 1)], axis=1
        )

    state_bands = [row_band(padded_state, row_step) for row_step in (-1, 0, 1)]
    response = jnp.zeros((pixel_rows, width), jnp.float32)
    for position, row_step in enumerate((-1, 0, 1)):
        band_weight = kernel[3 * position : 3 * position + 3].reshape(3 * width, width)
        response = response + jnp.dot(
            state_bands[position], band_weight, preferred_element_type=jnp.float32
        )
    total = float(FACES * side * side)
    sum_first, sum_square = gathered_sum(
        jnp.stack([jnp.sum(response, axis=0), jnp.sum(response * response, axis=0)])
    )
    centre = sum_first / total
    inverse_spread = lax.rsqrt(sum_square / total - centre * centre + 1e-05)
    normed = (response - centre) * inverse_spread
    before = gain * normed + shift
    incoming = upstream.reshape(pixel_rows, width).astype(jnp.float32)
    before_grad = incoming * gelu_slope(before)
    centred = response - centre
    state_sums = []
    centred_sums = []
    slope_sums = []
    for position in range(3):
        state_sums.append(jnp.sum(state_bands[position].astype(jnp.float32), axis=0))
        centred_sums.append(
            lax.dot_general(
                state_bands[position],
                centred,
                (((0,), (0,)), ((), ())),
                precision=lax.Precision.HIGHEST,
                preferred_element_type=jnp.float32,
            )
        )
        slope_sums.append(
            lax.dot_general(
                state_bands[position],
                before_grad,
                (((0,), (0,)), ((), ())),
                precision=lax.Precision.HIGHEST,
                preferred_element_type=jnp.float32,
            )
        )
    taps = 9
    carried = Carried(
        jnp.concatenate(
            [
                jnp.stack(slope_sums).reshape(-1),
                jnp.stack(centred_sums).reshape(-1),
                jnp.stack(state_sums).reshape(-1),
            ]
        )
    )
    shift_grad, gain_grad = channel_pair(
        jnp.sum(before_grad, axis=0), jnp.sum(before_grad * normed, axis=0), carried
    )
    response_grad = (
        gain * inverse_spread * (before_grad - shift_grad / total - normed * gain_grad / total)
    ).astype(jnp.bfloat16)
    grad_tile = response_grad.reshape(local_faces, tile_rows, tile_cols, width)
    padded_grad = extend(grad_tile, carried)
    kernel_sums = carried.finish()
    block = taps * width * width
    slope_total = kernel_sums[:block].reshape(taps, width, width)
    centred_total = kernel_sums[block : 2 * block].reshape(taps, width, width)
    state_total = kernel_sums[2 * block :].reshape(taps, width, 1)
    kernel_grad = (gain * inverse_spread) * (
        slope_total
        - state_total * (shift_grad / total)
        - centred_total * (gain_grad * inverse_spread / total)
    )
    zero_padded = jnp.pad(grad_tile, ((0, 0), (1, 1), (1, 1), (0, 0)))
    state_part = jnp.zeros((pixel_rows, width), jnp.float32)
    for row_step in (-1, 0, 1):
        flipped = jnp.concatenate(
            [kernel[kernel_tap(-row_step, -col_step)].T for col_step in (-1, 0, 1)], axis=0
        )
        state_part = state_part + jnp.dot(
            row_band(zero_padded, row_step), flipped, preferred_element_type=jnp.float32
        )
    state_part = state_part.reshape(local_faces, tile_rows, tile_cols, width)
    side_turns = links[:, :4, 2]
    corner_turns = links[:, 4:, 2]
    full_top_turn = lined(corner_turns[:, 0], side_turns[:, 0], corner_turns[:, 3], side)
    full_bottom_turn = lined(corner_turns[:, 1], side_turns[:, 2], corner_turns[:, 2], side)
    full_left_turn = lined(corner_turns[:, 0], side_turns[:, 1], corner_turns[:, 1], side)
    full_right_turn = lined(corner_turns[:, 3], side_turns[:, 3], corner_turns[:, 2], side)
    top_turn = jnp.where(
        row_index == 0,
        lax.dynamic_slice_in_dim(full_top_turn, col_index * tile_cols, tile_cols + 2, 1),
        0,
    )
    top_turn = top_turn.at[:, 0].set(
        jnp.where(col_index == 0, full_left_turn[:, row_index * tile_rows], top_turn[:, 0])
    )
    top_turn = top_turn.at[:, tile_cols + 1].set(
        jnp.where(
            col_index == col_count - 1,
            full_right_turn[:, row_index * tile_rows],
            top_turn[:, tile_cols + 1],
        )
    )
    bottom_turn = jnp.where(
        row_index == row_count - 1,
        lax.dynamic_slice_in_dim(full_bottom_turn, col_index * tile_cols, tile_cols + 2, 1),
        0,
    )
    bottom_turn = bottom_turn.at[:, 0].set(
        jnp.where(
            col_index == 0,
            full_left_turn[:, row_index * tile_rows + tile_rows + 1],
            bottom_turn[:, 0],
        )
    )
    bottom_turn = bottom_turn.at[:, tile_cols + 1].set(
        jnp.where(
            col_index == col_count - 1,
            full_right_turn[:, row_index * tile_rows + tile_rows + 1],
            bottom_turn[:, tile_cols + 1],
        )
    )
    left_turn = jnp.broadcast_to(
        jnp.where(col_index == 0, side_turns[:, 1], 0)[:, None], (local_faces, tile_rows + 2)
    )
    right_turn = jnp.broadcast_to(
        jnp.where(col_index == col_count - 1, side_turns[:, 3], 0)[:, None],
        (local_faces, tile_rows + 2),
    )

    def strip_terms(strip, turn_codes, steps, length):
        selector = (turn_codes[:, :, None] == side_range).astype(jnp.bfloat16)
        spread = strip[:, :, None, :] * selector[:, :, :, None]
        pieces = jnp.stack(
            [spread[:, 1 + offset : 1 + offset + length] for offset in (-1, 0, 1)], axis=2
        )
        pieces = pieces.reshape(local_faces * length, 12 * width)
        stacked = jnp.concatenate(
            [
                kernel[turned_tap(turn, step_pair[0], step_pair[1])].T
                for step_pair in steps
                for turn in range(4)
            ],
            axis=0,
        )
        summed = jnp.dot(pieces, stacked, preferred_element_type=jnp.float32)
        return summed.reshape(local_faces, length, width)

    left_strip = jnp.pad(padded_grad[:, 1 : tile_rows + 1, 0], ((0, 0), (1, 1), (0, 0)))
    right_strip = jnp.pad(
        padded_grad[:, 1 : tile_rows + 1, tile_cols + 1], ((0, 0), (1, 1), (0, 0))
    )
    top_terms = strip_terms(padded_grad[:, 0], top_turn, ((-1, -1), (-1, 0), (-1, 1)), tile_cols)
    bottom_terms = strip_terms(
        padded_grad[:, tile_rows + 1], bottom_turn, ((1, -1), (1, 0), (1, 1)), tile_cols
    )
    left_terms = strip_terms(left_strip, left_turn, ((-1, -1), (0, -1), (1, -1)), tile_rows)
    right_terms = strip_terms(right_strip, right_turn, ((-1, 1), (0, 1), (1, 1)), tile_rows)
    state_part = state_part.at[:, 0].add(top_terms)
    state_part = state_part.at[:, tile_rows - 1].add(bottom_terms)
    state_part = state_part.at[:, :, 0].add(left_terms)
    state_part = state_part.at[:, :, tile_cols - 1].add(right_terms)
    state_grad = state_part.astype(jnp.bfloat16).reshape(local_faces, tile_rows, tile_cols * width)
    return (state_grad, kernel_grad, gain_grad, shift_grad)


def solution(mesh):
    return jax.shard_map(
        on_device,
        mesh=mesh,
        in_specs=(P("face", "row", "col"), P(), P(), P(), P("face", "row", "col"), P()),
        out_specs=(P("face", "row", "col"), P(), P(), P()),
        check_vma=False,
    )
```

```python
import jax
import jax.numpy as jnp
from jax import lax
from jax.sharding import PartitionSpec as P

FACES = 12


HALF_ROOT = 0.7071067811865476
GAUSS_NORM = 0.3989422804014327


def halo_strips(cells, axis, dim):
    count = lax.axis_size(axis)
    ends = count - 1
    head = lax.slice_in_dim(cells, 0, 1, axis=dim)
    tail = lax.slice_in_dim(cells, cells.shape[dim] - 1, cells.shape[dim], axis=dim)
    from_before = lax.ppermute(tail, axis, [(i, (i + 1) % count) for i in range(ends)])
    from_after = lax.ppermute(head, axis, [((i + 1) % count, i) for i in range(ends)])
    return from_before, from_after


def gelu_slope(values):
    return (
        0.5 * (1.0 + lax.erf(values * HALF_ROOT))
        + values * jnp.exp(-0.5 * values * values) * GAUSS_NORM
    )


def kernel_tap(row_step, col_step):
    return (row_step + 1) * 3 + (col_step + 1)


def turned_tap(turns, row_step, col_step):
    for repeat in range(turns):
        row_step, col_step = (-col_step, row_step)
    return kernel_tap(-row_step, -col_step)


def nested_sum(values, carried=None):
    for axis in ("col", "row", "face"):
        if carried is None:
            values = lax.psum(values, axis)
        else:
            values = carried.beside(
                lambda part, axis=axis: jnp.sum(
                    lax.all_gather(part, axis, axis=0, tiled=False), axis=0
                ),
                values,
            )
    return values


def channel_pair(first_sum, second_sum, carried=None):
    both = nested_sum(jnp.stack([first_sum, second_sum]), carried)
    return both[0], both[1]


def gathered_sum(values):
    for axis in ("col", "row", "face"):
        values = jnp.sum(lax.all_gather(values, axis, axis=0, tiled=False), axis=0)
    return values


def sum_steps():
    faces = lax.axis_size("face")
    steps = [
        (
            "face",
            [
                [(i, (i + 4) % faces) for i in range(faces)],
                [(i, (i + 8) % faces) for i in range(faces)],
            ],
        ),
        ("face", [[(i, i ^ 1) for i in range(faces)]]),
    ]
    count = lax.axis_size("col")
    steps.append(("col", [[(i, i ^ 1) for i in range(count)]]))
    steps.append(("face", [[(i, i ^ 2) for i in range(faces)]]))
    rows = lax.axis_size("row")
    step = rows // 2
    while step >= 1:
        steps.append(("row", [[(i, i ^ step) for i in range(rows)]]))
        step //= 2
    step = count // 2
    while step >= 2:
        steps.append(("col", [[(i, i ^ step) for i in range(count)]]))
        step //= 2
    return steps


def step_send(step, values):
    axis, pair_sets = step
    return [lax.ppermute(values, axis, pairs) for pairs in pair_sets]


def step_land(step, values, moved):
    if len(moved) == 1:
        return values + moved[0]
    from_before, from_after = moved
    group = lax.axis_index("face") // 4
    first = jnp.where(group == 0, values, jnp.where(group == 1, from_before, from_after))
    second = jnp.where(group == 0, from_after, jnp.where(group == 1, values, from_before))
    third = jnp.where(group == 0, from_before, jnp.where(group == 1, from_after, values))
    return (first + second) + third


class Carried:
    def __init__(self, values):
        self.values = values
        self.steps = sum_steps()

    def beside(self, collective, operand):
        if not self.steps:
            return collective(operand)
        step = self.steps.pop(0)
        values, operand = lax.optimization_barrier((self.values, operand))
        moved = step_send(step, values)
        result = collective(operand)
        self.values = step_land(step, values, moved)
        return result

    def doubling(self, part, axis):
        count = lax.axis_size(axis)
        index = lax.axis_index(axis)
        gathered = part[None]
        step_size = 1
        while step_size < count:
            step = self.steps.pop(0) if self.steps else None
            values, gathered = lax.optimization_barrier((self.values, gathered))
            moved = step_send(step, values) if step else None
            arrived = lax.ppermute(
                gathered, axis, [(i, i ^ step_size) for i in range(count)]
            )
            gathered = jnp.where(
                (index // step_size) % 2 == 1,
                jnp.concatenate([arrived, gathered], axis=0),
                jnp.concatenate([gathered, arrived], axis=0),
            )
            self.values = step_land(step, values, moved) if step else values
            step_size *= 2
        return gathered

    def finish(self):
        while self.steps:
            step = self.steps.pop(0)
            self.values = step_land(step, self.values, step_send(step, self.values))
        return self.values


def lined(first_val, middle_val, last_val, length):
    middle_part = jnp.broadcast_to(middle_val[:, None], (middle_val.shape[0], length))
    return jnp.concatenate([first_val[:, None], middle_part, last_val[:, None]], axis=1)


def on_device(state, kernel, gain, shift, upstream, face_links):
    local_faces = state.shape[0]
    tile_rows = state.shape[1]
    width = kernel.shape[1]
    tile_cols = state.shape[2] // width
    row_count = lax.axis_size("row")
    col_count = lax.axis_size("col")
    side = tile_rows * row_count
    row_index = lax.axis_index("row")
    col_index = lax.axis_index("col")
    face_ids = lax.axis_index("face") * local_faces + jnp.arange(local_faces, dtype=jnp.int32)
    links = face_links[face_ids]
    face_range = jnp.arange(FACES, dtype=jnp.int32)
    side_range = jnp.arange(4, dtype=jnp.int32)
    pixel_rows = local_faces * tile_rows * tile_cols

    def extend(values, carried=None):
        def gather(part, axis, tiled):
            if carried is None or axis == "face":
                return lax.all_gather(part, axis, axis=0, tiled=tiled)
            return carried.doubling(part, axis)

        col_strip = jnp.where(col_index == 0, values[:, :, 0], values[:, :, tile_cols - 1])
        by_row = gather(
            jnp.concatenate([values[:, 0], values[:, tile_rows - 1], col_strip], axis=1), "row", False
        )
        above = lax.dynamic_index_in_dim(by_row, (row_index + row_count - 1) % row_count, 0, False)
        below = lax.dynamic_index_in_dim(by_row, (row_index + 1) % row_count, 0, False)
        padded = jnp.concatenate(
            [above[:, None, tile_cols : 2 * tile_cols], values, below[:, None, :tile_cols]], axis=1
        )
        top_seg = by_row[0, :, :tile_cols]
        bottom_seg = by_row[row_count - 1, :, tile_cols : 2 * tile_cols]
        side_line = jnp.moveaxis(by_row[:, :, 2 * tile_cols :], 0, 1).reshape(
            local_faces, side, width
        )
        by_col = gather(
            jnp.concatenate(
                [top_seg, bottom_seg, side_line, padded[:, :, 0], padded[:, :, tile_cols - 1]],
                axis=1,
            ),
            "col",
            False,
        )
        lined_up = 2 * tile_cols + side
        before_col = lax.dynamic_index_in_dim(by_col, (col_index + col_count - 1) % col_count, 0, False)
        after_col = lax.dynamic_index_in_dim(by_col, (col_index + 1) % col_count, 0, False)
        padded = jnp.concatenate(
            [
                before_col[:, lined_up + tile_rows + 2 :, None],
                padded,
                after_col[:, lined_up : lined_up + tile_rows + 2, None],
            ],
            axis=2,
        )
        top_row = jnp.moveaxis(by_col[:, :, :tile_cols], 0, 1).reshape(local_faces, side, width)
        bottom_row = jnp.moveaxis(by_col[:, :, tile_cols : 2 * tile_cols], 0, 1).reshape(
            local_faces, side, width
        )
        left_col = by_col[0, :, 2 * tile_cols : lined_up]
        right_col = by_col[col_count - 1, :, 2 * tile_cols : lined_up]
        cycle = jnp.stack([top_row[:, ::-1], left_col, bottom_row, right_col[:, ::-1]], axis=1)
        all_cycle = gather(cycle, "face", True)
        all_corner = all_cycle[:, :, side - 1]
        side_pick = (
            (links[:, :4, 0][:, :, None, None] == face_range[:, None])
            & (links[:, :4, 1][:, :, None, None] == side_range)
        ).astype(jnp.bfloat16)
        halo_sides = jnp.einsum(
            "ksgt,gtpc->kspc", side_pick, all_cycle, preferred_element_type=jnp.float32
        ).astype(jnp.bfloat16)[:, :, ::-1]
        corner_pick = (
            (links[:, 4:, 0][:, :, None, None] == face_range[:, None])
            & (links[:, 4:, 1][:, :, None, None] == side_range)
            & (links[:, 4:, 3] == 0)[:, :, None, None]
        ).astype(jnp.bfloat16)
        corner_vals = jnp.einsum(
            "kqgt,gtc->kqc", corner_pick, all_corner, preferred_element_type=jnp.float32
        ).astype(jnp.bfloat16)
        full_top = jnp.concatenate(
            [corner_vals[:, 0:1], halo_sides[:, 0, ::-1], corner_vals[:, 3:4]], axis=1
        )
        full_bottom = jnp.concatenate(
            [corner_vals[:, 1:2], halo_sides[:, 2], corner_vals[:, 2:3]], axis=1
        )
        full_left = jnp.concatenate(
            [corner_vals[:, 0:1], halo_sides[:, 1], corner_vals[:, 1:2]], axis=1
        )
        full_right = jnp.concatenate(
            [corner_vals[:, 3:4], halo_sides[:, 3, ::-1], corner_vals[:, 2:3]], axis=1
        )
        top_piece = lax.dynamic_slice_in_dim(full_top, col_index * tile_cols, tile_cols + 2, 1)
        bottom_piece = lax.dynamic_slice_in_dim(
            full_bottom, col_index * tile_cols, tile_cols + 2, 1
        )
        left_piece = lax.dynamic_slice_in_dim(full_left, row_index * tile_rows, tile_rows + 2, 1)
        right_piece = lax.dynamic_slice_in_dim(full_right, row_index * tile_rows, tile_rows + 2, 1)
        padded = padded.at[:, 0].set(jnp.where(row_index == 0, top_piece, padded[:, 0]))
        padded = padded.at[:, tile_rows + 1].set(
            jnp.where(row_index == row_count - 1, bottom_piece, padded[:, tile_rows + 1])
        )
        padded = padded.at[:, :, 0].set(jnp.where(col_index == 0, left_piece, padded[:, :, 0]))
        padded = padded.at[:, :, tile_cols + 1].set(
            jnp.where(col_index == col_count - 1, right_piece, padded[:, :, tile_cols + 1])
        )
        return padded

    values = state.reshape(local_faces, tile_rows, tile_cols, width)
    padded_state = extend(values)

    def window(padded, row_step, col_step):
        return padded[
            :, 1 + row_step : 1 + row_step + tile_rows, 1 + col_step : 1 + col_step + tile_cols
        ].reshape(pixel_rows, width)

    def row_band(padded, row_step):
        return jnp.concatenate(
            [window(padded, row_step, col_step) for col_step in (-1, 0, 1)], axis=1
        )

    state_bands = [row_band(padded_state, row_step) for row_step in (-1, 0, 1)]
    response = jnp.zeros((pixel_rows, width), jnp.float32)
    for position, row_step in enumerate((-1, 0, 1)):
        band_weight = kernel[3 * position : 3 * position + 3].reshape(3 * width, width)
        response = response + jnp.dot(
            state_bands[position], band_weight, preferred_element_type=jnp.float32
        )
    total = float(FACES * side * side)
    sum_first, sum_square = gathered_sum(
        jnp.stack([jnp.sum(response, axis=0), jnp.sum(response * response, axis=0)])
    )
    centre = sum_first / total
    inverse_spread = lax.rsqrt(sum_square / total - centre * centre + 1e-05)
    normed = (response - centre) * inverse_spread
    before = gain * normed + shift
    incoming = upstream.reshape(pixel_rows, width).astype(jnp.float32)
    before_grad = incoming * gelu_slope(before)
    centred = response - centre
    state_sums = []
    centred_sums = []
    slope_sums = []
    for position in range(3):
        state_sums.append(jnp.sum(state_bands[position].astype(jnp.float32), axis=0))
        centred_sums.append(
            lax.dot_general(
                state_bands[position],
                centred,
                (((0,), (0,)), ((), ())),
                precision=lax.Precision.HIGHEST,
                preferred_element_type=jnp.float32,
            )
        )
        slope_sums.append(
            lax.dot_general(
                state_bands[position],
                before_grad,
                (((0,), (0,)), ((), ())),
                precision=lax.Precision.HIGHEST,
                preferred_element_type=jnp.float32,
            )
        )
    taps = 9
    carried = Carried(
        jnp.concatenate(
            [
                jnp.stack(slope_sums).reshape(-1),
                jnp.stack(centred_sums).reshape(-1),
                jnp.stack(state_sums).reshape(-1),
            ]
        )
    )
    shift_grad, gain_grad = channel_pair(
        jnp.sum(before_grad, axis=0), jnp.sum(before_grad * normed, axis=0), carried
    )
    response_grad = (
        gain * inverse_spread * (before_grad - shift_grad / total - normed * gain_grad / total)
    ).astype(jnp.bfloat16)
    grad_tile = response_grad.reshape(local_faces, tile_rows, tile_cols, width)
    padded_grad = extend(grad_tile, carried)
    kernel_sums = carried.finish()
    block = taps * width * width
    slope_total = kernel_sums[:block].reshape(taps, width, width)
    centred_total = kernel_sums[block : 2 * block].reshape(taps, width, width)
    state_total = kernel_sums[2 * block :].reshape(taps, width, 1)
    kernel_grad = (gain * inverse_spread) * (
        slope_total
        - state_total * (shift_grad / total)
        - centred_total * (gain_grad * inverse_spread / total)
    )
    zero_padded = jnp.pad(grad_tile, ((0, 0), (1, 1), (1, 1), (0, 0)))
    state_part = jnp.zeros((pixel_rows, width), jnp.float32)
    for row_step in (-1, 0, 1):
        flipped = jnp.concatenate(
            [kernel[kernel_tap(-row_step, -col_step)].T for col_step in (-1, 0, 1)], axis=0
        )
        state_part = state_part + jnp.dot(
            row_band(zero_padded, row_step), flipped, preferred_element_type=jnp.float32
        )
    state_part = state_part.reshape(local_faces, tile_rows, tile_cols, width)
    side_turns = links[:, :4, 2]
    corner_turns = links[:, 4:, 2]
    full_top_turn = lined(corner_turns[:, 0], side_turns[:, 0], corner_turns[:, 3], side)
    full_bottom_turn = lined(corner_turns[:, 1], side_turns[:, 2], corner_turns[:, 2], side)
    full_left_turn = lined(corner_turns[:, 0], side_turns[:, 1], corner_turns[:, 1], side)
    full_right_turn = lined(corner_turns[:, 3], side_turns[:, 3], corner_turns[:, 2], side)
    top_turn = jnp.where(
        row_index == 0,
        lax.dynamic_slice_in_dim(full_top_turn, col_index * tile_cols, tile_cols + 2, 1),
        0,
    )
    top_turn = top_turn.at[:, 0].set(
        jnp.where(col_index == 0, full_left_turn[:, row_index * tile_rows], top_turn[:, 0])
    )
    top_turn = top_turn.at[:, tile_cols + 1].set(
        jnp.where(
            col_index == col_count - 1,
            full_right_turn[:, row_index * tile_rows],
            top_turn[:, tile_cols + 1],
        )
    )
    bottom_turn = jnp.where(
        row_index == row_count - 1,
        lax.dynamic_slice_in_dim(full_bottom_turn, col_index * tile_cols, tile_cols + 2, 1),
        0,
    )
    bottom_turn = bottom_turn.at[:, 0].set(
        jnp.where(
            col_index == 0,
            full_left_turn[:, row_index * tile_rows + tile_rows + 1],
            bottom_turn[:, 0],
        )
    )
    bottom_turn = bottom_turn.at[:, tile_cols + 1].set(
        jnp.where(
            col_index == col_count - 1,
            full_right_turn[:, row_index * tile_rows + tile_rows + 1],
            bottom_turn[:, tile_cols + 1],
        )
    )
    left_turn = jnp.broadcast_to(
        jnp.where(col_index == 0, side_turns[:, 1], 0)[:, None], (local_faces, tile_rows + 2)
    )
    right_turn = jnp.broadcast_to(
        jnp.where(col_index == col_count - 1, side_turns[:, 3], 0)[:, None],
        (local_faces, tile_rows + 2),
    )

    def strip_terms(strip, turn_codes, steps, length):
        selector = (turn_codes[:, :, None] == side_range).astype(jnp.bfloat16)
        spread = strip[:, :, None, :] * selector[:, :, :, None]
        pieces = jnp.stack(
            [spread[:, 1 + offset : 1 + offset + length] for offset in (-1, 0, 1)], axis=2
        )
        pieces = pieces.reshape(local_faces * length, 12 * width)
        stacked = jnp.concatenate(
            [
                kernel[turned_tap(turn, step_pair[0], step_pair[1])].T
                for step_pair in steps
                for turn in range(4)
            ],
            axis=0,
        )
        summed = jnp.dot(pieces, stacked, preferred_element_type=jnp.float32)
        return summed.reshape(local_faces, length, width)

    left_strip = jnp.pad(padded_grad[:, 1 : tile_rows + 1, 0], ((0, 0), (1, 1), (0, 0)))
    right_strip = jnp.pad(
        padded_grad[:, 1 : tile_rows + 1, tile_cols + 1], ((0, 0), (1, 1), (0, 0))
    )
    top_terms = strip_terms(padded_grad[:, 0], top_turn, ((-1, -1), (-1, 0), (-1, 1)), tile_cols)
    bottom_terms = strip_terms(
        padded_grad[:, tile_rows + 1], bottom_turn, ((1, -1), (1, 0), (1, 1)), tile_cols
    )
    left_terms = strip_terms(left_strip, left_turn, ((-1, -1), (0, -1), (1, -1)), tile_rows)
    right_terms = strip_terms(right_strip, right_turn, ((-1, 1), (0, 1), (1, 1)), tile_rows)
    state_part = state_part.at[:, 0].add(top_terms)
    state_part = state_part.at[:, tile_rows - 1].add(bottom_terms)
    state_part = state_part.at[:, :, 0].add(left_terms)
    state_part = state_part.at[:, :, tile_cols - 1].add(right_terms)
    state_grad = state_part.astype(jnp.bfloat16).reshape(local_faces, tile_rows, tile_cols * width)
    return (state_grad, kernel_grad, gain_grad, shift_grad)


def solution(mesh):
    return jax.shard_map(
        on_device,
        mesh=mesh,
        in_specs=(P("face", "row", "col"), P(), P(), P(), P("face", "row", "col"), P()),
        out_specs=(P("face", "row", "col"), P(), P(), P()),
        check_vma=False,
    )
```

```python
import jax
import jax.numpy as jnp
from jax import lax
from jax.sharding import PartitionSpec as P

FACES = 12


HALF_ROOT = 0.7071067811865476
GAUSS_NORM = 0.3989422804014327


def halo_strips(cells, axis, dim):
    count = lax.axis_size(axis)
    ends = count - 1
    head = lax.slice_in_dim(cells, 0, 1, axis=dim)
    tail = lax.slice_in_dim(cells, cells.shape[dim] - 1, cells.shape[dim], axis=dim)
    from_before = lax.ppermute(tail, axis, [(i, (i + 1) % count) for i in range(ends)])
    from_after = lax.ppermute(head, axis, [((i + 1) % count, i) for i in range(ends)])
    return from_before, from_after


def doubling_gather(part, axis):
    count = lax.axis_size(axis)
    index = lax.axis_index(axis)
    gathered = part[None]
    step_size = 1
    while step_size < count:
        arrived = lax.ppermute(gathered, axis, [(i, i ^ step_size) for i in range(count)])
        gathered = jnp.where(
            (index // step_size) % 2 == 1,
            jnp.concatenate([arrived, gathered], axis=0),
            jnp.concatenate([gathered, arrived], axis=0),
        )
        step_size *= 2
    return gathered


def gelu_slope(values):
    return (
        0.5 * (1.0 + lax.erf(values * HALF_ROOT))
        + values * jnp.exp(-0.5 * values * values) * GAUSS_NORM
    )


def kernel_tap(row_step, col_step):
    return (row_step + 1) * 3 + (col_step + 1)


def turned_tap(turns, row_step, col_step):
    for repeat in range(turns):
        row_step, col_step = (-col_step, row_step)
    return kernel_tap(-row_step, -col_step)


def nested_sum(values, carried=None):
    for axis in ("col", "row", "face"):
        if carried is None:
            values = lax.psum(values, axis)
        else:
            values = carried.beside(
                lambda part, axis=axis: jnp.sum(
                    lax.all_gather(part, axis, axis=0, tiled=False), axis=0
                ),
                values,
            )
    return values


def channel_pair(first_sum, second_sum, carried=None):
    both = nested_sum(jnp.stack([first_sum, second_sum]), carried)
    return both[0], both[1]


def gathered_sum(values):
    for axis in ("col", "row", "face"):
        values = jnp.sum(lax.all_gather(values, axis, axis=0, tiled=False), axis=0)
    return values


def sum_steps():
    faces = lax.axis_size("face")
    steps = [
        (
            "face",
            [
                [(i, (i + 4) % faces) for i in range(faces)],
                [(i, (i + 8) % faces) for i in range(faces)],
            ],
        ),
        ("face", [[(i, i ^ 1) for i in range(faces)]]),
        ("face", [[(i, i ^ 2) for i in range(faces)]]),
    ]
    for axis in ("row", "col"):
        count = lax.axis_size(axis)
        step = count // 2
        while step >= 1:
            steps.append((axis, [[(i, i ^ step) for i in range(count)]]))
            step //= 2
    return steps


def step_send(step, values):
    axis, pair_sets = step
    return [lax.ppermute(values, axis, pairs) for pairs in pair_sets]


def step_land(step, values, moved):
    if len(moved) == 1:
        return values + moved[0]
    from_before, from_after = moved
    group = lax.axis_index("face") // 4
    first = jnp.where(group == 0, values, jnp.where(group == 1, from_before, from_after))
    second = jnp.where(group == 0, from_after, jnp.where(group == 1, values, from_before))
    third = jnp.where(group == 0, from_before, jnp.where(group == 1, from_after, values))
    return (first + second) + third


class Carried:
    def __init__(self, values):
        self.values = values
        self.steps = sum_steps()

    def beside(self, collective, operand):
        if not self.steps:
            return collective(operand)
        step = self.steps.pop(0)
        values, operand = lax.optimization_barrier((self.values, operand))
        moved = step_send(step, values)
        result = collective(operand)
        self.values = step_land(step, values, moved)
        return result

    def doubling(self, part, axis):
        count = lax.axis_size(axis)
        index = lax.axis_index(axis)
        gathered = part[None]
        step_size = 1
        while step_size < count:
            step = self.steps.pop(0) if self.steps else None
            values, gathered = lax.optimization_barrier((self.values, gathered))
            moved = step_send(step, values) if step else None
            arrived = lax.ppermute(
                gathered, axis, [(i, i ^ step_size) for i in range(count)]
            )
            gathered = jnp.where(
                (index // step_size) % 2 == 1,
                jnp.concatenate([arrived, gathered], axis=0),
                jnp.concatenate([gathered, arrived], axis=0),
            )
            self.values = step_land(step, values, moved) if step else values
            step_size *= 2
        return gathered

    def finish(self):
        while self.steps:
            step = self.steps.pop(0)
            self.values = step_land(step, self.values, step_send(step, self.values))
        return self.values


def lined(first_val, middle_val, last_val, length):
    middle_part = jnp.broadcast_to(middle_val[:, None], (middle_val.shape[0], length))
    return jnp.concatenate([first_val[:, None], middle_part, last_val[:, None]], axis=1)


def on_device(state, kernel, gain, shift, upstream, face_links):
    local_faces = state.shape[0]
    tile_rows = state.shape[1]
    width = kernel.shape[1]
    tile_cols = state.shape[2] // width
    row_count = lax.axis_size("row")
    col_count = lax.axis_size("col")
    side = tile_rows * row_count
    row_index = lax.axis_index("row")
    col_index = lax.axis_index("col")
    face_ids = lax.axis_index("face") * local_faces + jnp.arange(local_faces, dtype=jnp.int32)
    links = face_links[face_ids]
    face_range = jnp.arange(FACES, dtype=jnp.int32)
    side_range = jnp.arange(4, dtype=jnp.int32)
    pixel_rows = local_faces * tile_rows * tile_cols

    def extend(values, carried=None):
        def gather(part, axis, tiled):
            if axis == "face":
                return lax.all_gather(part, axis, axis=0, tiled=tiled)
            if carried is None:
                return doubling_gather(part, axis)
            return carried.doubling(part, axis)

        col_strip = jnp.where(col_index == 0, values[:, :, 0], values[:, :, tile_cols - 1])
        by_row = gather(
            jnp.concatenate([values[:, 0], values[:, tile_rows - 1], col_strip], axis=1), "row", False
        )
        above = lax.dynamic_index_in_dim(by_row, (row_index + row_count - 1) % row_count, 0, False)
        below = lax.dynamic_index_in_dim(by_row, (row_index + 1) % row_count, 0, False)
        padded = jnp.concatenate(
            [above[:, None, tile_cols : 2 * tile_cols], values, below[:, None, :tile_cols]], axis=1
        )
        top_seg = by_row[0, :, :tile_cols]
        bottom_seg = by_row[row_count - 1, :, tile_cols : 2 * tile_cols]
        side_line = jnp.moveaxis(by_row[:, :, 2 * tile_cols :], 0, 1).reshape(
            local_faces, side, width
        )
        by_col = gather(
            jnp.concatenate(
                [top_seg, bottom_seg, side_line, padded[:, :, 0], padded[:, :, tile_cols - 1]],
                axis=1,
            ),
            "col",
            False,
        )
        lined_up = 2 * tile_cols + side
        before_col = lax.dynamic_index_in_dim(by_col, (col_index + col_count - 1) % col_count, 0, False)
        after_col = lax.dynamic_index_in_dim(by_col, (col_index + 1) % col_count, 0, False)
        padded = jnp.concatenate(
            [
                before_col[:, lined_up + tile_rows + 2 :, None],
                padded,
                after_col[:, lined_up : lined_up + tile_rows + 2, None],
            ],
            axis=2,
        )
        top_row = jnp.moveaxis(by_col[:, :, :tile_cols], 0, 1).reshape(local_faces, side, width)
        bottom_row = jnp.moveaxis(by_col[:, :, tile_cols : 2 * tile_cols], 0, 1).reshape(
            local_faces, side, width
        )
        left_col = by_col[0, :, 2 * tile_cols : lined_up]
        right_col = by_col[col_count - 1, :, 2 * tile_cols : lined_up]
        cycle = jnp.stack([top_row[:, ::-1], left_col, bottom_row, right_col[:, ::-1]], axis=1)
        all_cycle = gather(cycle, "face", True)
        all_corner = all_cycle[:, :, side - 1]
        side_pick = (
            (links[:, :4, 0][:, :, None, None] == face_range[:, None])
            & (links[:, :4, 1][:, :, None, None] == side_range)
        ).astype(jnp.bfloat16)
        halo_sides = jnp.einsum(
            "ksgt,gtpc->kspc", side_pick, all_cycle, preferred_element_type=jnp.float32
        ).astype(jnp.bfloat16)[:, :, ::-1]
        corner_pick = (
            (links[:, 4:, 0][:, :, None, None] == face_range[:, None])
            & (links[:, 4:, 1][:, :, None, None] == side_range)
            & (links[:, 4:, 3] == 0)[:, :, None, None]
        ).astype(jnp.bfloat16)
        corner_vals = jnp.einsum(
            "kqgt,gtc->kqc", corner_pick, all_corner, preferred_element_type=jnp.float32
        ).astype(jnp.bfloat16)
        full_top = jnp.concatenate(
            [corner_vals[:, 0:1], halo_sides[:, 0, ::-1], corner_vals[:, 3:4]], axis=1
        )
        full_bottom = jnp.concatenate(
            [corner_vals[:, 1:2], halo_sides[:, 2], corner_vals[:, 2:3]], axis=1
        )
        full_left = jnp.concatenate(
            [corner_vals[:, 0:1], halo_sides[:, 1], corner_vals[:, 1:2]], axis=1
        )
        full_right = jnp.concatenate(
            [corner_vals[:, 3:4], halo_sides[:, 3, ::-1], corner_vals[:, 2:3]], axis=1
        )
        top_piece = lax.dynamic_slice_in_dim(full_top, col_index * tile_cols, tile_cols + 2, 1)
        bottom_piece = lax.dynamic_slice_in_dim(
            full_bottom, col_index * tile_cols, tile_cols + 2, 1
        )
        left_piece = lax.dynamic_slice_in_dim(full_left, row_index * tile_rows, tile_rows + 2, 1)
        right_piece = lax.dynamic_slice_in_dim(full_right, row_index * tile_rows, tile_rows + 2, 1)
        padded = padded.at[:, 0].set(jnp.where(row_index == 0, top_piece, padded[:, 0]))
        padded = padded.at[:, tile_rows + 1].set(
            jnp.where(row_index == row_count - 1, bottom_piece, padded[:, tile_rows + 1])
        )
        padded = padded.at[:, :, 0].set(jnp.where(col_index == 0, left_piece, padded[:, :, 0]))
        padded = padded.at[:, :, tile_cols + 1].set(
            jnp.where(col_index == col_count - 1, right_piece, padded[:, :, tile_cols + 1])
        )
        return padded

    values = state.reshape(local_faces, tile_rows, tile_cols, width)
    padded_state = extend(values)

    def window(padded, row_step, col_step):
        return padded[
            :, 1 + row_step : 1 + row_step + tile_rows, 1 + col_step : 1 + col_step + tile_cols
        ].reshape(pixel_rows, width)

    def row_band(padded, row_step):
        return jnp.concatenate(
            [window(padded, row_step, col_step) for col_step in (-1, 0, 1)], axis=1
        )

    state_bands = [row_band(padded_state, row_step) for row_step in (-1, 0, 1)]
    response = jnp.zeros((pixel_rows, width), jnp.float32)
    for position, row_step in enumerate((-1, 0, 1)):
        band_weight = kernel[3 * position : 3 * position + 3].reshape(3 * width, width)
        response = response + jnp.dot(
            state_bands[position], band_weight, preferred_element_type=jnp.float32
        )
    total = float(FACES * side * side)
    sum_first, sum_square = gathered_sum(
        jnp.stack([jnp.sum(response, axis=0), jnp.sum(response * response, axis=0)])
    )
    centre = sum_first / total
    inverse_spread = lax.rsqrt(sum_square / total - centre * centre + 1e-05)
    normed = (response - centre) * inverse_spread
    before = gain * normed + shift
    incoming = upstream.reshape(pixel_rows, width).astype(jnp.float32)
    before_grad = incoming * gelu_slope(before)
    centred = response - centre
    state_sums = []
    centred_sums = []
    slope_sums = []
    for position in range(3):
        state_sums.append(jnp.sum(state_bands[position].astype(jnp.float32), axis=0))
        centred_sums.append(
            lax.dot_general(
                state_bands[position],
                centred,
                (((0,), (0,)), ((), ())),
                precision=lax.Precision.HIGHEST,
                preferred_element_type=jnp.float32,
            )
        )
        slope_sums.append(
            lax.dot_general(
                state_bands[position],
                before_grad,
                (((0,), (0,)), ((), ())),
                precision=lax.Precision.HIGHEST,
                preferred_element_type=jnp.float32,
            )
        )
    taps = 9
    carried = Carried(
        jnp.concatenate(
            [
                jnp.stack(slope_sums).reshape(-1),
                jnp.stack(centred_sums).reshape(-1),
                jnp.stack(state_sums).reshape(-1),
            ]
        )
    )
    shift_grad, gain_grad = channel_pair(
        jnp.sum(before_grad, axis=0), jnp.sum(before_grad * normed, axis=0), carried
    )
    response_grad = (
        gain * inverse_spread * (before_grad - shift_grad / total - normed * gain_grad / total)
    ).astype(jnp.bfloat16)
    grad_tile = response_grad.reshape(local_faces, tile_rows, tile_cols, width)
    padded_grad = extend(grad_tile, carried)
    kernel_sums = carried.finish()
    block = taps * width * width
    slope_total = kernel_sums[:block].reshape(taps, width, width)
    centred_total = kernel_sums[block : 2 * block].reshape(taps, width, width)
    state_total = kernel_sums[2 * block :].reshape(taps, width, 1)
    kernel_grad = (gain * inverse_spread) * (
        slope_total
        - state_total * (shift_grad / total)
        - centred_total * (gain_grad * inverse_spread / total)
    )
    zero_padded = jnp.pad(grad_tile, ((0, 0), (1, 1), (1, 1), (0, 0)))
    state_part = jnp.zeros((pixel_rows, width), jnp.float32)
    for row_step in (-1, 0, 1):
        flipped = jnp.concatenate(
            [kernel[kernel_tap(-row_step, -col_step)].T for col_step in (-1, 0, 1)], axis=0
        )
        state_part = state_part + jnp.dot(
            row_band(zero_padded, row_step), flipped, preferred_element_type=jnp.float32
        )
    state_part = state_part.reshape(local_faces, tile_rows, tile_cols, width)
    side_turns = links[:, :4, 2]
    corner_turns = links[:, 4:, 2]
    full_top_turn = lined(corner_turns[:, 0], side_turns[:, 0], corner_turns[:, 3], side)
    full_bottom_turn = lined(corner_turns[:, 1], side_turns[:, 2], corner_turns[:, 2], side)
    full_left_turn = lined(corner_turns[:, 0], side_turns[:, 1], corner_turns[:, 1], side)
    full_right_turn = lined(corner_turns[:, 3], side_turns[:, 3], corner_turns[:, 2], side)
    top_turn = jnp.where(
        row_index == 0,
        lax.dynamic_slice_in_dim(full_top_turn, col_index * tile_cols, tile_cols + 2, 1),
        0,
    )
    top_turn = top_turn.at[:, 0].set(
        jnp.where(col_index == 0, full_left_turn[:, row_index * tile_rows], top_turn[:, 0])
    )
    top_turn = top_turn.at[:, tile_cols + 1].set(
        jnp.where(
            col_index == col_count - 1,
            full_right_turn[:, row_index * tile_rows],
            top_turn[:, tile_cols + 1],
        )
    )
    bottom_turn = jnp.where(
        row_index == row_count - 1,
        lax.dynamic_slice_in_dim(full_bottom_turn, col_index * tile_cols, tile_cols + 2, 1),
        0,
    )
    bottom_turn = bottom_turn.at[:, 0].set(
        jnp.where(
            col_index == 0,
            full_left_turn[:, row_index * tile_rows + tile_rows + 1],
            bottom_turn[:, 0],
        )
    )
    bottom_turn = bottom_turn.at[:, tile_cols + 1].set(
        jnp.where(
            col_index == col_count - 1,
            full_right_turn[:, row_index * tile_rows + tile_rows + 1],
            bottom_turn[:, tile_cols + 1],
        )
    )
    left_turn = jnp.broadcast_to(
        jnp.where(col_index == 0, side_turns[:, 1], 0)[:, None], (local_faces, tile_rows + 2)
    )
    right_turn = jnp.broadcast_to(
        jnp.where(col_index == col_count - 1, side_turns[:, 3], 0)[:, None],
        (local_faces, tile_rows + 2),
    )

    def strip_terms(strip, turn_codes, steps, length):
        selector = (turn_codes[:, :, None] == side_range).astype(jnp.bfloat16)
        spread = strip[:, :, None, :] * selector[:, :, :, None]
        pieces = jnp.stack(
            [spread[:, 1 + offset : 1 + offset + length] for offset in (-1, 0, 1)], axis=2
        )
        pieces = pieces.reshape(local_faces * length, 12 * width)
        stacked = jnp.concatenate(
            [
                kernel[turned_tap(turn, step_pair[0], step_pair[1])].T
                for step_pair in steps
                for turn in range(4)
            ],
            axis=0,
        )
        summed = jnp.dot(pieces, stacked, preferred_element_type=jnp.float32)
        return summed.reshape(local_faces, length, width)

    left_strip = jnp.pad(padded_grad[:, 1 : tile_rows + 1, 0], ((0, 0), (1, 1), (0, 0)))
    right_strip = jnp.pad(
        padded_grad[:, 1 : tile_rows + 1, tile_cols + 1], ((0, 0), (1, 1), (0, 0))
    )
    top_terms = strip_terms(padded_grad[:, 0], top_turn, ((-1, -1), (-1, 0), (-1, 1)), tile_cols)
    bottom_terms = strip_terms(
        padded_grad[:, tile_rows + 1], bottom_turn, ((1, -1), (1, 0), (1, 1)), tile_cols
    )
    left_terms = strip_terms(left_strip, left_turn, ((-1, -1), (0, -1), (1, -1)), tile_rows)
    right_terms = strip_terms(right_strip, right_turn, ((-1, 1), (0, 1), (1, 1)), tile_rows)
    state_part = state_part.at[:, 0].add(top_terms)
    state_part = state_part.at[:, tile_rows - 1].add(bottom_terms)
    state_part = state_part.at[:, :, 0].add(left_terms)
    state_part = state_part.at[:, :, tile_cols - 1].add(right_terms)
    state_grad = state_part.astype(jnp.bfloat16).reshape(local_faces, tile_rows, tile_cols * width)
    return (state_grad, kernel_grad, gain_grad, shift_grad)


def solution(mesh):
    return jax.shard_map(
        on_device,
        mesh=mesh,
        in_specs=(P("face", "row", "col"), P(), P(), P(), P("face", "row", "col"), P()),
        out_specs=(P("face", "row", "col"), P(), P(), P()),
        check_vma=False,
    )
```

```python
import jax
import jax.numpy as jnp
from jax import lax
from jax.sharding import PartitionSpec as P

FACES = 12


HALF_ROOT = 0.7071067811865476
GAUSS_NORM = 0.3989422804014327


def halo_strips(cells, axis, dim):
    count = lax.axis_size(axis)
    ends = count - 1
    head = lax.slice_in_dim(cells, 0, 1, axis=dim)
    tail = lax.slice_in_dim(cells, cells.shape[dim] - 1, cells.shape[dim], axis=dim)
    from_before = lax.ppermute(tail, axis, [(i, (i + 1) % count) for i in range(ends)])
    from_after = lax.ppermute(head, axis, [((i + 1) % count, i) for i in range(ends)])
    return from_before, from_after


def gelu_slope(values):
    return (
        0.5 * (1.0 + lax.erf(values * HALF_ROOT))
        + values * jnp.exp(-0.5 * values * values) * GAUSS_NORM
    )


def kernel_tap(row_step, col_step):
    return (row_step + 1) * 3 + (col_step + 1)


def turned_tap(turns, row_step, col_step):
    for repeat in range(turns):
        row_step, col_step = (-col_step, row_step)
    return kernel_tap(-row_step, -col_step)


def nested_sum(values, carried=None):
    for axis in ("col", "row", "face"):
        if carried is None:
            values = lax.psum(values, axis)
        else:
            values = carried.beside(
                lambda part, axis=axis: jnp.sum(
                    lax.all_gather(part, axis, axis=0, tiled=False), axis=0
                ),
                values,
            )
    return values


def channel_pair(first_sum, second_sum, carried=None):
    both = nested_sum(jnp.stack([first_sum, second_sum]), carried)
    return both[0], both[1]


def gathered_sum(values):
    for axis in ("col", "row", "face"):
        values = jnp.sum(lax.all_gather(values, axis, axis=0, tiled=False), axis=0)
    return values


def sum_steps():
    faces = lax.axis_size("face")
    rows = lax.axis_size("row")
    steps = [
        (
            "face",
            [
                [(i, (i + 4) % faces) for i in range(faces)],
                [(i, (i + 8) % faces) for i in range(faces)],
            ],
        ),
        ("row", [[(i, i ^ (rows // 2)) for i in range(rows)]]),
        ("face", [[(i, i ^ 2) for i in range(faces)]]),
        ("face", [[(i, i ^ 1) for i in range(faces)]]),
    ]
    step = rows // 4
    while step >= 1:
        steps.append(("row", [[(i, i ^ step) for i in range(rows)]]))
        step //= 2
    count = lax.axis_size("col")
    step = count // 2
    while step >= 1:
        steps.append(("col", [[(i, i ^ step) for i in range(count)]]))
        step //= 2
    return steps


def step_send(step, values):
    axis, pair_sets = step
    return [lax.ppermute(values, axis, pairs) for pairs in pair_sets]


def step_land(step, values, moved):
    if len(moved) == 1:
        return values + moved[0]
    from_before, from_after = moved
    group = lax.axis_index("face") // 4
    first = jnp.where(group == 0, values, jnp.where(group == 1, from_before, from_after))
    second = jnp.where(group == 0, from_after, jnp.where(group == 1, values, from_before))
    third = jnp.where(group == 0, from_before, jnp.where(group == 1, from_after, values))
    return (first + second) + third


class Carried:
    def __init__(self, values):
        self.values = values
        self.steps = sum_steps()

    def beside(self, collective, operand):
        if not self.steps:
            return collective(operand)
        step = self.steps.pop(0)
        values, operand = lax.optimization_barrier((self.values, operand))
        moved = step_send(step, values)
        result = collective(operand)
        self.values = step_land(step, values, moved)
        return result

    def doubling(self, part, axis):
        count = lax.axis_size(axis)
        index = lax.axis_index(axis)
        gathered = part[None]
        step_size = 1
        while step_size < count:
            step = self.steps.pop(0) if self.steps else None
            values, gathered = lax.optimization_barrier((self.values, gathered))
            moved = step_send(step, values) if step else None
            arrived = lax.ppermute(
                gathered, axis, [(i, i ^ step_size) for i in range(count)]
            )
            gathered = jnp.where(
                (index // step_size) % 2 == 1,
                jnp.concatenate([arrived, gathered], axis=0),
                jnp.concatenate([gathered, arrived], axis=0),
            )
            self.values = step_land(step, values, moved) if step else values
            step_size *= 2
        return gathered

    def finish(self):
        while self.steps:
            step = self.steps.pop(0)
            self.values = step_land(step, self.values, step_send(step, self.values))
        return self.values


def lined(first_val, middle_val, last_val, length):
    middle_part = jnp.broadcast_to(middle_val[:, None], (middle_val.shape[0], length))
    return jnp.concatenate([first_val[:, None], middle_part, last_val[:, None]], axis=1)


def on_device(state, kernel, gain, shift, upstream, face_links):
    local_faces = state.shape[0]
    tile_rows = state.shape[1]
    width = kernel.shape[1]
    tile_cols = state.shape[2] // width
    row_count = lax.axis_size("row")
    col_count = lax.axis_size("col")
    side = tile_rows * row_count
    row_index = lax.axis_index("row")
    col_index = lax.axis_index("col")
    face_ids = lax.axis_index("face") * local_faces + jnp.arange(local_faces, dtype=jnp.int32)
    links = face_links[face_ids]
    face_range = jnp.arange(FACES, dtype=jnp.int32)
    side_range = jnp.arange(4, dtype=jnp.int32)
    pixel_rows = local_faces * tile_rows * tile_cols

    def extend(values, carried=None):
        def gather(part, axis, tiled):
            if carried is None or axis == "face":
                return lax.all_gather(part, axis, axis=0, tiled=tiled)
            return carried.doubling(part, axis)

        col_strip = jnp.where(col_index == 0, values[:, :, 0], values[:, :, tile_cols - 1])
        by_row = gather(
            jnp.concatenate([values[:, 0], values[:, tile_rows - 1], col_strip], axis=1), "row", False
        )
        above = lax.dynamic_index_in_dim(by_row, (row_index + row_count - 1) % row_count, 0, False)
        below = lax.dynamic_index_in_dim(by_row, (row_index + 1) % row_count, 0, False)
        padded = jnp.concatenate(
            [above[:, None, tile_cols : 2 * tile_cols], values, below[:, None, :tile_cols]], axis=1
        )
        top_seg = by_row[0, :, :tile_cols]
        bottom_seg = by_row[row_count - 1, :, tile_cols : 2 * tile_cols]
        side_line = jnp.moveaxis(by_row[:, :, 2 * tile_cols :], 0, 1).reshape(
            local_faces, side, width
        )
        by_col = gather(
            jnp.concatenate(
                [top_seg, bottom_seg, side_line, padded[:, :, 0], padded[:, :, tile_cols - 1]],
                axis=1,
            ),
            "col",
            False,
        )
        lined_up = 2 * tile_cols + side
        before_col = lax.dynamic_index_in_dim(by_col, (col_index + col_count - 1) % col_count, 0, False)
        after_col = lax.dynamic_index_in_dim(by_col, (col_index + 1) % col_count, 0, False)
        padded = jnp.concatenate(
            [
                before_col[:, lined_up + tile_rows + 2 :, None],
                padded,
                after_col[:, lined_up : lined_up + tile_rows + 2, None],
            ],
            axis=2,
        )
        top_row = jnp.moveaxis(by_col[:, :, :tile_cols], 0, 1).reshape(local_faces, side, width)
        bottom_row = jnp.moveaxis(by_col[:, :, tile_cols : 2 * tile_cols], 0, 1).reshape(
            local_faces, side, width
        )
        left_col = by_col[0, :, 2 * tile_cols : lined_up]
        right_col = by_col[col_count - 1, :, 2 * tile_cols : lined_up]
        cycle = jnp.stack([top_row[:, ::-1], left_col, bottom_row, right_col[:, ::-1]], axis=1)
        all_cycle = gather(cycle, "face", True)
        all_corner = all_cycle[:, :, side - 1]
        side_pick = (
            (links[:, :4, 0][:, :, None, None] == face_range[:, None])
            & (links[:, :4, 1][:, :, None, None] == side_range)
        ).astype(jnp.bfloat16)
        halo_sides = jnp.einsum(
            "ksgt,gtpc->kspc", side_pick, all_cycle, preferred_element_type=jnp.float32
        ).astype(jnp.bfloat16)[:, :, ::-1]
        corner_pick = (
            (links[:, 4:, 0][:, :, None, None] == face_range[:, None])
            & (links[:, 4:, 1][:, :, None, None] == side_range)
            & (links[:, 4:, 3] == 0)[:, :, None, None]
        ).astype(jnp.bfloat16)
        corner_vals = jnp.einsum(
            "kqgt,gtc->kqc", corner_pick, all_corner, preferred_element_type=jnp.float32
        ).astype(jnp.bfloat16)
        full_top = jnp.concatenate(
            [corner_vals[:, 0:1], halo_sides[:, 0, ::-1], corner_vals[:, 3:4]], axis=1
        )
        full_bottom = jnp.concatenate(
            [corner_vals[:, 1:2], halo_sides[:, 2], corner_vals[:, 2:3]], axis=1
        )
        full_left = jnp.concatenate(
            [corner_vals[:, 0:1], halo_sides[:, 1], corner_vals[:, 1:2]], axis=1
        )
        full_right = jnp.concatenate(
            [corner_vals[:, 3:4], halo_sides[:, 3, ::-1], corner_vals[:, 2:3]], axis=1
        )
        top_piece = lax.dynamic_slice_in_dim(full_top, col_index * tile_cols, tile_cols + 2, 1)
        bottom_piece = lax.dynamic_slice_in_dim(
            full_bottom, col_index * tile_cols, tile_cols + 2, 1
        )
        left_piece = lax.dynamic_slice_in_dim(full_left, row_index * tile_rows, tile_rows + 2, 1)
        right_piece = lax.dynamic_slice_in_dim(full_right, row_index * tile_rows, tile_rows + 2, 1)
        padded = padded.at[:, 0].set(jnp.where(row_index == 0, top_piece, padded[:, 0]))
        padded = padded.at[:, tile_rows + 1].set(
            jnp.where(row_index == row_count - 1, bottom_piece, padded[:, tile_rows + 1])
        )
        padded = padded.at[:, :, 0].set(jnp.where(col_index == 0, left_piece, padded[:, :, 0]))
        padded = padded.at[:, :, tile_cols + 1].set(
            jnp.where(col_index == col_count - 1, right_piece, padded[:, :, tile_cols + 1])
        )
        return padded

    values = state.reshape(local_faces, tile_rows, tile_cols, width)
    padded_state = extend(values)

    def window(padded, row_step, col_step):
        return padded[
            :, 1 + row_step : 1 + row_step + tile_rows, 1 + col_step : 1 + col_step + tile_cols
        ].reshape(pixel_rows, width)

    def row_band(padded, row_step):
        return jnp.concatenate(
            [window(padded, row_step, col_step) for col_step in (-1, 0, 1)], axis=1
        )

    state_bands = [row_band(padded_state, row_step) for row_step in (-1, 0, 1)]
    response = jnp.zeros((pixel_rows, width), jnp.float32)
    for position, row_step in enumerate((-1, 0, 1)):
        band_weight = kernel[3 * position : 3 * position + 3].reshape(3 * width, width)
        response = response + jnp.dot(
            state_bands[position], band_weight, preferred_element_type=jnp.float32
        )
    total = float(FACES * side * side)
    sum_first, sum_square = gathered_sum(
        jnp.stack([jnp.sum(response, axis=0), jnp.sum(response * response, axis=0)])
    )
    centre = sum_first / total
    inverse_spread = lax.rsqrt(sum_square / total - centre * centre + 1e-05)
    normed = (response - centre) * inverse_spread
    before = gain * normed + shift
    incoming = upstream.reshape(pixel_rows, width).astype(jnp.float32)
    before_grad = incoming * gelu_slope(before)
    centred = response - centre
    state_sums = []
    centred_sums = []
    slope_sums = []
    for position in range(3):
        state_sums.append(jnp.sum(state_bands[position].astype(jnp.float32), axis=0))
        centred_sums.append(
            lax.dot_general(
                state_bands[position],
                centred,
                (((0,), (0,)), ((), ())),
                precision=lax.Precision.HIGHEST,
                preferred_element_type=jnp.float32,
            )
        )
        slope_sums.append(
            lax.dot_general(
                state_bands[position],
                before_grad,
                (((0,), (0,)), ((), ())),
                precision=lax.Precision.HIGHEST,
                preferred_element_type=jnp.float32,
            )
        )
    taps = 9
    carried = Carried(
        jnp.concatenate(
            [
                jnp.stack(slope_sums).reshape(-1),
                jnp.stack(centred_sums).reshape(-1),
                jnp.stack(state_sums).reshape(-1),
            ]
        )
    )
    shift_grad, gain_grad = channel_pair(
        jnp.sum(before_grad, axis=0), jnp.sum(before_grad * normed, axis=0), carried
    )
    response_grad = (
        gain * inverse_spread * (before_grad - shift_grad / total - normed * gain_grad / total)
    ).astype(jnp.bfloat16)
    grad_tile = response_grad.reshape(local_faces, tile_rows, tile_cols, width)
    padded_grad = extend(grad_tile, carried)
    kernel_sums = carried.finish()
    block = taps * width * width
    slope_total = kernel_sums[:block].reshape(taps, width, width)
    centred_total = kernel_sums[block : 2 * block].reshape(taps, width, width)
    state_total = kernel_sums[2 * block :].reshape(taps, width, 1)
    kernel_grad = (gain * inverse_spread) * (
        slope_total
        - state_total * (shift_grad / total)
        - centred_total * (gain_grad * inverse_spread / total)
    )
    zero_padded = jnp.pad(grad_tile, ((0, 0), (1, 1), (1, 1), (0, 0)))
    state_part = jnp.zeros((pixel_rows, width), jnp.float32)
    for row_step in (-1, 0, 1):
        flipped = jnp.concatenate(
            [kernel[kernel_tap(-row_step, -col_step)].T for col_step in (-1, 0, 1)], axis=0
        )
        state_part = state_part + jnp.dot(
            row_band(zero_padded, row_step), flipped, preferred_element_type=jnp.float32
        )
    state_part = state_part.reshape(local_faces, tile_rows, tile_cols, width)
    side_turns = links[:, :4, 2]
    corner_turns = links[:, 4:, 2]
    full_top_turn = lined(corner_turns[:, 0], side_turns[:, 0], corner_turns[:, 3], side)
    full_bottom_turn = lined(corner_turns[:, 1], side_turns[:, 2], corner_turns[:, 2], side)
    full_left_turn = lined(corner_turns[:, 0], side_turns[:, 1], corner_turns[:, 1], side)
    full_right_turn = lined(corner_turns[:, 3], side_turns[:, 3], corner_turns[:, 2], side)
    top_turn = jnp.where(
        row_index == 0,
        lax.dynamic_slice_in_dim(full_top_turn, col_index * tile_cols, tile_cols + 2, 1),
        0,
    )
    top_turn = top_turn.at[:, 0].set(
        jnp.where(col_index == 0, full_left_turn[:, row_index * tile_rows], top_turn[:, 0])
    )
    top_turn = top_turn.at[:, tile_cols + 1].set(
        jnp.where(
            col_index == col_count - 1,
            full_right_turn[:, row_index * tile_rows],
            top_turn[:, tile_cols + 1],
        )
    )
    bottom_turn = jnp.where(
        row_index == row_count - 1,
        lax.dynamic_slice_in_dim(full_bottom_turn, col_index * tile_cols, tile_cols + 2, 1),
        0,
    )
    bottom_turn = bottom_turn.at[:, 0].set(
        jnp.where(
            col_index == 0,
            full_left_turn[:, row_index * tile_rows + tile_rows + 1],
            bottom_turn[:, 0],
        )
    )
    bottom_turn = bottom_turn.at[:, tile_cols + 1].set(
        jnp.where(
            col_index == col_count - 1,
            full_right_turn[:, row_index * tile_rows + tile_rows + 1],
            bottom_turn[:, tile_cols + 1],
        )
    )
    left_turn = jnp.broadcast_to(
        jnp.where(col_index == 0, side_turns[:, 1], 0)[:, None], (local_faces, tile_rows + 2)
    )
    right_turn = jnp.broadcast_to(
        jnp.where(col_index == col_count - 1, side_turns[:, 3], 0)[:, None],
        (local_faces, tile_rows + 2),
    )

    def strip_terms(strip, turn_codes, steps, length):
        selector = (turn_codes[:, :, None] == side_range).astype(jnp.bfloat16)
        spread = strip[:, :, None, :] * selector[:, :, :, None]
        pieces = jnp.stack(
            [spread[:, 1 + offset : 1 + offset + length] for offset in (-1, 0, 1)], axis=2
        )
        pieces = pieces.reshape(local_faces * length, 12 * width)
        stacked = jnp.concatenate(
            [
                kernel[turned_tap(turn, step_pair[0], step_pair[1])].T
                for step_pair in steps
                for turn in range(4)
            ],
            axis=0,
        )
        summed = jnp.dot(pieces, stacked, preferred_element_type=jnp.float32)
        return summed.reshape(local_faces, length, width)

    left_strip = jnp.pad(padded_grad[:, 1 : tile_rows + 1, 0], ((0, 0), (1, 1), (0, 0)))
    right_strip = jnp.pad(
        padded_grad[:, 1 : tile_rows + 1, tile_cols + 1], ((0, 0), (1, 1), (0, 0))
    )
    top_terms = strip_terms(padded_grad[:, 0], top_turn, ((-1, -1), (-1, 0), (-1, 1)), tile_cols)
    bottom_terms = strip_terms(
        padded_grad[:, tile_rows + 1], bottom_turn, ((1, -1), (1, 0), (1, 1)), tile_cols
    )
    left_terms = strip_terms(left_strip, left_turn, ((-1, -1), (0, -1), (1, -1)), tile_rows)
    right_terms = strip_terms(right_strip, right_turn, ((-1, 1), (0, 1), (1, 1)), tile_rows)
    state_part = state_part.at[:, 0].add(top_terms)
    state_part = state_part.at[:, tile_rows - 1].add(bottom_terms)
    state_part = state_part.at[:, :, 0].add(left_terms)
    state_part = state_part.at[:, :, tile_cols - 1].add(right_terms)
    state_grad = state_part.astype(jnp.bfloat16).reshape(local_faces, tile_rows, tile_cols * width)
    return (state_grad, kernel_grad, gain_grad, shift_grad)


def solution(mesh):
    return jax.shard_map(
        on_device,
        mesh=mesh,
        in_specs=(P("face", "row", "col"), P(), P(), P(), P("face", "row", "col"), P()),
        out_specs=(P("face", "row", "col"), P(), P(), P()),
        check_vma=False,
    )
```

```python
import jax
import jax.numpy as jnp
from jax import lax
from jax.sharding import PartitionSpec as P

FACES = 12


HALF_ROOT = 0.7071067811865476
GAUSS_NORM = 0.3989422804014327


def halo_strips(cells, axis, dim):
    count = lax.axis_size(axis)
    ends = count - 1
    head = lax.slice_in_dim(cells, 0, 1, axis=dim)
    tail = lax.slice_in_dim(cells, cells.shape[dim] - 1, cells.shape[dim], axis=dim)
    from_before = lax.ppermute(tail, axis, [(i, (i + 1) % count) for i in range(ends)])
    from_after = lax.ppermute(head, axis, [((i + 1) % count, i) for i in range(ends)])
    return from_before, from_after


def gelu_slope(values):
    return (
        0.5 * (1.0 + lax.erf(values * HALF_ROOT))
        + values * jnp.exp(-0.5 * values * values) * GAUSS_NORM
    )


def kernel_tap(row_step, col_step):
    return (row_step + 1) * 3 + (col_step + 1)


def turned_tap(turns, row_step, col_step):
    for repeat in range(turns):
        row_step, col_step = (-col_step, row_step)
    return kernel_tap(-row_step, -col_step)


def nested_sum(values, carried=None):
    for axis in ("col", "face", "row"):
        if carried is None:
            values = lax.psum(values, axis)
        else:
            values = carried.beside(
                lambda part, axis=axis: jnp.sum(
                    lax.all_gather(part, axis, axis=0, tiled=False), axis=0
                ),
                values,
            )
    return values


def channel_pair(first_sum, second_sum, carried=None):
    both = nested_sum(jnp.stack([first_sum, second_sum]), carried)
    return both[0], both[1]


def gathered_sum(values):
    for axis in ("col", "row", "face"):
        values = jnp.sum(lax.all_gather(values, axis, axis=0, tiled=False), axis=0)
    return values


def sum_steps():
    faces = lax.axis_size("face")
    steps = [
        (
            "face",
            [
                [(i, (i + 4) % faces) for i in range(faces)],
                [(i, (i + 8) % faces) for i in range(faces)],
            ],
        ),
        ("face", [[(i, i ^ 1) for i in range(faces)]]),
        ("face", [[(i, i ^ 2) for i in range(faces)]]),
    ]
    for axis in ("row", "col"):
        count = lax.axis_size(axis)
        step = count // 2
        while step >= 1:
            steps.append((axis, [[(i, i ^ step) for i in range(count)]]))
            step //= 2
    return steps


def step_send(step, values):
    axis, pair_sets = step
    return [lax.ppermute(values, axis, pairs) for pairs in pair_sets]


def step_land(step, values, moved):
    if len(moved) == 1:
        return values + moved[0]
    from_before, from_after = moved
    group = lax.axis_index("face") // 4
    first = jnp.where(group == 0, values, jnp.where(group == 1, from_before, from_after))
    second = jnp.where(group == 0, from_after, jnp.where(group == 1, values, from_before))
    third = jnp.where(group == 0, from_before, jnp.where(group == 1, from_after, values))
    return (first + second) + third


class Carried:
    def __init__(self, values):
        self.values = values
        self.steps = sum_steps()

    def beside(self, collective, operand):
        if not self.steps:
            return collective(operand)
        step = self.steps.pop(0)
        values, operand = lax.optimization_barrier((self.values, operand))
        moved = step_send(step, values)
        result = collective(operand)
        self.values = step_land(step, values, moved)
        return result

    def doubling(self, part, axis):
        count = lax.axis_size(axis)
        index = lax.axis_index(axis)
        gathered = part[None]
        step_size = 1
        while step_size < count:
            step = self.steps.pop(0) if self.steps else None
            values, gathered = lax.optimization_barrier((self.values, gathered))
            moved = step_send(step, values) if step else None
            arrived = lax.ppermute(
                gathered, axis, [(i, i ^ step_size) for i in range(count)]
            )
            gathered = jnp.where(
                (index // step_size) % 2 == 1,
                jnp.concatenate([arrived, gathered], axis=0),
                jnp.concatenate([gathered, arrived], axis=0),
            )
            self.values = step_land(step, values, moved) if step else values
            step_size *= 2
        return gathered

    def finish(self):
        while self.steps:
            step = self.steps.pop(0)
            self.values = step_land(step, self.values, step_send(step, self.values))
        return self.values


def lined(first_val, middle_val, last_val, length):
    middle_part = jnp.broadcast_to(middle_val[:, None], (middle_val.shape[0], length))
    return jnp.concatenate([first_val[:, None], middle_part, last_val[:, None]], axis=1)


def on_device(state, kernel, gain, shift, upstream, face_links):
    local_faces = state.shape[0]
    tile_rows = state.shape[1]
    width = kernel.shape[1]
    tile_cols = state.shape[2] // width
    row_count = lax.axis_size("row")
    col_count = lax.axis_size("col")
    side = tile_rows * row_count
    row_index = lax.axis_index("row")
    col_index = lax.axis_index("col")
    face_ids = lax.axis_index("face") * local_faces + jnp.arange(local_faces, dtype=jnp.int32)
    links = face_links[face_ids]
    face_range = jnp.arange(FACES, dtype=jnp.int32)
    side_range = jnp.arange(4, dtype=jnp.int32)
    pixel_rows = local_faces * tile_rows * tile_cols

    def extend(values, carried=None):
        def gather(part, axis, tiled):
            if carried is None or axis == "face":
                return lax.all_gather(part, axis, axis=0, tiled=tiled)
            return carried.doubling(part, axis)

        col_strip = jnp.where(col_index == 0, values[:, :, 0], values[:, :, tile_cols - 1])
        by_row = gather(
            jnp.concatenate([values[:, 0], values[:, tile_rows - 1], col_strip], axis=1), "row", False
        )
        above = lax.dynamic_index_in_dim(by_row, (row_index + row_count - 1) % row_count, 0, False)
        below = lax.dynamic_index_in_dim(by_row, (row_index + 1) % row_count, 0, False)
        padded = jnp.concatenate(
            [above[:, None, tile_cols : 2 * tile_cols], values, below[:, None, :tile_cols]], axis=1
        )
        top_seg = by_row[0, :, :tile_cols]
        bottom_seg = by_row[row_count - 1, :, tile_cols : 2 * tile_cols]
        side_line = jnp.moveaxis(by_row[:, :, 2 * tile_cols :], 0, 1).reshape(
            local_faces, side, width
        )
        by_col = gather(
            jnp.concatenate(
                [top_seg, bottom_seg, side_line, padded[:, :, 0], padded[:, :, tile_cols - 1]],
                axis=1,
            ),
            "col",
            False,
        )
        lined_up = 2 * tile_cols + side
        before_col = lax.dynamic_index_in_dim(by_col, (col_index + col_count - 1) % col_count, 0, False)
        after_col = lax.dynamic_index_in_dim(by_col, (col_index + 1) % col_count, 0, False)
        padded = jnp.concatenate(
            [
                before_col[:, lined_up + tile_rows + 2 :, None],
                padded,
                after_col[:, lined_up : lined_up + tile_rows + 2, None],
            ],
            axis=2,
        )
        top_row = jnp.moveaxis(by_col[:, :, :tile_cols], 0, 1).reshape(local_faces, side, width)
        bottom_row = jnp.moveaxis(by_col[:, :, tile_cols : 2 * tile_cols], 0, 1).reshape(
            local_faces, side, width
        )
        left_col = by_col[0, :, 2 * tile_cols : lined_up]
        right_col = by_col[col_count - 1, :, 2 * tile_cols : lined_up]
        cycle = jnp.stack([top_row[:, ::-1], left_col, bottom_row, right_col[:, ::-1]], axis=1)
        all_cycle = gather(cycle, "face", True)
        all_corner = all_cycle[:, :, side - 1]
        side_pick = (
            (links[:, :4, 0][:, :, None, None] == face_range[:, None])
            & (links[:, :4, 1][:, :, None, None] == side_range)
        ).astype(jnp.bfloat16)
        halo_sides = jnp.einsum(
            "ksgt,gtpc->kspc", side_pick, all_cycle, preferred_element_type=jnp.float32
        ).astype(jnp.bfloat16)[:, :, ::-1]
        corner_pick = (
            (links[:, 4:, 0][:, :, None, None] == face_range[:, None])
            & (links[:, 4:, 1][:, :, None, None] == side_range)
            & (links[:, 4:, 3] == 0)[:, :, None, None]
        ).astype(jnp.bfloat16)
        corner_vals = jnp.einsum(
            "kqgt,gtc->kqc", corner_pick, all_corner, preferred_element_type=jnp.float32
        ).astype(jnp.bfloat16)
        full_top = jnp.concatenate(
            [corner_vals[:, 0:1], halo_sides[:, 0, ::-1], corner_vals[:, 3:4]], axis=1
        )
        full_bottom = jnp.concatenate(
            [corner_vals[:, 1:2], halo_sides[:, 2], corner_vals[:, 2:3]], axis=1
        )
        full_left = jnp.concatenate(
            [corner_vals[:, 0:1], halo_sides[:, 1], corner_vals[:, 1:2]], axis=1
        )
        full_right = jnp.concatenate(
            [corner_vals[:, 3:4], halo_sides[:, 3, ::-1], corner_vals[:, 2:3]], axis=1
        )
        top_piece = lax.dynamic_slice_in_dim(full_top, col_index * tile_cols, tile_cols + 2, 1)
        bottom_piece = lax.dynamic_slice_in_dim(
            full_bottom, col_index * tile_cols, tile_cols + 2, 1
        )
        left_piece = lax.dynamic_slice_in_dim(full_left, row_index * tile_rows, tile_rows + 2, 1)
        right_piece = lax.dynamic_slice_in_dim(full_right, row_index * tile_rows, tile_rows + 2, 1)
        padded = padded.at[:, 0].set(jnp.where(row_index == 0, top_piece, padded[:, 0]))
        padded = padded.at[:, tile_rows + 1].set(
            jnp.where(row_index == row_count - 1, bottom_piece, padded[:, tile_rows + 1])
        )
        padded = padded.at[:, :, 0].set(jnp.where(col_index == 0, left_piece, padded[:, :, 0]))
        padded = padded.at[:, :, tile_cols + 1].set(
            jnp.where(col_index == col_count - 1, right_piece, padded[:, :, tile_cols + 1])
        )
        return padded

    values = state.reshape(local_faces, tile_rows, tile_cols, width)
    padded_state = extend(values)

    def window(padded, row_step, col_step):
        return padded[
            :, 1 + row_step : 1 + row_step + tile_rows, 1 + col_step : 1 + col_step + tile_cols
        ].reshape(pixel_rows, width)

    def row_band(padded, row_step):
        return jnp.concatenate(
            [window(padded, row_step, col_step) for col_step in (-1, 0, 1)], axis=1
        )

    state_bands = [row_band(padded_state, row_step) for row_step in (-1, 0, 1)]
    response = jnp.zeros((pixel_rows, width), jnp.float32)
    for position, row_step in enumerate((-1, 0, 1)):
        band_weight = kernel[3 * position : 3 * position + 3].reshape(3 * width, width)
        response = response + jnp.dot(
            state_bands[position], band_weight, preferred_element_type=jnp.float32
        )
    total = float(FACES * side * side)
    sum_first, sum_square = gathered_sum(
        jnp.stack([jnp.sum(response, axis=0), jnp.sum(response * response, axis=0)])
    )
    centre = sum_first / total
    inverse_spread = lax.rsqrt(sum_square / total - centre * centre + 1e-05)
    normed = (response - centre) * inverse_spread
    before = gain * normed + shift
    incoming = upstream.reshape(pixel_rows, width).astype(jnp.float32)
    before_grad = incoming * gelu_slope(before)
    centred = response - centre
    state_sums = []
    centred_sums = []
    slope_sums = []
    for position in range(3):
        state_sums.append(jnp.sum(state_bands[position].astype(jnp.float32), axis=0))
        centred_sums.append(
            lax.dot_general(
                state_bands[position],
                centred,
                (((0,), (0,)), ((), ())),
                precision=lax.Precision.HIGHEST,
                preferred_element_type=jnp.float32,
            )
        )
        slope_sums.append(
            lax.dot_general(
                state_bands[position],
                before_grad,
                (((0,), (0,)), ((), ())),
                precision=lax.Precision.HIGHEST,
                preferred_element_type=jnp.float32,
            )
        )
    taps = 9
    carried = Carried(
        jnp.concatenate(
            [
                jnp.stack(slope_sums).reshape(-1),
                jnp.stack(centred_sums).reshape(-1),
                jnp.stack(state_sums).reshape(-1),
            ]
        )
    )
    shift_grad, gain_grad = channel_pair(
        jnp.sum(before_grad, axis=0), jnp.sum(before_grad * normed, axis=0), carried
    )
    response_grad = (
        gain * inverse_spread * (before_grad - shift_grad / total - normed * gain_grad / total)
    ).astype(jnp.bfloat16)
    grad_tile = response_grad.reshape(local_faces, tile_rows, tile_cols, width)
    padded_grad = extend(grad_tile, carried)
    kernel_sums = carried.finish()
    block = taps * width * width
    slope_total = kernel_sums[:block].reshape(taps, width, width)
    centred_total = kernel_sums[block : 2 * block].reshape(taps, width, width)
    state_total = kernel_sums[2 * block :].reshape(taps, width, 1)
    kernel_grad = (gain * inverse_spread) * (
        slope_total
        - state_total * (shift_grad / total)
        - centred_total * (gain_grad * inverse_spread / total)
    )
    zero_padded = jnp.pad(grad_tile, ((0, 0), (1, 1), (1, 1), (0, 0)))
    state_part = jnp.zeros((pixel_rows, width), jnp.float32)
    for row_step in (-1, 0, 1):
        flipped = jnp.concatenate(
            [kernel[kernel_tap(-row_step, -col_step)].T for col_step in (-1, 0, 1)], axis=0
        )
        state_part = state_part + jnp.dot(
            row_band(zero_padded, row_step), flipped, preferred_element_type=jnp.float32
        )
    state_part = state_part.reshape(local_faces, tile_rows, tile_cols, width)
    side_turns = links[:, :4, 2]
    corner_turns = links[:, 4:, 2]
    full_top_turn = lined(corner_turns[:, 0], side_turns[:, 0], corner_turns[:, 3], side)
    full_bottom_turn = lined(corner_turns[:, 1], side_turns[:, 2], corner_turns[:, 2], side)
    full_left_turn = lined(corner_turns[:, 0], side_turns[:, 1], corner_turns[:, 1], side)
    full_right_turn = lined(corner_turns[:, 3], side_turns[:, 3], corner_turns[:, 2], side)
    top_turn = jnp.where(
        row_index == 0,
        lax.dynamic_slice_in_dim(full_top_turn, col_index * tile_cols, tile_cols + 2, 1),
        0,
    )
    top_turn = top_turn.at[:, 0].set(
        jnp.where(col_index == 0, full_left_turn[:, row_index * tile_rows], top_turn[:, 0])
    )
    top_turn = top_turn.at[:, tile_cols + 1].set(
        jnp.where(
            col_index == col_count - 1,
            full_right_turn[:, row_index * tile_rows],
            top_turn[:, tile_cols + 1],
        )
    )
    bottom_turn = jnp.where(
        row_index == row_count - 1,
        lax.dynamic_slice_in_dim(full_bottom_turn, col_index * tile_cols, tile_cols + 2, 1),
        0,
    )
    bottom_turn = bottom_turn.at[:, 0].set(
        jnp.where(
            col_index == 0,
            full_left_turn[:, row_index * tile_rows + tile_rows + 1],
            bottom_turn[:, 0],
        )
    )
    bottom_turn = bottom_turn.at[:, tile_cols + 1].set(
        jnp.where(
            col_index == col_count - 1,
            full_right_turn[:, row_index * tile_rows + tile_rows + 1],
            bottom_turn[:, tile_cols + 1],
        )
    )
    left_turn = jnp.broadcast_to(
        jnp.where(col_index == 0, side_turns[:, 1], 0)[:, None], (local_faces, tile_rows + 2)
    )
    right_turn = jnp.broadcast_to(
        jnp.where(col_index == col_count - 1, side_turns[:, 3], 0)[:, None],
        (local_faces, tile_rows + 2),
    )

    def strip_terms(strip, turn_codes, steps, length):
        selector = (turn_codes[:, :, None] == side_range).astype(jnp.bfloat16)
        spread = strip[:, :, None, :] * selector[:, :, :, None]
        pieces = jnp.stack(
            [spread[:, 1 + offset : 1 + offset + length] for offset in (-1, 0, 1)], axis=2
        )
        pieces = pieces.reshape(local_faces * length, 12 * width)
        stacked = jnp.concatenate(
            [
                kernel[turned_tap(turn, step_pair[0], step_pair[1])].T
                for step_pair in steps
                for turn in range(4)
            ],
            axis=0,
        )
        summed = jnp.dot(pieces, stacked, preferred_element_type=jnp.float32)
        return summed.reshape(local_faces, length, width)

    left_strip = jnp.pad(padded_grad[:, 1 : tile_rows + 1, 0], ((0, 0), (1, 1), (0, 0)))
    right_strip = jnp.pad(
        padded_grad[:, 1 : tile_rows + 1, tile_cols + 1], ((0, 0), (1, 1), (0, 0))
    )
    top_terms = strip_terms(padded_grad[:, 0], top_turn, ((-1, -1), (-1, 0), (-1, 1)), tile_cols)
    bottom_terms = strip_terms(
        padded_grad[:, tile_rows + 1], bottom_turn, ((1, -1), (1, 0), (1, 1)), tile_cols
    )
    left_terms = strip_terms(left_strip, left_turn, ((-1, -1), (0, -1), (1, -1)), tile_rows)
    right_terms = strip_terms(right_strip, right_turn, ((-1, 1), (0, 1), (1, 1)), tile_rows)
    state_part = state_part.at[:, 0].add(top_terms)
    state_part = state_part.at[:, tile_rows - 1].add(bottom_terms)
    state_part = state_part.at[:, :, 0].add(left_terms)
    state_part = state_part.at[:, :, tile_cols - 1].add(right_terms)
    state_grad = state_part.astype(jnp.bfloat16).reshape(local_faces, tile_rows, tile_cols * width)
    return (state_grad, kernel_grad, gain_grad, shift_grad)


def solution(mesh):
    return jax.shard_map(
        on_device,
        mesh=mesh,
        in_specs=(P("face", "row", "col"), P(), P(), P(), P("face", "row", "col"), P()),
        out_specs=(P("face", "row", "col"), P(), P(), P()),
        check_vma=False,
    )
```
